256 devices in a mesh: gx: 32 (over z_hi, y, x), gy: 2 (over core), gz: 4 (over z_lo).
Axes of the slice: x: 4, y: 4, z: 8 (z_hi: 2, z_lo: 4; z = z_hi * 4 + z_lo), core: 2. Of those that a mesh axis runs over, the one named last changes fastest.
Arguments:
- inputs: bfloat16 [4, 256, 32, 256], P(None, 'gx', 'gz', 'gy'), may hold values from -6 to 6
- w_in: bfloat16 [16, 4, 3, 3, 3], replicated, may hold values from -0.875 to 0.875
- w_fine_enc: bfloat16 [16, 16, 3, 3, 3], replicated, may hold values from -0.4375 to 0.4375
- w_down_mid: bfloat16 [64, 16, 2, 2, 2], replicated, may hold values from -0.75 to 0.75
- w_mid_enc: bfloat16 [27, 4096], replicated, may hold values from -0.21875 to 0.21875
- w_down_bottom: bfloat16 [8, 16384], replicated, may hold values from -0.375 to 0.375
- w_query: bfloat16 [256, 256], replicated, may hold values from -8 to 8
- w_key: bfloat16 [256, 256], replicated, may hold values from -0.375 to 0.375
- w_value: bfloat16 [256, 256], replicated, may hold values from -0.375 to 0.375
- w_attn_out: bfloat16 [256, 256], replicated, may hold values from -0.375 to 0.375
- w_up_mid: bfloat16 [8, 16384], replicated, may hold values from -0.375 to 0.375
- w_mid_dec: bfloat16 [27, 4096], replicated, may hold values from -0.21875 to 0.21875
- w_up_fine: bfloat16 [64, 16, 2, 2, 2], replicated, may hold values from -0.75 to 0.75
- w_fine_dec: bfloat16 [16, 16, 3, 3, 3], replicated, may hold values from -0.4375 to 0.4375
- w_head: bfloat16 [4, 16], replicated, may hold values from -1.5 to 1.5
Outputs:
- wake: float32 [4, 256, 32, 256], P(None, 'gx', 'gz', 'gy')
The draws below stay inside these ranges and needn't reach their ends.
All inputs are finite; a program needn't handle non-finite values.
Results may differ from the reference program's by a relative error of at most 0.023.
The reference program's roundings to bfloat16 on the way count: a program that leaves them out, or rounds other values in their place, can miss the bound.
Values may be sent and summed in bfloat16 or wider, within the bound.
No kernel may reach another device: no remote copies, remote signals or barrier semaphores. Data moves between devices by JAX's collectives and lax.ppermute only.
A program may use at most 64 MiB of HBM per device.

```python
import jax
import jax.numpy as jnp
from jax import lax

CH_IN = 4
C0 = 16
C1 = 64
C2 = 256
HEADS = 4
HEAD_DIM = 64
CH_OUT = 4
NX = 256
NV = 32
NS = 256


def draw_w_query(key, part):
    first_key = jax.random.fold_in(key, 11)
    base = jax.random.normal(first_key, (C2, C2), jnp.float32) * C2 ** (-0.5)
    return jnp.clip(base, -8.0, 8.0).astype(jnp.bfloat16)


def shard_levels(stream_key, extent, split, low, largest):
    loudness = 1.0
    for dim, parts in split:
        heights = jax.random.uniform(jax.random.fold_in(jax.random.fold_in(stream_key, 6), dim), (parts,), jnp.float32, low / len(split), largest / len(split))
        loudness = loudness * jnp.repeat(jnp.exp(heights), extent[dim] // parts).reshape((-1,) + (1,) * (len(extent) - 1 - dim))
    return loudness


def scatter_about(stream_key, shape, deviation, bound, split=(), kind=jnp.bfloat16):
    values = jax.random.normal(stream_key, shape, jnp.float32) * deviation
    if len(split) > 0:
        values = shard_levels(stream_key, shape, split, -0.22, 0.18) * values
    return jnp.clip(values, min=-bound, max=bound).astype(kind)


def setup_inputs(seed: int = 0) -> dict:
    arg_keys = jax.random.split(jax.random.key(seed), 16)
    inputs = scatter_about(arg_keys[0], (CH_IN, NX, NV, NS), 1.0, 6.0, ((1, 32), (2, 4), (3, 2)))
    w_in = scatter_about(arg_keys[1], (C0, CH_IN, 3, 3, 3), (CH_IN * 27 // 2) ** -0.5, 0.875)
    w_fine_enc = scatter_about(arg_keys[2], (C0, C0, 3, 3, 3), (C0 * 27 // 2) ** -0.5, 0.4375)
    w_down_mid = scatter_about(arg_keys[3], (C1, C0, 2, 2, 2), (C0 * 4) ** -0.5, 0.75)
    w_mid_enc = scatter_about(arg_keys[4], (27, C1 * C1), (C1 * 27 // 2) ** -0.5, 0.21875)
    w_down_bottom = scatter_about(arg_keys[5], (8, C2 * C1), (C1 * 4) ** -0.5, 0.375)
    w_query = draw_w_query(jax.random.fold_in(arg_keys[15], 71), 0)
    w_key = scatter_about(arg_keys[7], (C2, C2), C2 ** -0.5, 0.375)
    w_value = scatter_about(arg_keys[8], (C2, C2), C2 ** -0.5, 0.375)
    w_attn_out = scatter_about(arg_keys[9], (C2, C2), C2 ** -0.5, 0.375)
    w_up_mid = scatter_about(arg_keys[10], (8, C2 * C1), C2 ** -0.5, 0.375)
    w_mid_dec = scatter_about(arg_keys[11], (27, C1 * C1), (C1 * 27 // 2) ** -0.5, 0.21875)
    w_up_fine = scatter_about(arg_keys[12], (C1, C0, 2, 2, 2), C1 ** -0.5, 0.75)
    w_fine_dec = scatter_about(arg_keys[13], (C0, C0, 3, 3, 3), (C0 * 27 // 2) ** -0.5, 0.4375)
    w_head = scatter_about(arg_keys[14], (CH_OUT, C0), C0 ** -0.5, 1.5)
    return dict(inputs=inputs, w_in=w_in, w_fine_enc=w_fine_enc, w_down_mid=w_down_mid, w_mid_enc=w_mid_enc, w_down_bottom=w_down_bottom, w_query=w_query, w_key=w_key, w_value=w_value, w_attn_out=w_attn_out, w_up_mid=w_up_mid, w_mid_dec=w_mid_dec, w_up_fine=w_up_fine, w_fine_dec=w_fine_dec, w_head=w_head)


HIGH = lax.Precision.HIGHEST
NUMS = ('NCDHW', 'OIDHW', 'NCDHW')

def unfold(weight, side, first, second):
    return weight.reshape(side, side, side, first, second).transpose(3, 4, 0, 1, 2)

def conv_same(field, weight):
    padded = jnp.pad(field.astype(jnp.float32), ((0, 0), (1, 1), (1, 1), (1, 1)))
    return lax.conv_general_dilated(padded[None], weight.astype(jnp.float32), (1, 1, 1), 'VALID', dimension_numbers=NUMS, precision=HIGH)[0]

def conv_down(field, weight):
    return lax.conv_general_dilated(field.astype(jnp.float32)[None], weight.astype(jnp.float32), (2, 2, 2), 'VALID', dimension_numbers=NUMS, precision=HIGH)[0]

def conv_up(field, weight):
    outer = jnp.einsum('ixvs,ioabc->oxavbsc', field.astype(jnp.float32), weight.astype(jnp.float32), precision=HIGH)
    chans, sx, sv, ss = (weight.shape[1], field.shape[1], field.shape[2], field.shape[3])
    return outer.reshape(chans, 2 * sx, 2 * sv, 2 * ss)

def activate(value):
    return jax.nn.silu(value).astype(jnp.bfloat16)

def project(weight, field):
    return jnp.einsum('oc,cxp->oxp', weight.astype(jnp.float32), field.astype(jnp.float32), precision=HIGH)

def reference(inputs, w_in, w_fine_enc, w_down_mid, w_mid_enc, w_down_bottom, w_query, w_key, w_value, w_attn_out, w_up_mid, w_mid_dec, w_up_fine, w_fine_dec, w_head):
    first = activate(conv_same(inputs, w_in))
    fine_skip = activate(conv_same(first, w_fine_enc))
    mid_in = activate(conv_down(fine_skip, w_down_mid))
    mid_skip = activate(conv_same(mid_in, unfold(w_mid_enc, 3, C1, C1)))
    bottom = activate(conv_down(mid_skip, unfold(w_down_bottom, 2, C2, C1)))
    chans, sx, sv, ss = bottom.shape
    flat = bottom.reshape(chans, sx, sv * ss)
    values_f = flat.astype(jnp.float32)
    mean_sq = lax.optimization_barrier(jnp.mean(values_f * values_f, axis=0))
    normed = (values_f * lax.rsqrt(mean_sq + 1e-05)).astype(jnp.bfloat16)
    queries = project(w_query, normed).astype(jnp.bfloat16).reshape(HEADS, HEAD_DIM, sx, sv * ss)
    keys = project(w_key, normed).astype(jnp.bfloat16).reshape(HEADS, HEAD_DIM, sx, sv * ss)
    values = project(w_value, normed).astype(jnp.bfloat16).reshape(HEADS, HEAD_DIM, sx, sv * ss)
    scores = jnp.einsum('hdxp,hdyp->hxyp', queries.astype(jnp.float32), keys.astype(jnp.float32), precision=HIGH) / jnp.sqrt(jnp.float32(HEAD_DIM))
    weights = jax.nn.softmax(scores, axis=2).astype(jnp.bfloat16)
    attended = jnp.einsum('hxyp,hdyp->hdxp', weights.astype(jnp.float32), values.astype(jnp.float32), precision=HIGH)
    attended = attended.astype(jnp.bfloat16).reshape(chans, sx, sv * ss)
    bottom_out = (values_f + project(w_attn_out, attended)).astype(jnp.bfloat16).reshape(chans, sx, sv, ss)
    mid_up = (conv_up(bottom_out, unfold(w_up_mid, 2, C2, C1)) + mid_skip.astype(jnp.float32)).astype(jnp.bfloat16)
    mid_dec = activate(conv_same(mid_up, unfold(w_mid_dec, 3, C1, C1)))
    fine_up = (conv_up(mid_dec, w_up_fine) + fine_skip.astype(jnp.float32)).astype(jnp.bfloat16)
    fine_dec = activate(conv_same(fine_up, w_fine_dec))
    return jnp.einsum('oc,cxvs->oxvs', w_head.astype(jnp.float32), fine_dec.astype(jnp.float32), precision=HIGH)
```

```python
import jax
import jax.numpy as jnp
from jax import lax
from jax.experimental import pallas as pl
from jax.experimental.pallas import tpu as pltpu
from jax.sharding import PartitionSpec as P

C1 = 64
C2 = 256
HEADS = 4


NUMS = ("NCDHW", "OIDHW", "NCDHW")
FINE_SIDES = (("gx", 0), ("gy", 3), ("gz", 2))
MID_SIDES = (("gx", 1), ("gy", 3), ("gz", 2))


def extended(block, sides, width):
    for axis, dim in sides:
        count = lax.axis_size(axis)
        forward = [(i, i + 1) for i in range(count - 1)]
        backward = [(target, source) for source, target in forward]
        low = lax.ppermute(
            lax.slice_in_dim(block, block.shape[dim] - width, None, axis=dim), axis, forward
        )
        high = lax.ppermute(lax.slice_in_dim(block, 0, width, axis=dim), axis, backward)
        block = jnp.concatenate([low, block, high], axis=dim)
    return block


def unfold(weight, side, first, second):
    return weight.reshape(side, side, side, first, second).transpose(3, 4, 0, 1, 2)


def round_up(value, step):
    return (value + step - 1) // step * step


def band_weights(weight, sv, rows):
    out_c, in_c = weight.shape[:2]
    taps = jnp.arange(3)[:, None, None]
    eye = (jnp.arange(rows)[None, None, :] == jnp.arange(sv)[None, :, None] + taps).astype(
        jnp.float32
    )
    band = jnp.einsum("oiabc,bvw->acoviw", weight.astype(jnp.float32), eye)
    return band.reshape(9, out_c * sv, in_c * rows).astype(jnp.bfloat16)


def fine_kernel(p_ref, w_ref, *rest, sx, sv, ss, cout, head):
    if head:
        h_ref, o_ref = rest
    else:
        (o_ref,) = rest
    lanes = p_ref.shape[-1]
    for x in range(sx):
        acc = jnp.zeros((cout * sv, ss), jnp.float32)
        for a in range(3):
            slab = p_ref[x + a].astype(jnp.float32)
            for c in range(3):
                piece = slab if c == 0 else pltpu.roll(slab, lanes - c, 1)
                piece = piece[:, :ss].astype(jnp.bfloat16)
                acc = acc + jnp.dot(w_ref[a * 3 + c], piece, preferred_element_type=jnp.float32)
        act = (acc * jax.nn.sigmoid(acc)).astype(jnp.bfloat16)
        if head:
            res = jnp.dot(h_ref[...], act, preferred_element_type=jnp.float32)
            o_ref[:, x] = res.reshape(res.shape[0] // sv, sv, ss)
        else:
            o_ref[x] = act.astype(jnp.float32).reshape(cout, sv, ss)


def fine_conv(field, weight, head=None):
    sx, cin, sv, ss = field.shape
    cout = weight.shape[0]
    rows = round_up(sv + 2, 16)
    lanes = round_up(ss + 2, 128)
    padded = extended(field, FINE_SIDES, 1)
    padded = jnp.pad(padded, ((0, 0), (0, 0), (0, rows - sv - 2), (0, lanes - ss - 2)))
    padded = padded.reshape(sx + 2, cin * rows, lanes)
    operands = [padded, band_weights(weight, sv, rows)]
    if head is None:
        out_shape = jax.ShapeDtypeStruct((sx, cout, sv, ss), jnp.float32)
    else:
        eye = jnp.eye(sv, dtype=jnp.float32)
        kron = jnp.einsum("po,vw->pvow", head.astype(jnp.float32), eye)
        operands.append(kron.reshape(head.shape[0] * sv, cout * sv).astype(jnp.bfloat16))
        out_shape = jax.ShapeDtypeStruct((head.shape[0], sx, sv, ss), jnp.float32)
    kernel = lambda *refs: fine_kernel(
        *refs, sx=sx, sv=sv, ss=ss, cout=cout, head=head is not None
    )
    return pl.pallas_call(kernel, out_shape=out_shape)(*operands)


def conv_valid(padded, weight):
    return lax.conv_general_dilated(
        padded[None],
        weight,
        (1, 1, 1),
        "VALID",
        dimension_numbers=NUMS,
        preferred_element_type=jnp.float32,
    )[0]


def mid_conv(field, weight):
    padded = extended(field, MID_SIDES, 1)
    return conv_valid(padded, weight)


def conv_down(field, weight):
    return lax.conv_general_dilated(
        field[None],
        weight,
        (2, 2, 2),
        "VALID",
        dimension_numbers=NUMS,
        preferred_element_type=jnp.float32,
    )[0]


def fine_down(field, weight):
    sx, c, sv, ss = field.shape
    blocks = field.reshape(sx // 2, 2, c, sv // 2, 2, ss // 2, 2)
    return jnp.einsum("xaivbsc,oiabc->oxvs", blocks, weight, preferred_element_type=jnp.float32)


def fine_up(field, weight):
    outer = jnp.einsum("ixvs,ioabc->xaovbsc", field, weight, preferred_element_type=jnp.float32)
    chans, sx, sv, ss = (weight.shape[1], field.shape[1], field.shape[2], field.shape[3])
    return outer.reshape(2 * sx, chans, 2 * sv, 2 * ss)


def conv_up(field, weight):
    outer = jnp.einsum("ixvs,ioabc->oxavbsc", field, weight, preferred_element_type=jnp.float32)
    chans, sx, sv, ss = (weight.shape[1], field.shape[1], field.shape[2], field.shape[3])
    return outer.reshape(chans, 2 * sx, 2 * sv, 2 * ss)


def activate(value):
    return jax.nn.silu(value).astype(jnp.bfloat16)


def project(weight, field):
    return jnp.einsum("oc,cxp->oxp", weight, field, preferred_element_type=jnp.float32)


def normalize(block):
    values_f = block.astype(jnp.float32)
    mean_sq = jnp.mean(values_f * values_f, axis=0)
    return (values_f * lax.rsqrt(mean_sq + 1e-05)).astype(jnp.bfloat16)


def split_heads(weight, normed):
    chans, sx, count = normed.shape
    return project(weight, normed).astype(jnp.bfloat16).reshape(HEADS, chans // HEADS, sx, count)


def combine(queries, keys, values):
    scale = 1.0 / jnp.sqrt(jnp.float32(queries.shape[1]))
    scores = (
        jnp.einsum("hdxp,hdyp->hxyp", queries, keys, preferred_element_type=jnp.float32) * scale
    )
    weights = jax.nn.softmax(scores, axis=2).astype(jnp.bfloat16)
    attended = jnp.einsum("hxyp,hdyp->hdxp", weights, values, preferred_element_type=jnp.float32)
    heads, depth, sx, count = attended.shape
    return attended.astype(jnp.bfloat16).reshape(heads * depth, sx, count)


def finish(block, attended, w_attn_out):
    return (block.astype(jnp.float32) + project(w_attn_out, attended)).astype(jnp.bfloat16)


def on_device(
    inputs,
    w_in,
    w_fine_enc,
    w_down_mid,
    w_mid_enc,
    w_down_bottom,
    w_query,
    w_key,
    w_value,
    w_attn_out,
    w_up_mid,
    w_mid_dec,
    w_up_fine,
    w_fine_dec,
    w_head,
):
    fields = inputs.transpose(1, 0, 2, 3)
    first = fine_conv(fields, w_in).astype(jnp.bfloat16)
    fine_skip = fine_conv(first, w_fine_enc).astype(jnp.bfloat16)
    mid_in = activate(fine_down(fine_skip, w_down_mid))
    mid_skip = activate(mid_conv(mid_in, unfold(w_mid_enc, 3, C1, C1)))
    bottom = activate(conv_down(mid_skip, unfold(w_down_bottom, 2, C2, C1)))
    chans, sx, sv, ss = bottom.shape
    flat = bottom.reshape(chans, sx, sv * ss)
    rows = lax.all_to_all(flat, "gx", split_axis=2, concat_axis=1, tiled=True)
    normed = normalize(rows)
    queries = split_heads(w_query, normed)
    keys = split_heads(w_key, normed)
    values = split_heads(w_value, normed)
    result = finish(rows, combine(queries, keys, values), w_attn_out)
    mixed = lax.all_to_all(result, "gx", split_axis=1, concat_axis=2, tiled=True)
    bottom_out = mixed.reshape(chans, sx, sv, ss)
    mid_up = (
        conv_up(bottom_out, unfold(w_up_mid, 2, C2, C1)) + mid_skip.astype(jnp.float32)
    ).astype(jnp.bfloat16)
    mid_dec = activate(mid_conv(mid_up, unfold(w_mid_dec, 3, C1, C1)))
    fine_up_field = (fine_up(mid_dec, w_up_fine) + fine_skip.astype(jnp.float32)).astype(
        jnp.bfloat16
    )
    return fine_conv(fine_up_field, w_fine_dec, head=w_head)


def solution(mesh):
    placed = (P(None, "gx", "gz", "gy"),) + (P(),) * 14
    return jax.shard_map(
        on_device, mesh=mesh, in_specs=placed, out_specs=P(None, "gx", "gz", "gy"), check_vma=False
    )
```

```python
import jax
import jax.numpy as jnp
from jax import lax
from jax.experimental import pallas as pl
from jax.experimental.pallas import tpu as pltpu
from jax.sharding import PartitionSpec as P

C1 = 64
C2 = 256
HEADS = 4


NUMS = ("NCDHW", "OIDHW", "NCDHW")
FINE_SIDES = (("gx", 0), ("gy", 3), ("gz", 2))
MID_SIDES = (("gx", 1), ("gy", 3), ("gz", 2))


def extended(block, sides, width):
    for axis, dim in sides:
        count = lax.axis_size(axis)
        forward = [(i, i + 1) for i in range(count - 1)]
        backward = [(target, source) for source, target in forward]
        low = lax.ppermute(
            lax.slice_in_dim(block, block.shape[dim] - width, None, axis=dim), axis, forward
        )
        high = lax.ppermute(lax.slice_in_dim(block, 0, width, axis=dim), axis, backward)
        block = jnp.concatenate([low, block, high], axis=dim)
    return block


def unfold(weight, side, first, second):
    return weight.reshape(side, side, side, first, second).transpose(3, 4, 0, 1, 2)


def round_up(value, step):
    return (value + step - 1) // step * step


def band_weights(weight, sv, rows):
    out_c, in_c = weight.shape[:2]
    taps = weight.astype(jnp.float32).transpose(2, 4, 0, 3, 1)
    shift = jnp.arange(rows)[None, :] - jnp.arange(sv)[:, None]
    band = sum(
        jnp.where((shift == b)[None, None, None, :, None, :], taps[:, :, :, b, None, :, None], 0.0)
        for b in range(3)
    )
    return band.reshape(9, out_c * sv, in_c * rows).astype(jnp.bfloat16)


def fine_kernel(p_ref, w_ref, *rest, sx, sv, ss, cout, head):
    if head:
        h_ref, o_ref = rest
    else:
        (o_ref,) = rest
    lanes = p_ref.shape[-1]
    for x in range(sx):
        acc = jnp.zeros((cout * sv, ss), jnp.float32)
        for a in range(3):
            slab = p_ref[x + a].astype(jnp.float32)
            for c in range(3):
                piece = slab if c == 0 else pltpu.roll(slab, lanes - c, 1)
                piece = piece[:, :ss].astype(jnp.bfloat16)
                acc = acc + jnp.dot(w_ref[a * 3 + c], piece, preferred_element_type=jnp.float32)
        act = (acc * jax.nn.sigmoid(acc)).astype(jnp.bfloat16)
        if head:
            res = jnp.dot(h_ref[...], act, preferred_element_type=jnp.float32)
            o_ref[:, x] = res.reshape(res.shape[0] // sv, sv, ss)
        else:
            o_ref[x] = act.astype(jnp.float32).reshape(cout, sv, ss)


def fine_conv(field, weight, head=None):
    sx, cin, sv, ss = field.shape
    cout = weight.shape[0]
    rows = round_up(sv + 2, 16)
    lanes = round_up(ss + 2, 128)
    padded = extended(field, FINE_SIDES, 1)
    padded = jnp.pad(padded, ((0, 0), (0, 0), (0, rows - sv - 2), (0, lanes - ss - 2)))
    padded = padded.reshape(sx + 2, cin * rows, lanes)
    operands = [padded, band_weights(weight, sv, rows)]
    if head is None:
        out_shape = jax.ShapeDtypeStruct((sx, cout, sv, ss), jnp.float32)
    else:
        eye = jnp.eye(sv, dtype=jnp.float32)
        kron = jnp.einsum("po,vw->pvow", head.astype(jnp.float32), eye)
        operands.append(kron.reshape(head.shape[0] * sv, cout * sv).astype(jnp.bfloat16))
        out_shape = jax.ShapeDtypeStruct((head.shape[0], sx, sv, ss), jnp.float32)
    kernel = lambda *refs: fine_kernel(
        *refs, sx=sx, sv=sv, ss=ss, cout=cout, head=head is not None
    )
    return pl.pallas_call(kernel, out_shape=out_shape)(*operands)


def conv_valid(padded, weight):
    return lax.conv_general_dilated(
        padded[None],
        weight,
        (1, 1, 1),
        "VALID",
        dimension_numbers=NUMS,
        preferred_element_type=jnp.float32,
    )[0]


def mid_conv(field, weight):
    padded = extended(field, MID_SIDES, 1)
    return conv_valid(padded, weight)


def conv_down(field, weight):
    return lax.conv_general_dilated(
        field[None],
        weight,
        (2, 2, 2),
        "VALID",
        dimension_numbers=NUMS,
        preferred_element_type=jnp.float32,
    )[0]


def fine_down(field, weight):
    sx, c, sv, ss = field.shape
    blocks = field.reshape(sx // 2, 2, c, sv // 2, 2, ss // 2, 2)
    return jnp.einsum("xaivbsc,oiabc->oxvs", blocks, weight, preferred_element_type=jnp.float32)


def fine_up(field, weight):
    outer = jnp.einsum("ixvs,ioabc->xaovbsc", field, weight, preferred_element_type=jnp.float32)
    chans, sx, sv, ss = (weight.shape[1], field.shape[1], field.shape[2], field.shape[3])
    return outer.reshape(2 * sx, chans, 2 * sv, 2 * ss)


def conv_up(field, weight):
    outer = jnp.einsum("ixvs,ioabc->oxavbsc", field, weight, preferred_element_type=jnp.float32)
    chans, sx, sv, ss = (weight.shape[1], field.shape[1], field.shape[2], field.shape[3])
    return outer.reshape(chans, 2 * sx, 2 * sv, 2 * ss)


def activate(value):
    return jax.nn.silu(value).astype(jnp.bfloat16)


def project(weight, field):
    return jnp.einsum("oc,cxp->oxp", weight, field, preferred_element_type=jnp.float32)


def normalize(block):
    values_f = block.astype(jnp.float32)
    mean_sq = jnp.mean(values_f * values_f, axis=0)
    return (values_f * lax.rsqrt(mean_sq + 1e-05)).astype(jnp.bfloat16)


def split_heads(weight, normed):
    chans, sx, count = normed.shape
    return project(weight, normed).astype(jnp.bfloat16).reshape(HEADS, chans // HEADS, sx, count)


def combine(queries, keys, values):
    scale = 1.0 / jnp.sqrt(jnp.float32(queries.shape[1]))
    scores = (
        jnp.einsum("hdxp,hdyp->hxyp", queries, keys, preferred_element_type=jnp.float32) * scale
    )
    weights = jax.nn.softmax(scores, axis=2).astype(jnp.bfloat16)
    attended = jnp.einsum("hxyp,hdyp->hdxp", weights, values, preferred_element_type=jnp.float32)
    heads, depth, sx, count = attended.shape
    return attended.astype(jnp.bfloat16).reshape(heads * depth, sx, count)


def finish(block, attended, w_attn_out):
    return (block.astype(jnp.float32) + project(w_attn_out, attended)).astype(jnp.bfloat16)


def on_device(
    inputs,
    w_in,
    w_fine_enc,
    w_down_mid,
    w_mid_enc,
    w_down_bottom,
    w_query,
    w_key,
    w_value,
    w_attn_out,
    w_up_mid,
    w_mid_dec,
    w_up_fine,
    w_fine_dec,
    w_head,
):
    fields = inputs.transpose(1, 0, 2, 3)
    first = fine_conv(fields, w_in).astype(jnp.bfloat16)
    fine_skip = fine_conv(first, w_fine_enc).astype(jnp.bfloat16)
    mid_in = activate(conv_down(fine_skip.transpose(1, 0, 2, 3), w_down_mid))
    mid_skip = activate(mid_conv(mid_in, unfold(w_mid_enc, 3, C1, C1)))
    bottom = activate(conv_down(mid_skip, unfold(w_down_bottom, 2, C2, C1)))
    chans, sx, sv, ss = bottom.shape
    flat = bottom.reshape(chans, sx, sv * ss)
    rows = lax.all_to_all(flat, "gx", split_axis=2, concat_axis=1, tiled=True)
    normed = normalize(rows)
    queries = split_heads(w_query, normed)
    keys = split_heads(w_key, normed)
    values = split_heads(w_value, normed)
    result = finish(rows, combine(queries, keys, values), w_attn_out)
    mixed = lax.all_to_all(result, "gx", split_axis=1, concat_axis=2, tiled=True)
    bottom_out = mixed.reshape(chans, sx, sv, ss)
    mid_up = (
        conv_up(bottom_out, unfold(w_up_mid, 2, C2, C1)) + mid_skip.astype(jnp.float32)
    ).astype(jnp.bfloat16)
    mid_dec = activate(mid_conv(mid_up, unfold(w_mid_dec, 3, C1, C1)))
    fine_up_field = (fine_up(mid_dec, w_up_fine) + fine_skip.astype(jnp.float32)).astype(
        jnp.bfloat16
    )
    return fine_conv(fine_up_field, w_fine_dec, head=w_head)


def solution(mesh):
    placed = (P(None, "gx", "gz", "gy"),) + (P(),) * 14
    return jax.shard_map(
        on_device, mesh=mesh, in_specs=placed, out_specs=P(None, "gx", "gz", "gy"), check_vma=False
    )
```

```python
import jax
import jax.numpy as jnp
from jax import lax
from jax.experimental import pallas as pl
from jax.experimental.pallas import tpu as pltpu
from jax.sharding import PartitionSpec as P

C1 = 64
C2 = 256
HEADS = 4


NUMS = ("NCDHW", "OIDHW", "NCDHW")
FINE_SIDES = (("gx", 0), ("gy", 3), ("gz", 2))
MID_SIDES = (("gx", 1), ("gy", 3), ("gz", 2))


def extended(block, sides, width):
    for axis, dim in sides:
        count = lax.axis_size(axis)
        forward = [(i, i + 1) for i in range(count - 1)]
        backward = [(target, source) for source, target in forward]
        low = lax.ppermute(
            lax.slice_in_dim(block, block.shape[dim] - width, None, axis=dim), axis, forward
        )
        high = lax.ppermute(lax.slice_in_dim(block, 0, width, axis=dim), axis, backward)
        block = jnp.concatenate([low, block, high], axis=dim)
    return block


def unfold(weight, side, first, second):
    return weight.reshape(side, side, side, first, second).transpose(3, 4, 0, 1, 2)


def round_up(value, step):
    return (value + step - 1) // step * step


def fine_kernel(p_ref, w_ref, *rest, sx, sv, ss, rows, head):
    if head:
        h_ref, o_ref, band_ref = rest
    else:
        o_ref, band_ref = rest
    cout, cin = w_ref.shape[1:]
    depth = cin * rows
    lanes = p_ref.shape[-1]
    sv_bits, row_bits = sv.bit_length() - 1, rows.bit_length() - 1
    r = lax.broadcasted_iota(jnp.int32, (cout * sv, cout), 0)
    q = lax.broadcasted_iota(jnp.int32, (cout * sv, cout), 1)
    widen_rows = ((r >> sv_bits) == q).astype(jnp.bfloat16)
    r = lax.broadcasted_iota(jnp.int32, (cin, depth), 0)
    q = lax.broadcasted_iota(jnp.int32, (cin, depth), 1)
    widen_cols = ((q >> row_bits) == r).astype(jnp.bfloat16)
    r = lax.broadcasted_iota(jnp.int32, (cout * sv, depth), 0)
    q = lax.broadcasted_iota(jnp.int32, (cout * sv, depth), 1)
    offset = (q & (rows - 1)) - (r & (sv - 1))
    for a in range(3):
        for c in range(3):
            band = jnp.zeros((cout * sv, depth), jnp.float32)
            for b in range(3):
                tap = w_ref[(a * 3 + b) * 3 + c]
                grown = jnp.dot(widen_rows, tap, preferred_element_type=jnp.float32)
                grown = jnp.dot(
                    grown.astype(jnp.bfloat16), widen_cols, preferred_element_type=jnp.float32
                )
                band = band + jnp.where(offset == b, grown, 0.0)
            band_ref[a * 3 + c] = band.astype(jnp.bfloat16)
    for x in range(sx):
        acc = jnp.zeros((cout * sv, ss), jnp.float32)
        for a in range(3):
            slab = p_ref[x + a].astype(jnp.float32)
            for c in range(3):
                piece = slab if c == 0 else pltpu.roll(slab, lanes - c, 1)
                piece = piece[:, :ss].astype(jnp.bfloat16)
                acc = acc + jnp.dot(band_ref[a * 3 + c], piece, preferred_element_type=jnp.float32)
        act = (acc * jax.nn.sigmoid(acc)).astype(jnp.bfloat16)
        if head:
            res = jnp.dot(h_ref[...], act, preferred_element_type=jnp.float32)
            o_ref[:, x] = res.reshape(res.shape[0] // sv, sv, ss)
        else:
            o_ref[x] = act.astype(jnp.float32).reshape(cout, sv, ss)


def fine_conv(field, weight, head=None):
    sx, cin, sv, ss = field.shape
    cout = weight.shape[0]
    rows = round_up(sv + 2, 16)
    lanes = round_up(ss + 2, 128)
    padded = extended(field, FINE_SIDES, 1)
    padded = jnp.pad(padded, ((0, 0), (0, 0), (0, rows - sv - 2), (0, lanes - ss - 2)))
    padded = padded.reshape(sx + 2, cin * rows, lanes)
    operands = [padded, weight.transpose(2, 3, 4, 0, 1).reshape(27, cout, cin)]
    if head is None:
        out_shape = jax.ShapeDtypeStruct((sx, cout, sv, ss), jnp.float32)
    else:
        eye = jnp.eye(sv, dtype=jnp.float32)
        kron = jnp.einsum("po,vw->pvow", head.astype(jnp.float32), eye)
        operands.append(kron.reshape(head.shape[0] * sv, cout * sv).astype(jnp.bfloat16))
        out_shape = jax.ShapeDtypeStruct((head.shape[0], sx, sv, ss), jnp.float32)
    kernel = lambda *refs: fine_kernel(
        *refs, sx=sx, sv=sv, ss=ss, rows=rows, head=head is not None
    )
    return pl.pallas_call(
        kernel,
        out_shape=out_shape,
        scratch_shapes=[pltpu.VMEM((9, cout * sv, cin * rows), jnp.bfloat16)],
    )(*operands)


def conv_valid(padded, weight):
    return lax.conv_general_dilated(
        padded[None],
        weight,
        (1, 1, 1),
        "VALID",
        dimension_numbers=NUMS,
        preferred_element_type=jnp.float32,
    )[0]


def mid_conv(field, weight):
    padded = extended(field, MID_SIDES, 1)
    return conv_valid(padded, weight)


def conv_down(field, weight):
    return lax.conv_general_dilated(
        field[None],
        weight,
        (2, 2, 2),
        "VALID",
        dimension_numbers=NUMS,
        preferred_element_type=jnp.float32,
    )[0]


def fine_down(field, weight):
    sx, c, sv, ss = field.shape
    blocks = field.reshape(sx // 2, 2, c, sv // 2, 2, ss // 2, 2)
    return jnp.einsum("xaivbsc,oiabc->oxvs", blocks, weight, preferred_element_type=jnp.float32)


def fine_up(field, weight):
    outer = jnp.einsum("ixvs,ioabc->xaovbsc", field, weight, preferred_element_type=jnp.float32)
    chans, sx, sv, ss = (weight.shape[1], field.shape[1], field.shape[2], field.shape[3])
    return outer.reshape(2 * sx, chans, 2 * sv, 2 * ss)


def conv_up(field, weight):
    outer = jnp.einsum("ixvs,ioabc->oxavbsc", field, weight, preferred_element_type=jnp.float32)
    chans, sx, sv, ss = (weight.shape[1], field.shape[1], field.shape[2], field.shape[3])
    return outer.reshape(chans, 2 * sx, 2 * sv, 2 * ss)


def activate(value):
    return jax.nn.silu(value).astype(jnp.bfloat16)


def project(weight, field):
    return jnp.einsum("oc,cxp->oxp", weight, field, preferred_element_type=jnp.float32)


def normalize(block):
    values_f = block.astype(jnp.float32)
    mean_sq = jnp.mean(values_f * values_f, axis=0)
    return (values_f * lax.rsqrt(mean_sq + 1e-05)).astype(jnp.bfloat16)


def split_heads(weight, normed):
    chans, sx, count = normed.shape
    return project(weight, normed).astype(jnp.bfloat16).reshape(HEADS, chans // HEADS, sx, count)


def combine(queries, keys, values):
    scale = 1.0 / jnp.sqrt(jnp.float32(queries.shape[1]))
    scores = (
        jnp.einsum("hdxp,hdyp->hxyp", queries, keys, preferred_element_type=jnp.float32) * scale
    )
    weights = jax.nn.softmax(scores, axis=2).astype(jnp.bfloat16)
    attended = jnp.einsum("hxyp,hdyp->hdxp", weights, values, preferred_element_type=jnp.float32)
    heads, depth, sx, count = attended.shape
    return attended.astype(jnp.bfloat16).reshape(heads * depth, sx, count)


def finish(block, attended, w_attn_out):
    return (block.astype(jnp.float32) + project(w_attn_out, attended)).astype(jnp.bfloat16)


def on_device(
    inputs,
    w_in,
    w_fine_enc,
    w_down_mid,
    w_mid_enc,
    w_down_bottom,
    w_query,
    w_key,
    w_value,
    w_attn_out,
    w_up_mid,
    w_mid_dec,
    w_up_fine,
    w_fine_dec,
    w_head,
):
    fields = inputs.transpose(1, 0, 2, 3)
    first = fine_conv(fields, w_in).astype(jnp.bfloat16)
    fine_skip = fine_conv(first, w_fine_enc).astype(jnp.bfloat16)
    mid_in = activate(fine_down(fine_skip, w_down_mid))
    mid_skip = activate(mid_conv(mid_in, unfold(w_mid_enc, 3, C1, C1)))
    bottom = activate(conv_down(mid_skip, unfold(w_down_bottom, 2, C2, C1)))
    chans, sx, sv, ss = bottom.shape
    flat = bottom.reshape(chans, sx, sv * ss)
    rows = lax.all_to_all(flat, "gx", split_axis=2, concat_axis=1, tiled=True)
    normed = normalize(rows)
    queries = split_heads(w_query, normed)
    keys = split_heads(w_key, normed)
    values = split_heads(w_value, normed)
    result = finish(rows, combine(queries, keys, values), w_attn_out)
    mixed = lax.all_to_all(result, "gx", split_axis=1, concat_axis=2, tiled=True)
    bottom_out = mixed.reshape(chans, sx, sv, ss)
    mid_up = (
        conv_up(bottom_out, unfold(w_up_mid, 2, C2, C1)) + mid_skip.astype(jnp.float32)
    ).astype(jnp.bfloat16)
    mid_dec = activate(mid_conv(mid_up, unfold(w_mid_dec, 3, C1, C1)))
    fine_up_field = (fine_up(mid_dec, w_up_fine) + fine_skip.astype(jnp.float32)).astype(
        jnp.bfloat16
    )
    return fine_conv(fine_up_field, w_fine_dec, head=w_head)


def solution(mesh):
    placed = (P(None, "gx", "gz", "gy"),) + (P(),) * 14
    return jax.shard_map(
        on_device, mesh=mesh, in_specs=placed, out_specs=P(None, "gx", "gz", "gy"), check_vma=False
    )
```

```python
import jax
import jax.numpy as jnp
from jax import lax
from jax.experimental import pallas as pl
from jax.experimental.pallas import tpu as pltpu
from jax.sharding import PartitionSpec as P

C1 = 64
C2 = 256
HEADS = 4


NUMS = ("NCDHW", "OIDHW", "NCDHW")
FINE_SIDES = (("gx", 0, 1), ("gy", 3, 1), ("gz", 2, 1))
FINE_CROSS = (("gy", 3, 1), ("gz", 2, 1))
MID_SIDES = (("gx", 1, 1), ("gy", 3, 1), ("gz", 2, 1))
MID_CROSS = (("gy", 3, 1), ("gz", 2, 1))


def extended(block, sides):
    for axis, dim, width in sides:
        count = lax.axis_size(axis)
        top = lax.slice_in_dim(block, block.shape[dim] - width, None, axis=dim)
        bottom = lax.slice_in_dim(block, 0, width, axis=dim)
        if count == 2:
            first = lax.axis_index(axis) == 0
            got = lax.ppermute(jnp.where(first, top, bottom), axis, [(0, 1), (1, 0)])
            low = jnp.where(first, jnp.zeros_like(got), got)
            high = jnp.where(first, got, jnp.zeros_like(got))
        else:
            forward = [(i, i + 1) for i in range(count - 1)]
            backward = [(target, source) for source, target in forward]
            low = lax.ppermute(top, axis, forward)
            high = lax.ppermute(bottom, axis, backward)
        block = jnp.concatenate([low, block, high], axis=dim)
    return block


def inside_rows(field, offset):
    rows = field.shape[0]
    start = lax.axis_index("gx") * (rows + 2 * offset) + offset
    index = start + jnp.arange(rows)
    keep = (index >= 0) & (index < (rows + 2 * offset) * lax.axis_size("gx"))
    return jnp.where(keep[:, None, None, None], field, jnp.zeros_like(field))


def unfold(weight, side, first, second):
    return weight.reshape(side, side, side, first, second).transpose(3, 4, 0, 1, 2)


def round_up(value, step):
    return (value + step - 1) // step * step


def fine_kernel(p_ref, w_ref, *rest, sx, sv, ss, rows, head):
    if head:
        h_ref, o_ref, band_ref = rest
    else:
        o_ref, band_ref = rest
    cout, cin = w_ref.shape[1:]
    depth = cin * rows
    lanes = p_ref.shape[-1]
    sv_bits, row_bits = sv.bit_length() - 1, rows.bit_length() - 1
    r = lax.broadcasted_iota(jnp.int32, (cout * sv, cout), 0)
    q = lax.broadcasted_iota(jnp.int32, (cout * sv, cout), 1)
    widen_rows = ((r >> sv_bits) == q).astype(jnp.bfloat16)
    r = lax.broadcasted_iota(jnp.int32, (cin, depth), 0)
    q = lax.broadcasted_iota(jnp.int32, (cin, depth), 1)
    widen_cols = ((q >> row_bits) == r).astype(jnp.bfloat16)
    r = lax.broadcasted_iota(jnp.int32, (cout * sv, depth), 0)
    q = lax.broadcasted_iota(jnp.int32, (cout * sv, depth), 1)
    offset = (q & (rows - 1)) - (r & (sv - 1))
    for a in range(3):
        for c in range(3):
            band = jnp.zeros((cout * sv, depth), jnp.float32)
            for b in range(3):
                tap = w_ref[(a * 3 + b) * 3 + c]
                grown = jnp.dot(widen_rows, tap, preferred_element_type=jnp.float32)
                grown = jnp.dot(
                    grown.astype(jnp.bfloat16), widen_cols, preferred_element_type=jnp.float32
                )
                band = band + jnp.where(offset == b, grown, 0.0)
            band_ref[a * 3 + c] = band.astype(jnp.bfloat16)
    def row(x, carry):
        acc = jnp.zeros((cout * sv, ss), jnp.float32)
        for a in range(3):
            slab = p_ref[x + a].astype(jnp.float32)
            for c in range(3):
                piece = slab if c == 0 else pltpu.roll(slab, lanes - c, 1)
                piece = piece[:, :ss].astype(jnp.bfloat16)
                acc = acc + jnp.dot(band_ref[a * 3 + c], piece, preferred_element_type=jnp.float32)
        act = (acc * jax.nn.sigmoid(acc)).astype(jnp.bfloat16)
        if head:
            res = jnp.dot(h_ref[...], act, preferred_element_type=jnp.float32)
            o_ref[:, x] = res.reshape(res.shape[0] // sv, sv, ss)
        else:
            o_ref[x] = act.astype(jnp.float32).reshape(cout, sv, ss)
        return carry

    lax.fori_loop(0, sx, row, 0)


def fine_conv(field, weight, sides, head=None):
    _, cin, sv, ss = field.shape
    cout = weight.shape[0]
    rows = round_up(sv + 2, 16)
    lanes = round_up(ss + 2, 128)
    padded = extended(field, sides)
    sx = padded.shape[0] - 2
    padded = jnp.pad(padded, ((0, 0), (0, 0), (0, rows - sv - 2), (0, lanes - ss - 2)))
    padded = padded.reshape(sx + 2, cin * rows, lanes)
    operands = [padded, weight.transpose(2, 3, 4, 0, 1).reshape(27, cout, cin)]
    if head is None:
        out_shape = jax.ShapeDtypeStruct((sx, cout, sv, ss), jnp.float32)
    else:
        eye = jnp.eye(sv, dtype=jnp.float32)
        kron = jnp.einsum("po,vw->pvow", head.astype(jnp.float32), eye)
        operands.append(kron.reshape(head.shape[0] * sv, cout * sv).astype(jnp.bfloat16))
        out_shape = jax.ShapeDtypeStruct((head.shape[0], sx, sv, ss), jnp.float32)
    kernel = lambda *refs: fine_kernel(
        *refs, sx=sx, sv=sv, ss=ss, rows=rows, head=head is not None
    )
    return pl.pallas_call(
        kernel,
        out_shape=out_shape,
        scratch_shapes=[pltpu.VMEM((9, cout * sv, cin * rows), jnp.bfloat16)],
    )(*operands)


def conv_valid(padded, weight):
    return lax.conv_general_dilated(
        padded[None],
        weight,
        (1, 1, 1),
        "VALID",
        dimension_numbers=NUMS,
        preferred_element_type=jnp.float32,
    )[0]


def mid_conv(field, weight, sides=MID_SIDES):
    padded = extended(field, sides)
    return conv_valid(padded, weight)


def conv_down(field, weight):
    return lax.conv_general_dilated(
        field[None],
        weight,
        (2, 2, 2),
        "VALID",
        dimension_numbers=NUMS,
        preferred_element_type=jnp.float32,
    )[0]


def fine_down(field, weight):
    sx, c, sv, ss = field.shape
    blocks = field.reshape(sx // 2, 2, c, sv // 2, 2, ss // 2, 2)
    return jnp.einsum("xaivbsc,oiabc->oxvs", blocks, weight, preferred_element_type=jnp.float32)


def fine_up(field, weight):
    outer = jnp.einsum("ixvs,ioabc->xaovbsc", field, weight, preferred_element_type=jnp.float32)
    chans, sx, sv, ss = (weight.shape[1], field.shape[1], field.shape[2], field.shape[3])
    return outer.reshape(2 * sx, chans, 2 * sv, 2 * ss)


def conv_up(field, weight):
    outer = jnp.einsum("ixvs,ioabc->oxavbsc", field, weight, preferred_element_type=jnp.float32)
    chans, sx, sv, ss = (weight.shape[1], field.shape[1], field.shape[2], field.shape[3])
    return outer.reshape(chans, 2 * sx, 2 * sv, 2 * ss)


def activate(value):
    return jax.nn.silu(value).astype(jnp.bfloat16)


def project(weight, field):
    return jnp.einsum("oc,cxp->oxp", weight, field, preferred_element_type=jnp.float32)


def normalize(block):
    values_f = block.astype(jnp.float32)
    mean_sq = jnp.mean(values_f * values_f, axis=0)
    return (values_f * lax.rsqrt(mean_sq + 1e-05)).astype(jnp.bfloat16)


def split_heads(weight, normed):
    chans, sx, count = normed.shape
    return project(weight, normed).astype(jnp.bfloat16).reshape(HEADS, chans // HEADS, sx, count)


def combine(queries, keys, values):
    scale = 1.0 / jnp.sqrt(jnp.float32(queries.shape[1]))
    scores = (
        jnp.einsum("hdxp,hdyp->hxyp", queries, keys, preferred_element_type=jnp.float32) * scale
    )
    weights = jax.nn.softmax(scores, axis=2).astype(jnp.bfloat16)
    attended = jnp.einsum("hxyp,hdyp->hdxp", weights, values, preferred_element_type=jnp.float32)
    heads, depth, sx, count = attended.shape
    return attended.astype(jnp.bfloat16).reshape(heads * depth, sx, count)


def finish(block, attended, w_attn_out):
    return (block.astype(jnp.float32) + project(w_attn_out, attended)).astype(jnp.bfloat16)


def on_device(
    inputs,
    w_in,
    w_fine_enc,
    w_down_mid,
    w_mid_enc,
    w_down_bottom,
    w_query,
    w_key,
    w_value,
    w_attn_out,
    w_up_mid,
    w_mid_dec,
    w_up_fine,
    w_fine_dec,
    w_head,
):
    fields = extended(inputs.transpose(1, 0, 2, 3), (("gx", 0, 4),))
    first = inside_rows(fine_conv(fields, w_in, FINE_CROSS).astype(jnp.bfloat16), -3)
    fine_wide = inside_rows(fine_conv(first, w_fine_enc, FINE_CROSS).astype(jnp.bfloat16), -2)
    fine_skip = fine_wide[2:-2]
    mid_in = activate(fine_down(fine_wide, w_down_mid))
    mid_skip = activate(mid_conv(mid_in, unfold(w_mid_enc, 3, C1, C1), MID_CROSS))
    bottom = activate(conv_down(mid_skip, unfold(w_down_bottom, 2, C2, C1)))
    chans, sx, sv, ss = bottom.shape
    flat = bottom.reshape(chans, sx, sv * ss)
    rows = lax.all_to_all(flat, "gx", split_axis=2, concat_axis=1, tiled=True)
    normed = normalize(rows)
    queries = split_heads(w_query, normed)
    keys = split_heads(w_key, normed)
    values = split_heads(w_value, normed)
    result = finish(rows, combine(queries, keys, values), w_attn_out)
    mixed = lax.all_to_all(result, "gx", split_axis=1, concat_axis=2, tiled=True)
    bottom_out = mixed.reshape(chans, sx, sv, ss)
    mid_up = (
        conv_up(bottom_out, unfold(w_up_mid, 2, C2, C1)) + mid_skip.astype(jnp.float32)
    ).astype(jnp.bfloat16)
    mid_dec = activate(mid_conv(mid_up, unfold(w_mid_dec, 3, C1, C1)))
    fine_up_field = (fine_up(mid_dec, w_up_fine) + fine_skip.astype(jnp.float32)).astype(
        jnp.bfloat16
    )
    return fine_conv(fine_up_field, w_fine_dec, FINE_SIDES, head=w_head)


def solution(mesh):
    placed = (P(None, "gx", "gz", "gy"),) + (P(),) * 14
    return jax.shard_map(
        on_device, mesh=mesh, in_specs=placed, out_specs=P(None, "gx", "gz", "gy"), check_vma=False
    )
```

```python
import jax
import jax.numpy as jnp
from jax import lax
from jax.experimental import pallas as pl
from jax.experimental.pallas import tpu as pltpu
from jax.sharding import PartitionSpec as P

C1 = 64
C2 = 256
HEADS = 4


NUMS = ("NCDHW", "OIDHW", "NCDHW")
FINE_SIDES = (("gx", 0, 1), ("gy", 3, 1), ("gz", 2, 1))
FINE_CROSS = (("gy", 3, 1), ("gz", 2, 1))
MID_SIDES = (("gx", 1, 1), ("gy", 3, 1), ("gz", 2, 1))
MID_CROSS = (("gy", 3, 1), ("gz", 2, 1))


def extended(block, sides):
    for axis, dim, width in sides:
        count = lax.axis_size(axis)
        top = lax.slice_in_dim(block, block.shape[dim] - width, None, axis=dim)
        bottom = lax.slice_in_dim(block, 0, width, axis=dim)
        if count == 2:
            first = lax.axis_index(axis) == 0
            got = lax.ppermute(jnp.where(first, top, bottom), axis, [(0, 1), (1, 0)])
            low = jnp.where(first, jnp.zeros_like(got), got)
            high = jnp.where(first, got, jnp.zeros_like(got))
        else:
            forward = [(i, i + 1) for i in range(count - 1)]
            backward = [(target, source) for source, target in forward]
            low = lax.ppermute(top, axis, forward)
            high = lax.ppermute(bottom, axis, backward)
        block = jnp.concatenate([low, block, high], axis=dim)
    return block


def inside_rows(field, offset):
    rows = field.shape[0]
    start = lax.axis_index("gx") * (rows + 2 * offset) + offset
    index = start + jnp.arange(rows)
    keep = (index >= 0) & (index < (rows + 2 * offset) * lax.axis_size("gx"))
    return jnp.where(keep[:, None, None, None], field, jnp.zeros_like(field))


def unfold(weight, side, first, second):
    return weight.reshape(side, side, side, first, second).transpose(3, 4, 0, 1, 2)


def round_up(value, step):
    return (value + step - 1) // step * step


def fine_kernel(p_ref, w_ref, *rest, sx, sv, ss, rows, head):
    if head:
        h_ref, o_ref, band_ref, shifted_ref = rest
    else:
        o_ref, band_ref, shifted_ref = rest
    cout, cin = w_ref.shape[1:]
    depth = cin * rows
    lanes = p_ref.shape[-1]
    sv_bits, row_bits = sv.bit_length() - 1, rows.bit_length() - 1
    r = lax.broadcasted_iota(jnp.int32, (cout * sv, cout), 0)
    q = lax.broadcasted_iota(jnp.int32, (cout * sv, cout), 1)
    widen_rows = ((r >> sv_bits) == q).astype(jnp.bfloat16)
    r = lax.broadcasted_iota(jnp.int32, (cin, depth), 0)
    q = lax.broadcasted_iota(jnp.int32, (cin, depth), 1)
    widen_cols = ((q >> row_bits) == r).astype(jnp.bfloat16)
    r = lax.broadcasted_iota(jnp.int32, (cout * sv, depth), 0)
    q = lax.broadcasted_iota(jnp.int32, (cout * sv, depth), 1)
    offset = (q & (rows - 1)) - (r & (sv - 1))
    for a in range(3):
        for c in range(3):
            band = jnp.zeros((cout * sv, depth), jnp.float32)
            for b in range(3):
                tap = w_ref[(a * 3 + b) * 3 + c]
                grown = jnp.dot(widen_rows, tap, preferred_element_type=jnp.float32)
                grown = jnp.dot(
                    grown.astype(jnp.bfloat16), widen_cols, preferred_element_type=jnp.float32
                )
                band = band + jnp.where(offset == b, grown, 0.0)
            band_ref[:, pl.ds((a * 3 + c) * depth, depth)] = band.astype(jnp.bfloat16)

    def shift(x, carry):
        slab = p_ref[x].astype(jnp.float32)
        for c in range(3):
            piece = slab if c == 0 else pltpu.roll(slab, lanes - c, 1)
            shifted_ref[x, c] = piece[:, :ss].astype(jnp.bfloat16)
        return carry

    lax.fori_loop(0, sx + 2, shift, 0)

    def row(x, carry):
        stack = shifted_ref[pl.ds(x, 3)].reshape(9 * depth, ss)
        acc = jnp.dot(band_ref[...], stack, preferred_element_type=jnp.float32)
        act = (acc * jax.nn.sigmoid(acc)).astype(jnp.bfloat16)
        if head:
            res = jnp.dot(h_ref[...], act, preferred_element_type=jnp.float32)
            o_ref[:, x] = res.reshape(res.shape[0] // sv, sv, ss)
        else:
            o_ref[x] = act.astype(jnp.float32).reshape(cout, sv, ss)
        return carry

    lax.fori_loop(0, sx, row, 0)


def fine_conv(field, weight, sides, head=None):
    _, cin, sv, ss = field.shape
    cout = weight.shape[0]
    rows = round_up(sv + 2, 16)
    lanes = round_up(ss + 2, 128)
    wide = round_up(cin * rows, 128) // rows
    padded = extended(field, sides)
    sx = padded.shape[0] - 2
    padded = jnp.pad(
        padded, ((0, 0), (0, wide - cin), (0, rows - sv - 2), (0, lanes - ss - 2))
    )
    padded = padded.reshape(sx + 2, wide * rows, lanes)
    taps = jnp.pad(weight, ((0, 0), (0, wide - cin), (0, 0), (0, 0), (0, 0)))
    operands = [padded, taps.transpose(2, 3, 4, 0, 1).reshape(27, cout, wide)]
    if head is None:
        out_shape = jax.ShapeDtypeStruct((sx, cout, sv, ss), jnp.float32)
    else:
        eye = jnp.eye(sv, dtype=jnp.float32)
        kron = jnp.einsum("po,vw->pvow", head.astype(jnp.float32), eye)
        operands.append(kron.reshape(head.shape[0] * sv, cout * sv).astype(jnp.bfloat16))
        out_shape = jax.ShapeDtypeStruct((head.shape[0], sx, sv, ss), jnp.float32)
    kernel = lambda *refs: fine_kernel(
        *refs, sx=sx, sv=sv, ss=ss, rows=rows, head=head is not None
    )
    return pl.pallas_call(
        kernel,
        out_shape=out_shape,
        scratch_shapes=[
            pltpu.VMEM((cout * sv, 9 * wide * rows), jnp.bfloat16),
            pltpu.VMEM((sx + 2, 3, wide * rows, ss), jnp.bfloat16),
        ],
    )(*operands)


def conv_valid(padded, weight):
    return lax.conv_general_dilated(
        padded[None],
        weight,
        (1, 1, 1),
        "VALID",
        dimension_numbers=NUMS,
        preferred_element_type=jnp.float32,
    )[0]


def mid_conv(field, weight, sides=MID_SIDES):
    padded = extended(field, sides)
    return conv_valid(padded, weight)


def conv_down(field, weight):
    return lax.conv_general_dilated(
        field[None],
        weight,
        (2, 2, 2),
        "VALID",
        dimension_numbers=NUMS,
        preferred_element_type=jnp.float32,
    )[0]


def fine_down(field, weight):
    sx, c, sv, ss = field.shape
    blocks = field.reshape(sx // 2, 2, c, sv // 2, 2, ss // 2, 2)
    return jnp.einsum("xaivbsc,oiabc->oxvs", blocks, weight, preferred_element_type=jnp.float32)


def fine_up(field, weight):
    outer = jnp.einsum("ixvs,ioabc->xaovbsc", field, weight, preferred_element_type=jnp.float32)
    chans, sx, sv, ss = (weight.shape[1], field.shape[1], field.shape[2], field.shape[3])
    return outer.reshape(2 * sx, chans, 2 * sv, 2 * ss)


def conv_up(field, weight):
    outer = jnp.einsum("ixvs,ioabc->oxavbsc", field, weight, preferred_element_type=jnp.float32)
    chans, sx, sv, ss = (weight.shape[1], field.shape[1], field.shape[2], field.shape[3])
    return outer.reshape(chans, 2 * sx, 2 * sv, 2 * ss)


def activate(value):
    return jax.nn.silu(value).astype(jnp.bfloat16)


def project(weight, field):
    return jnp.einsum("oc,cxp->oxp", weight, field, preferred_element_type=jnp.float32)


def normalize(block):
    values_f = block.astype(jnp.float32)
    mean_sq = jnp.mean(values_f * values_f, axis=0)
    return (values_f * lax.rsqrt(mean_sq + 1e-05)).astype(jnp.bfloat16)


def split_heads(weight, normed):
    chans, sx, count = normed.shape
    return project(weight, normed).astype(jnp.bfloat16).reshape(HEADS, chans // HEADS, sx, count)


def combine(queries, keys, values):
    scale = 1.0 / jnp.sqrt(jnp.float32(queries.shape[1]))
    scores = (
        jnp.einsum("hdxp,hdyp->hxyp", queries, keys, preferred_element_type=jnp.float32) * scale
    )
    weights = jax.nn.softmax(scores, axis=2).astype(jnp.bfloat16)
    attended = jnp.einsum("hxyp,hdyp->hdxp", weights, values, preferred_element_type=jnp.float32)
    heads, depth, sx, count = attended.shape
    return attended.astype(jnp.bfloat16).reshape(heads * depth, sx, count)


def finish(block, attended, w_attn_out):
    return (block.astype(jnp.float32) + project(w_attn_out, attended)).astype(jnp.bfloat16)


def on_device(
    inputs,
    w_in,
    w_fine_enc,
    w_down_mid,
    w_mid_enc,
    w_down_bottom,
    w_query,
    w_key,
    w_value,
    w_attn_out,
    w_up_mid,
    w_mid_dec,
    w_up_fine,
    w_fine_dec,
    w_head,
):
    fields = extended(inputs.transpose(1, 0, 2, 3), (("gx", 0, 4),))
    first = inside_rows(fine_conv(fields, w_in, FINE_CROSS).astype(jnp.bfloat16), -3)
    fine_wide = inside_rows(fine_conv(first, w_fine_enc, FINE_CROSS).astype(jnp.bfloat16), -2)
    fine_skip = fine_wide[2:-2]
    mid_in = activate(fine_down(fine_wide, w_down_mid))
    mid_skip = activate(mid_conv(mid_in, unfold(w_mid_enc, 3, C1, C1), MID_CROSS))
    bottom = activate(conv_down(mid_skip, unfold(w_down_bottom, 2, C2, C1)))
    chans, sx, sv, ss = bottom.shape
    flat = bottom.reshape(chans, sx, sv * ss)
    rows = lax.all_to_all(flat, "gx", split_axis=2, concat_axis=1, tiled=True)
    normed = normalize(rows)
    queries = split_heads(w_query, normed)
    keys = split_heads(w_key, normed)
    values = split_heads(w_value, normed)
    result = finish(rows, combine(queries, keys, values), w_attn_out)
    mixed = lax.all_to_all(result, "gx", split_axis=1, concat_axis=2, tiled=True)
    bottom_out = mixed.reshape(chans, sx, sv, ss)
    mid_up = (
        conv_up(bottom_out, unfold(w_up_mid, 2, C2, C1)) + mid_skip.astype(jnp.float32)
    ).astype(jnp.bfloat16)
    mid_dec = activate(mid_conv(mid_up, unfold(w_mid_dec, 3, C1, C1)))
    fine_up_field = (fine_up(mid_dec, w_up_fine) + fine_skip.astype(jnp.float32)).astype(
        jnp.bfloat16
    )
    return fine_conv(fine_up_field, w_fine_dec, FINE_SIDES, head=w_head)


def solution(mesh):
    placed = (P(None, "gx", "gz", "gy"),) + (P(),) * 14
    return jax.shard_map(
        on_device, mesh=mesh, in_specs=placed, out_specs=P(None, "gx", "gz", "gy"), check_vma=False
    )
```

```python
import jax
import jax.numpy as jnp
from jax import lax
from jax.experimental import pallas as pl
from jax.experimental.pallas import tpu as pltpu
from jax.sharding import PartitionSpec as P

C1 = 64
C2 = 256
HEADS = 4


NUMS = ("NCDHW", "OIDHW", "NCDHW")
FINE_SIDES = (("gx", 0, 1), ("gy", 3, 1), ("gz", 2, 1))
FINE_CROSS = (("gy", 3, 1), ("gz", 2, 1))
MID_SIDES = (("gx", 1, 1), ("gy", 3, 1), ("gz", 2, 1))
MID_CROSS = (("gy", 3, 1), ("gz", 2, 1))


def extended(block, sides):
    for axis, dim, width in sides:
        count = lax.axis_size(axis)
        top = lax.slice_in_dim(block, block.shape[dim] - width, None, axis=dim)
        bottom = lax.slice_in_dim(block, 0, width, axis=dim)
        if count == 2:
            first = lax.axis_index(axis) == 0
            got = lax.ppermute(jnp.where(first, top, bottom), axis, [(0, 1), (1, 0)])
            low = jnp.where(first, jnp.zeros_like(got), got)
            high = jnp.where(first, got, jnp.zeros_like(got))
        else:
            forward = [(i, i + 1) for i in range(count - 1)]
            backward = [(target, source) for source, target in forward]
            low = lax.ppermute(top, axis, forward)
            high = lax.ppermute(bottom, axis, backward)
        block = jnp.concatenate([low, block, high], axis=dim)
    return block


def inside_rows(field, offset):
    rows = field.shape[0]
    start = lax.axis_index("gx") * (rows + 2 * offset) + offset
    index = start + jnp.arange(rows)
    keep = (index >= 0) & (index < (rows + 2 * offset) * lax.axis_size("gx"))
    return jnp.where(keep[:, None, None, None], field, jnp.zeros_like(field))


def unfold(weight, side, first, second):
    return weight.reshape(side, side, side, first, second).transpose(3, 4, 0, 1, 2)


def round_up(value, step):
    return (value + step - 1) // step * step


def fine_kernel(p_ref, w_ref, *rest, sx, sv, ss, rows, head):
    if head:
        h_ref, o_ref, band_ref, shifted_ref = rest
    else:
        o_ref, band_ref, shifted_ref = rest
    cout, cin = w_ref.shape[1:]
    depth = cin * rows
    lanes = p_ref.shape[-1]
    sv_bits, row_bits = sv.bit_length() - 1, rows.bit_length() - 1
    r = lax.broadcasted_iota(jnp.int32, (cout * sv, cout), 0)
    q = lax.broadcasted_iota(jnp.int32, (cout * sv, cout), 1)
    widen_rows = ((r >> sv_bits) == q).astype(jnp.bfloat16)
    r = lax.broadcasted_iota(jnp.int32, (cin, depth), 0)
    q = lax.broadcasted_iota(jnp.int32, (cin, depth), 1)
    widen_cols = ((q >> row_bits) == r).astype(jnp.bfloat16)
    r = lax.broadcasted_iota(jnp.int32, (cout * sv, depth), 0)
    q = lax.broadcasted_iota(jnp.int32, (cout * sv, depth), 1)
    offset = (q & (rows - 1)) - (r & (sv - 1))
    for a in range(3):
        for c in range(3):
            band = jnp.zeros((cout * sv, depth), jnp.float32)
            for b in range(3):
                tap = w_ref[(a * 3 + b) * 3 + c]
                grown = jnp.dot(widen_rows, tap, preferred_element_type=jnp.float32)
                grown = jnp.dot(
                    grown.astype(jnp.bfloat16), widen_cols, preferred_element_type=jnp.float32
                )
                band = band + jnp.where(offset == b, grown, 0.0)
            band_ref[:, pl.ds((a * 3 + c) * depth, depth)] = band.astype(jnp.bfloat16)

    def shift(x, carry):
        slab = p_ref[x].astype(jnp.float32)
        for c in range(3):
            piece = slab if c == 0 else pltpu.roll(slab, lanes - c, 1)
            shifted_ref[x, c] = piece[:, :ss].astype(jnp.bfloat16)
        return carry

    lax.fori_loop(0, sx + 2, shift, 0)

    def row(x, carry):
        stack = shifted_ref[pl.ds(x, 3)].reshape(9 * depth, ss)
        acc = jnp.dot(band_ref[...], stack, preferred_element_type=jnp.float32)
        act = (acc * jax.nn.sigmoid(acc)).astype(jnp.bfloat16)
        if head:
            res = jnp.dot(h_ref[...], act, preferred_element_type=jnp.float32)
            o_ref[:, x] = res.reshape(res.shape[0] // sv, sv, ss)
        else:
            o_ref[x] = act.astype(jnp.float32).reshape(cout, sv, ss)
        return carry

    lax.fori_loop(0, sx, row, 0)


def fine_conv(field, weight, sides, head=None):
    _, cin, sv, ss = field.shape
    cout = weight.shape[0]
    rows = round_up(sv + 2, 16)
    lanes = round_up(ss + 2, 128)
    wide = round_up(cin * rows, 128) // rows
    padded = extended(field, sides)
    sx = padded.shape[0] - 2
    padded = jnp.pad(
        padded, ((0, 0), (0, wide - cin), (0, rows - sv - 2), (0, lanes - ss - 2))
    )
    padded = padded.reshape(sx + 2, wide * rows, lanes)
    taps = jnp.pad(weight, ((0, 0), (0, wide - cin), (0, 0), (0, 0), (0, 0)))
    operands = [padded, taps.transpose(2, 3, 4, 0, 1).reshape(27, cout, wide)]
    if head is None:
        out_shape = jax.ShapeDtypeStruct((sx, cout, sv, ss), jnp.float32)
    else:
        eye = jnp.eye(sv, dtype=jnp.float32)
        kron = jnp.einsum("po,vw->pvow", head.astype(jnp.float32), eye)
        operands.append(kron.reshape(head.shape[0] * sv, cout * sv).astype(jnp.bfloat16))
        out_shape = jax.ShapeDtypeStruct((head.shape[0], sx, sv, ss), jnp.float32)
    kernel = lambda *refs: fine_kernel(
        *refs, sx=sx, sv=sv, ss=ss, rows=rows, head=head is not None
    )
    return pl.pallas_call(
        kernel,
        out_shape=out_shape,
        scratch_shapes=[
            pltpu.VMEM((cout * sv, 9 * wide * rows), jnp.bfloat16),
            pltpu.VMEM((sx + 2, 3, wide * rows, ss), jnp.bfloat16),
        ],
    )(*operands)


def conv_valid(padded, weight):
    return lax.conv_general_dilated(
        padded[None],
        weight,
        (1, 1, 1),
        "VALID",
        dimension_numbers=NUMS,
        preferred_element_type=jnp.float32,
    )[0]


def mid_kernel(p_ref, w_ref, o_ref, shifted_ref, *, sx, sv, ss, span):
    lanes = p_ref.shape[-1]
    pitch = ss + 2

    def shift(x, carry):
        slab = p_ref[x].astype(jnp.float32)
        for b in range(3):
            for c in range(3):
                step = b * pitch + c
                piece = slab if step == 0 else pltpu.roll(slab, lanes - step, 1)
                shifted_ref[x, b * 3 + c] = piece[:, :span].astype(jnp.bfloat16)
        return carry

    lax.fori_loop(0, sx + 2, shift, 0)
    chans = shifted_ref.shape[2]

    def row(x, carry):
        stack = shifted_ref[pl.ds(x, 3)].reshape(27 * chans, span)
        acc = jnp.dot(w_ref[...], stack, preferred_element_type=jnp.float32)
        act = (acc * jax.nn.sigmoid(acc)).astype(jnp.bfloat16).astype(jnp.float32)
        for v in range(sv):
            piece = act if v == 0 else pltpu.roll(act, span - v * pitch, 1)
            o_ref[x, v] = piece[:, :ss]
        return carry

    lax.fori_loop(0, sx, row, 0)


def mid_conv(field, weight, sides=MID_SIDES):
    chans = field.shape[0]
    padded = extended(field, sides)
    _, sx, sv, ss = padded.shape
    sx, sv, ss = sx - 2, sv - 2, ss - 2
    flat = (sv + 2) * (ss + 2)
    lanes = round_up(flat, 128)
    span = round_up((sv - 1) * (ss + 2) + ss, 128)
    padded = padded.transpose(1, 0, 2, 3).reshape(sx + 2, chans, flat)
    padded = jnp.pad(padded, ((0, 0), (0, 0), (0, lanes - flat)))
    cout = weight.shape[1] // chans
    taps = weight.reshape(27, cout, chans).transpose(1, 0, 2).reshape(cout, 27 * chans)
    kernel = lambda *refs: mid_kernel(*refs, sx=sx, sv=sv, ss=ss, span=span)
    out = pl.pallas_call(
        kernel,
        out_shape=jax.ShapeDtypeStruct((sx, sv, cout, ss), jnp.float32),
        scratch_shapes=[pltpu.VMEM((sx + 2, 9, chans, span), jnp.bfloat16)],
    )(padded, taps)
    return out.transpose(2, 0, 1, 3).astype(jnp.bfloat16)


def conv_down(field, weight):
    return lax.conv_general_dilated(
        field[None],
        weight,
        (2, 2, 2),
        "VALID",
        dimension_numbers=NUMS,
        preferred_element_type=jnp.float32,
    )[0]


def fine_down(field, weight):
    sx, c, sv, ss = field.shape
    blocks = field.reshape(sx // 2, 2, c, sv // 2, 2, ss // 2, 2)
    return jnp.einsum("xaivbsc,oiabc->oxvs", blocks, weight, preferred_element_type=jnp.float32)


def fine_up(field, weight):
    outer = jnp.einsum("ixvs,ioabc->xaovbsc", field, weight, preferred_element_type=jnp.float32)
    chans, sx, sv, ss = (weight.shape[1], field.shape[1], field.shape[2], field.shape[3])
    return outer.reshape(2 * sx, chans, 2 * sv, 2 * ss)


def conv_up(field, weight):
    outer = jnp.einsum("ixvs,ioabc->oxavbsc", field, weight, preferred_element_type=jnp.float32)
    chans, sx, sv, ss = (weight.shape[1], field.shape[1], field.shape[2], field.shape[3])
    return outer.reshape(chans, 2 * sx, 2 * sv, 2 * ss)


def activate(value):
    return jax.nn.silu(value).astype(jnp.bfloat16)


def project(weight, field):
    return jnp.einsum("oc,cxp->oxp", weight, field, preferred_element_type=jnp.float32)


def normalize(block):
    values_f = block.astype(jnp.float32)
    mean_sq = jnp.mean(values_f * values_f, axis=0)
    return (values_f * lax.rsqrt(mean_sq + 1e-05)).astype(jnp.bfloat16)


def split_heads(weight, normed):
    chans, sx, count = normed.shape
    return project(weight, normed).astype(jnp.bfloat16).reshape(HEADS, chans // HEADS, sx, count)


def combine(queries, keys, values):
    scale = 1.0 / jnp.sqrt(jnp.float32(queries.shape[1]))
    scores = (
        jnp.einsum("hdxp,hdyp->hxyp", queries, keys, preferred_element_type=jnp.float32) * scale
    )
    weights = jax.nn.softmax(scores, axis=2).astype(jnp.bfloat16)
    attended = jnp.einsum("hxyp,hdyp->hdxp", weights, values, preferred_element_type=jnp.float32)
    heads, depth, sx, count = attended.shape
    return attended.astype(jnp.bfloat16).reshape(heads * depth, sx, count)


def finish(block, attended, w_attn_out):
    return (block.astype(jnp.float32) + project(w_attn_out, attended)).astype(jnp.bfloat16)


def on_device(
    inputs,
    w_in,
    w_fine_enc,
    w_down_mid,
    w_mid_enc,
    w_down_bottom,
    w_query,
    w_key,
    w_value,
    w_attn_out,
    w_up_mid,
    w_mid_dec,
    w_up_fine,
    w_fine_dec,
    w_head,
):
    fields = extended(inputs.transpose(1, 0, 2, 3), (("gx", 0, 4),))
    first = inside_rows(fine_conv(fields, w_in, FINE_CROSS).astype(jnp.bfloat16), -3)
    fine_wide = inside_rows(fine_conv(first, w_fine_enc, FINE_CROSS).astype(jnp.bfloat16), -2)
    fine_skip = fine_wide[2:-2]
    mid_in = activate(fine_down(fine_wide, w_down_mid))
    mid_skip = mid_conv(mid_in, w_mid_enc, MID_CROSS)
    bottom = activate(conv_down(mid_skip, unfold(w_down_bottom, 2, C2, C1)))
    chans, sx, sv, ss = bottom.shape
    flat = bottom.reshape(chans, sx, sv * ss)
    rows = lax.all_to_all(flat, "gx", split_axis=2, concat_axis=1, tiled=True)
    normed = normalize(rows)
    queries = split_heads(w_query, normed)
    keys = split_heads(w_key, normed)
    values = split_heads(w_value, normed)
    result = finish(rows, combine(queries, keys, values), w_attn_out)
    mixed = lax.all_to_all(result, "gx", split_axis=1, concat_axis=2, tiled=True)
    bottom_out = mixed.reshape(chans, sx, sv, ss)
    mid_up = (
        conv_up(bottom_out, unfold(w_up_mid, 2, C2, C1)) + mid_skip.astype(jnp.float32)
    ).astype(jnp.bfloat16)
    mid_dec = mid_conv(mid_up, w_mid_dec)
    fine_up_field = (fine_up(mid_dec, w_up_fine) + fine_skip.astype(jnp.float32)).astype(
        jnp.bfloat16
    )
    return fine_conv(fine_up_field, w_fine_dec, FINE_SIDES, head=w_head)


def solution(mesh):
    placed = (P(None, "gx", "gz", "gy"),) + (P(),) * 14
    return jax.shard_map(
        on_device, mesh=mesh, in_specs=placed, out_specs=P(None, "gx", "gz", "gy"), check_vma=False
    )
```

```python
import jax
import jax.numpy as jnp
from jax import lax
from jax.experimental import pallas as pl
from jax.experimental.pallas import tpu as pltpu
from jax.sharding import PartitionSpec as P

C1 = 64
C2 = 256
HEADS = 4


NUMS = ("NCDHW", "OIDHW", "NCDHW")
FINE_SIDES = (("gx", 0, 1), ("gy", 3, 1), ("gz", 2, 1))
FINE_CROSS = (("gy", 3, 1), ("gz", 2, 1))
MID_SIDES = (("gx", 1, 1), ("gy", 3, 1), ("gz", 2, 1))
MID_CROSS = (("gy", 3, 1), ("gz", 2, 1))


def extended(block, sides):
    for axis, dim, width in sides:
        count = lax.axis_size(axis)
        top = lax.slice_in_dim(block, block.shape[dim] - width, None, axis=dim)
        bottom = lax.slice_in_dim(block, 0, width, axis=dim)
        if count == 2:
            first = lax.axis_index(axis) == 0
            got = lax.ppermute(jnp.where(first, top, bottom), axis, [(0, 1), (1, 0)])
            low = jnp.where(first, jnp.zeros_like(got), got)
            high = jnp.where(first, got, jnp.zeros_like(got))
        else:
            forward = [(i, i + 1) for i in range(count - 1)]
            backward = [(target, source) for source, target in forward]
            low = lax.ppermute(top, axis, forward)
            high = lax.ppermute(bottom, axis, backward)
        block = jnp.concatenate([low, block, high], axis=dim)
    return block


def inside_rows(field, offset, dim=0):
    rows = field.shape[dim]
    own = rows + 2 * offset
    index = lax.axis_index("gx") * own + offset + jnp.arange(rows)
    keep = (index >= 0) & (index < own * lax.axis_size("gx"))
    shape = [1] * field.ndim
    shape[dim] = rows
    return jnp.where(keep.reshape(shape), field, jnp.zeros_like(field))


def unfold(weight, side, first, second):
    return weight.reshape(side, side, side, first, second).transpose(3, 4, 0, 1, 2)


def round_up(value, step):
    return (value + step - 1) // step * step


def fine_kernel(p_ref, w_ref, *rest, sx, sv, ss, rows, head):
    if head:
        h_ref, o_ref, band_ref, shifted_ref = rest
    else:
        o_ref, band_ref, shifted_ref = rest
    cout, cin = w_ref.shape[1:]
    depth = cin * rows
    lanes = p_ref.shape[-1]
    sv_bits, row_bits = sv.bit_length() - 1, rows.bit_length() - 1
    r = lax.broadcasted_iota(jnp.int32, (cout * sv, cout), 0)
    q = lax.broadcasted_iota(jnp.int32, (cout * sv, cout), 1)
    widen_rows = ((r >> sv_bits) == q).astype(jnp.bfloat16)
    r = lax.broadcasted_iota(jnp.int32, (cin, depth), 0)
    q = lax.broadcasted_iota(jnp.int32, (cin, depth), 1)
    widen_cols = ((q >> row_bits) == r).astype(jnp.bfloat16)
    r = lax.broadcasted_iota(jnp.int32, (cout * sv, depth), 0)
    q = lax.broadcasted_iota(jnp.int32, (cout * sv, depth), 1)
    offset = (q & (rows - 1)) - (r & (sv - 1))
    for a in range(3):
        for c in range(3):
            band = jnp.zeros((cout * sv, depth), jnp.float32)
            for b in range(3):
                tap = w_ref[(a * 3 + b) * 3 + c]
                grown = jnp.dot(widen_rows, tap, preferred_element_type=jnp.float32)
                grown = jnp.dot(
                    grown.astype(jnp.bfloat16), widen_cols, preferred_element_type=jnp.float32
                )
                band = band + jnp.where(offset == b, grown, 0.0)
            band_ref[:, pl.ds((a * 3 + c) * depth, depth)] = band.astype(jnp.bfloat16)

    def shift(x, carry):
        slab = p_ref[x].astype(jnp.float32)
        for c in range(3):
            piece = slab if c == 0 else pltpu.roll(slab, lanes - c, 1)
            shifted_ref[x, c] = piece[:, :ss].astype(jnp.bfloat16)
        return carry

    lax.fori_loop(0, sx + 2, shift, 0)

    def row(x, carry):
        stack = shifted_ref[pl.ds(x, 3)].reshape(9 * depth, ss)
        acc = jnp.dot(band_ref[...], stack, preferred_element_type=jnp.float32)
        act = (acc * jax.nn.sigmoid(acc)).astype(jnp.bfloat16)
        if head:
            res = jnp.dot(h_ref[...], act, preferred_element_type=jnp.float32)
            o_ref[:, x] = res.reshape(res.shape[0] // sv, sv, ss)
        else:
            o_ref[x] = act.astype(jnp.float32).reshape(cout, sv, ss)
        return carry

    lax.fori_loop(0, sx, row, 0)


def fine_conv(field, weight, sides, head=None):
    _, cin, sv, ss = field.shape
    cout = weight.shape[0]
    rows = round_up(sv + 2, 16)
    lanes = round_up(ss + 2, 128)
    wide = round_up(cin * rows, 128) // rows
    padded = extended(field, sides)
    sx = padded.shape[0] - 2
    padded = jnp.pad(
        padded, ((0, 0), (0, wide - cin), (0, rows - sv - 2), (0, lanes - ss - 2))
    )
    padded = padded.reshape(sx + 2, wide * rows, lanes)
    taps = jnp.pad(weight, ((0, 0), (0, wide - cin), (0, 0), (0, 0), (0, 0)))
    operands = [padded, taps.transpose(2, 3, 4, 0, 1).reshape(27, cout, wide)]
    if head is None:
        out_shape = jax.ShapeDtypeStruct((sx, cout, sv, ss), jnp.float32)
    else:
        eye = jnp.eye(sv, dtype=jnp.float32)
        kron = jnp.einsum("po,vw->pvow", head.astype(jnp.float32), eye)
        operands.append(kron.reshape(head.shape[0] * sv, cout * sv).astype(jnp.bfloat16))
        out_shape = jax.ShapeDtypeStruct((head.shape[0], sx, sv, ss), jnp.float32)
    kernel = lambda *refs: fine_kernel(
        *refs, sx=sx, sv=sv, ss=ss, rows=rows, head=head is not None
    )
    return pl.pallas_call(
        kernel,
        out_shape=out_shape,
        scratch_shapes=[
            pltpu.VMEM((cout * sv, 9 * wide * rows), jnp.bfloat16),
            pltpu.VMEM((sx + 2, 3, wide * rows, ss), jnp.bfloat16),
        ],
    )(*operands)


def conv_valid(padded, weight):
    return lax.conv_general_dilated(
        padded[None],
        weight,
        (1, 1, 1),
        "VALID",
        dimension_numbers=NUMS,
        preferred_element_type=jnp.float32,
    )[0]


def mid_kernel(p_ref, w_ref, o_ref, shifted_ref, *, sx, sv, ss, span):
    lanes = p_ref.shape[-1]
    pitch = ss + 2

    def shift(x, carry):
        slab = p_ref[x].astype(jnp.float32)
        for b in range(3):
            for c in range(3):
                step = b * pitch + c
                piece = slab if step == 0 else pltpu.roll(slab, lanes - step, 1)
                shifted_ref[x, b * 3 + c] = piece[:, :span].astype(jnp.bfloat16)
        return carry

    lax.fori_loop(0, sx + 2, shift, 0)
    chans = shifted_ref.shape[2]

    def row(x, carry):
        stack = shifted_ref[pl.ds(x, 3)].reshape(27 * chans, span)
        acc = jnp.dot(w_ref[...], stack, preferred_element_type=jnp.float32)
        act = (acc * jax.nn.sigmoid(acc)).astype(jnp.bfloat16).astype(jnp.float32)
        for v in range(sv):
            piece = act if v == 0 else pltpu.roll(act, span - v * pitch, 1)
            o_ref[x, v] = piece[:, :ss]
        return carry

    lax.fori_loop(0, sx, row, 0)


def mid_conv(field, weight, sides=MID_SIDES):
    chans = field.shape[0]
    padded = extended(field, sides)
    _, sx, sv, ss = padded.shape
    sx, sv, ss = sx - 2, sv - 2, ss - 2
    flat = (sv + 2) * (ss + 2)
    lanes = round_up(flat, 128)
    span = round_up((sv - 1) * (ss + 2) + ss, 128)
    padded = padded.transpose(1, 0, 2, 3).reshape(sx + 2, chans, flat)
    padded = jnp.pad(padded, ((0, 0), (0, 0), (0, lanes - flat)))
    cout = weight.shape[1] // chans
    taps = weight.reshape(27, cout, chans).transpose(1, 0, 2).reshape(cout, 27 * chans)
    kernel = lambda *refs: mid_kernel(*refs, sx=sx, sv=sv, ss=ss, span=span)
    out = pl.pallas_call(
        kernel,
        out_shape=jax.ShapeDtypeStruct((sx, sv, cout, ss), jnp.float32),
        scratch_shapes=[pltpu.VMEM((sx + 2, 9, chans, span), jnp.bfloat16)],
    )(padded, taps)
    return out.transpose(2, 0, 1, 3).astype(jnp.bfloat16)


def conv_down(field, weight):
    return lax.conv_general_dilated(
        field[None],
        weight,
        (2, 2, 2),
        "VALID",
        dimension_numbers=NUMS,
        preferred_element_type=jnp.float32,
    )[0]


def fine_down(field, weight):
    sx, c, sv, ss = field.shape
    blocks = field.reshape(sx // 2, 2, c, sv // 2, 2, ss // 2, 2)
    return jnp.einsum("xaivbsc,oiabc->oxvs", blocks, weight, preferred_element_type=jnp.float32)


def fine_up(field, weight):
    outer = jnp.einsum("ixvs,ioabc->xaovbsc", field, weight, preferred_element_type=jnp.float32)
    chans, sx, sv, ss = (weight.shape[1], field.shape[1], field.shape[2], field.shape[3])
    return outer.reshape(2 * sx, chans, 2 * sv, 2 * ss)


def conv_up(field, weight):
    outer = jnp.einsum("ixvs,ioabc->oxavbsc", field, weight, preferred_element_type=jnp.float32)
    chans, sx, sv, ss = (weight.shape[1], field.shape[1], field.shape[2], field.shape[3])
    return outer.reshape(chans, 2 * sx, 2 * sv, 2 * ss)


def activate(value):
    return jax.nn.silu(value).astype(jnp.bfloat16)


def project(weight, field):
    return jnp.einsum("oc,cxp->oxp", weight, field, preferred_element_type=jnp.float32)


def normalize(block):
    values_f = block.astype(jnp.float32)
    mean_sq = jnp.mean(values_f * values_f, axis=0)
    return (values_f * lax.rsqrt(mean_sq + 1e-05)).astype(jnp.bfloat16)


def split_heads(weight, normed):
    chans, sx, count = normed.shape
    return project(weight, normed).astype(jnp.bfloat16).reshape(HEADS, chans // HEADS, sx, count)


def combine(queries, keys, values):
    scale = 1.0 / jnp.sqrt(jnp.float32(queries.shape[1]))
    scores = (
        jnp.einsum("hdxp,hdyp->hxyp", queries, keys, preferred_element_type=jnp.float32) * scale
    )
    weights = jax.nn.softmax(scores, axis=2).astype(jnp.bfloat16)
    attended = jnp.einsum("hxyp,hdyp->hdxp", weights, values, preferred_element_type=jnp.float32)
    heads, depth, sx, count = attended.shape
    return attended.astype(jnp.bfloat16).reshape(heads * depth, sx, count)


def finish(block, attended, w_attn_out):
    return (block.astype(jnp.float32) + project(w_attn_out, attended)).astype(jnp.bfloat16)


def on_device(
    inputs,
    w_in,
    w_fine_enc,
    w_down_mid,
    w_mid_enc,
    w_down_bottom,
    w_query,
    w_key,
    w_value,
    w_attn_out,
    w_up_mid,
    w_mid_dec,
    w_up_fine,
    w_fine_dec,
    w_head,
):
    fields = extended(inputs.transpose(1, 0, 2, 3), (("gx", 0, inputs.shape[1]),))
    first = inside_rows(fine_conv(fields, w_in, FINE_CROSS).astype(jnp.bfloat16), -7)
    fine_wide = inside_rows(fine_conv(first, w_fine_enc, FINE_CROSS).astype(jnp.bfloat16), -6)
    mid_in = activate(fine_down(fine_wide, w_down_mid))
    mid_wide = inside_rows(mid_conv(mid_in, w_mid_enc, MID_CROSS), -2, 1)
    mid_skip = mid_wide[:, 2:-2]
    bottom = activate(conv_down(mid_skip, unfold(w_down_bottom, 2, C2, C1)))
    chans, sx, sv, ss = bottom.shape
    flat = bottom.reshape(chans, sx, sv * ss)
    rows = lax.all_to_all(flat, "gx", split_axis=2, concat_axis=1, tiled=True)
    normed = normalize(rows)
    queries = split_heads(w_query, normed)
    keys = split_heads(w_key, normed)
    values = split_heads(w_value, normed)
    result = finish(rows, combine(queries, keys, values), w_attn_out)
    count = result.shape[2]
    groups = result.shape[1] // sx
    rim = jnp.pad(result, ((0, 0), (1, 1), (0, 0)))
    low = rim[:, : groups * sx].reshape(chans, groups, sx, count)
    high = rim[:, 2 : groups * sx + 2].reshape(chans, groups, sx, count)
    windows = jnp.concatenate([low, high], axis=2).reshape(chans, groups * 2 * sx, count)
    mixed = lax.all_to_all(windows, "gx", split_axis=1, concat_axis=2, tiled=True)
    bottom_out = mixed.reshape(chans, 2 * sx, sv, ss)
    mid_up = (
        conv_up(bottom_out, unfold(w_up_mid, 2, C2, C1)) + mid_wide.astype(jnp.float32)
    ).astype(jnp.bfloat16)
    mid_dec = inside_rows(mid_conv(mid_up, w_mid_dec, MID_CROSS), -1, 1)
    fine_up_field = (fine_up(mid_dec, w_up_fine) + fine_wide[4:-4].astype(jnp.float32)).astype(
        jnp.bfloat16
    )
    return fine_conv(fine_up_field[1:-1], w_fine_dec, FINE_CROSS, head=w_head)


def solution(mesh):
    placed = (P(None, "gx", "gz", "gy"),) + (P(),) * 14
    return jax.shard_map(
        on_device, mesh=mesh, in_specs=placed, out_specs=P(None, "gx", "gz", "gy"), check_vma=False
    )
```

```python
import jax
import jax.numpy as jnp
from jax import lax
from jax.experimental import pallas as pl
from jax.experimental.pallas import tpu as pltpu
from jax.sharding import PartitionSpec as P

C1 = 64
C2 = 256
HEADS = 4


NUMS = ("NCDHW", "OIDHW", "NCDHW")
FINE_SIDES = (("gx", 0, 1), ("gy", 3, 1), ("gz", 2, 1))
FINE_CROSS = (("gy", 3, 1), ("gz", 2, 1))
MID_SIDES = (("gx", 1, 1), ("gy", 3, 1), ("gz", 2, 1))
MID_CROSS = (("gy", 3, 1), ("gz", 2, 1))


def extended(block, sides):
    for axis, dim, width in sides:
        count = lax.axis_size(axis)
        top = lax.slice_in_dim(block, block.shape[dim] - width, None, axis=dim)
        bottom = lax.slice_in_dim(block, 0, width, axis=dim)
        if count == 2:
            first = lax.axis_index(axis) == 0
            got = lax.ppermute(jnp.where(first, top, bottom), axis, [(0, 1), (1, 0)])
            low = jnp.where(first, jnp.zeros_like(got), got)
            high = jnp.where(first, got, jnp.zeros_like(got))
        else:
            forward = [(i, i + 1) for i in range(count - 1)]
            backward = [(target, source) for source, target in forward]
            low = lax.ppermute(top, axis, forward)
            high = lax.ppermute(bottom, axis, backward)
        block = jnp.concatenate([low, block, high], axis=dim)
    return block


def inside_rows(field, offset, dim=0):
    rows = field.shape[dim]
    own = rows + 2 * offset
    index = lax.axis_index("gx") * own + offset + jnp.arange(rows)
    keep = (index >= 0) & (index < own * lax.axis_size("gx"))
    shape = [1] * field.ndim
    shape[dim] = rows
    return jnp.where(keep.reshape(shape), field, jnp.zeros_like(field))


def unfold(weight, side, first, second):
    return weight.reshape(side, side, side, first, second).transpose(3, 4, 0, 1, 2)


def round_up(value, step):
    return (value + step - 1) // step * step


def fine_kernel(p_ref, e_ref, w_ref, *rest, sx, sv, ss, rows, head):
    if head:
        h_ref, o_ref, band_ref, shifted_ref = rest
    else:
        o_ref, band_ref, shifted_ref = rest
    cout, cin = w_ref.shape[1:]
    depth = cin * rows
    sv_bits, row_bits = sv.bit_length() - 1, rows.bit_length() - 1
    r = lax.broadcasted_iota(jnp.int32, (cout * sv, cout), 0)
    q = lax.broadcasted_iota(jnp.int32, (cout * sv, cout), 1)
    widen_rows = ((r >> sv_bits) == q).astype(jnp.bfloat16)
    r = lax.broadcasted_iota(jnp.int32, (cin, depth), 0)
    q = lax.broadcasted_iota(jnp.int32, (cin, depth), 1)
    widen_cols = ((q >> row_bits) == r).astype(jnp.bfloat16)
    r = lax.broadcasted_iota(jnp.int32, (cout * sv, depth), 0)
    q = lax.broadcasted_iota(jnp.int32, (cout * sv, depth), 1)
    w = q & (rows - 1)
    place = jnp.where(w < sv, w + 1, jnp.where(w == sv, 0, jnp.where(w == sv + 1, sv + 1, -8)))
    offset = place - (r & (sv - 1))
    for a in range(3):
        for c in range(3):
            band = jnp.zeros((cout * sv, depth), jnp.float32)
            for b in range(3):
                tap = w_ref[(a * 3 + b) * 3 + c]
                grown = jnp.dot(widen_rows, tap, preferred_element_type=jnp.float32)
                grown = jnp.dot(
                    grown.astype(jnp.bfloat16), widen_cols, preferred_element_type=jnp.float32
                )
                band = band + jnp.where(offset == b, grown, 0.0)
            band_ref[:, pl.ds((a * 3 + c) * depth, depth)] = band.astype(jnp.bfloat16)

    lane = lax.broadcasted_iota(jnp.int32, (depth, ss), 1)

    def shift(x, carry):
        slab = p_ref[x].astype(jnp.float32)
        edges = jnp.transpose(e_ref[x].astype(jnp.float32))
        low = jnp.where(lane == 0, edges[:, 0:1], pltpu.roll(slab, 1, 1))
        high = jnp.where(lane == ss - 1, edges[:, 1:2], pltpu.roll(slab, ss - 1, 1))
        shifted_ref[x, 0] = low.astype(jnp.bfloat16)
        shifted_ref[x, 1] = slab.astype(jnp.bfloat16)
        shifted_ref[x, 2] = high.astype(jnp.bfloat16)
        return carry

    lax.fori_loop(0, sx + 2, shift, 0)

    def row(x, carry):
        stack = shifted_ref[pl.ds(x, 3)].reshape(9 * depth, ss)
        acc = jnp.dot(band_ref[...], stack, preferred_element_type=jnp.float32)
        act = (acc * jax.nn.sigmoid(acc)).astype(jnp.bfloat16)
        if head:
            res = jnp.dot(h_ref[...], act, preferred_element_type=jnp.float32)
            o_ref[:, x] = res.reshape(res.shape[0] // sv, sv, ss)
        else:
            o_ref[x] = act.astype(jnp.float32).reshape(cout, sv, ss)
        return carry

    lax.fori_loop(0, sx, row, 0)


def faces(block, axis, dim):
    count = lax.axis_size(axis)
    top = lax.slice_in_dim(block, block.shape[dim] - 1, None, axis=dim)
    bottom = lax.slice_in_dim(block, 0, 1, axis=dim)
    if count == 2:
        first = lax.axis_index(axis) == 0
        got = lax.ppermute(jnp.where(first, top, bottom), axis, [(0, 1), (1, 0)])
        return jnp.where(first, jnp.zeros_like(got), got), jnp.where(first, got, jnp.zeros_like(got))
    forward = [(i, i + 1) for i in range(count - 1)]
    backward = [(target, source) for source, target in forward]
    return lax.ppermute(top, axis, forward), lax.ppermute(bottom, axis, backward)


def fine_conv(field, weight, head=None):
    rows_x, cin, sv, ss = field.shape
    sx = rows_x - 2
    cout = weight.shape[0]
    rows = round_up(sv + 2, 16)
    wide = round_up(cin * rows, 128) // rows
    block = jnp.pad(field, ((0, 0), (0, wide - cin), (0, 0), (0, 0)))
    below, above = faces(block, "gz", 2)
    spare = jnp.zeros((rows_x, wide, rows - sv - 2, ss), block.dtype)
    padded = jnp.concatenate([block, below, above, spare], axis=2)
    left, right = faces(padded, "gy", 3)
    edges = jnp.concatenate([left, right], axis=3).transpose(0, 3, 1, 2)
    edges = jnp.pad(edges.reshape(rows_x, 2, wide * rows), ((0, 0), (0, 6), (0, 0)))
    padded = padded.reshape(rows_x, wide * rows, ss)
    taps = jnp.pad(weight, ((0, 0), (0, wide - cin), (0, 0), (0, 0), (0, 0)))
    operands = [padded, edges, taps.transpose(2, 3, 4, 0, 1).reshape(27, cout, wide)]
    if head is None:
        out_shape = jax.ShapeDtypeStruct((sx, cout, sv, ss), jnp.float32)
    else:
        eye = jnp.eye(sv, dtype=jnp.float32)
        kron = jnp.einsum("po,vw->pvow", head.astype(jnp.float32), eye)
        operands.append(kron.reshape(head.shape[0] * sv, cout * sv).astype(jnp.bfloat16))
        out_shape = jax.ShapeDtypeStruct((head.shape[0], sx, sv, ss), jnp.float32)
    kernel = lambda *refs: fine_kernel(
        *refs, sx=sx, sv=sv, ss=ss, rows=rows, head=head is not None
    )
    return pl.pallas_call(
        kernel,
        out_shape=out_shape,
        scratch_shapes=[
            pltpu.VMEM((cout * sv, 9 * wide * rows), jnp.bfloat16),
            pltpu.VMEM((sx + 2, 3, wide * rows, ss), jnp.bfloat16),
        ],
    )(*operands)


def mid_kernel(p_ref, w_ref, o_ref, shifted_ref, *, sx, sv, ss, span):
    lanes = p_ref.shape[-1]
    pitch = ss + 2

    def shift(x, carry):
        slab = p_ref[x].astype(jnp.float32)
        for b in range(3):
            for c in range(3):
                step = b * pitch + c
                piece = slab if step == 0 else pltpu.roll(slab, lanes - step, 1)
                shifted_ref[x, b * 3 + c] = piece[:, :span].astype(jnp.bfloat16)
        return carry

    lax.fori_loop(0, sx + 2, shift, 0)
    chans = shifted_ref.shape[2]

    def row(x, carry):
        stack = shifted_ref[pl.ds(x, 3)].reshape(27 * chans, span)
        acc = jnp.dot(w_ref[...], stack, preferred_element_type=jnp.float32)
        act = (acc * jax.nn.sigmoid(acc)).astype(jnp.bfloat16).astype(jnp.float32)
        for v in range(sv):
            piece = act if v == 0 else pltpu.roll(act, span - v * pitch, 1)
            o_ref[x, v] = piece[:, :ss]
        return carry

    lax.fori_loop(0, sx, row, 0)


def mid_conv(field, weight, sides=MID_SIDES):
    chans = field.shape[0]
    padded = extended(field, sides)
    _, sx, sv, ss = padded.shape
    sx, sv, ss = sx - 2, sv - 2, ss - 2
    flat = (sv + 2) * (ss + 2)
    lanes = round_up(flat, 128)
    span = round_up((sv - 1) * (ss + 2) + ss, 128)
    padded = padded.transpose(1, 0, 2, 3).reshape(sx + 2, chans, flat)
    padded = jnp.pad(padded, ((0, 0), (0, 0), (0, lanes - flat)))
    cout = weight.shape[1] // chans
    taps = weight.reshape(27, cout, chans).transpose(1, 0, 2).reshape(cout, 27 * chans)
    kernel = lambda *refs: mid_kernel(*refs, sx=sx, sv=sv, ss=ss, span=span)
    out = pl.pallas_call(
        kernel,
        out_shape=jax.ShapeDtypeStruct((sx, sv, cout, ss), jnp.float32),
        scratch_shapes=[pltpu.VMEM((sx + 2, 9, chans, span), jnp.bfloat16)],
    )(padded, taps)
    return out.transpose(2, 0, 1, 3).astype(jnp.bfloat16)


def conv_down(field, weight):
    return lax.conv_general_dilated(
        field[None],
        weight,
        (2, 2, 2),
        "VALID",
        dimension_numbers=NUMS,
        preferred_element_type=jnp.float32,
    )[0]


def fine_down(field, weight):
    sx, c, sv, ss = field.shape
    blocks = field.reshape(sx // 2, 2, c, sv // 2, 2, ss // 2, 2)
    return jnp.einsum("xaivbsc,oiabc->oxvs", blocks, weight, preferred_element_type=jnp.float32)


def fine_up(field, weight):
    outer = jnp.einsum("ixvs,ioabc->xaovbsc", field, weight, preferred_element_type=jnp.float32)
    chans, sx, sv, ss = (weight.shape[1], field.shape[1], field.shape[2], field.shape[3])
    return outer.reshape(2 * sx, chans, 2 * sv, 2 * ss)


def conv_up(field, weight):
    outer = jnp.einsum("ixvs,ioabc->oxavbsc", field, weight, preferred_element_type=jnp.float32)
    chans, sx, sv, ss = (weight.shape[1], field.shape[1], field.shape[2], field.shape[3])
    return outer.reshape(chans, 2 * sx, 2 * sv, 2 * ss)


def activate(value):
    return jax.nn.silu(value).astype(jnp.bfloat16)


def project(weight, field):
    return jnp.einsum("oc,cxp->oxp", weight, field, preferred_element_type=jnp.float32)


def normalize(block):
    values_f = block.astype(jnp.float32)
    mean_sq = jnp.mean(values_f * values_f, axis=0)
    return (values_f * lax.rsqrt(mean_sq + 1e-05)).astype(jnp.bfloat16)


def split_heads(weight, normed):
    chans, sx, count = normed.shape
    return project(weight, normed).astype(jnp.bfloat16).reshape(HEADS, chans // HEADS, sx, count)


def combine(queries, keys, values):
    scale = 1.0 / jnp.sqrt(jnp.float32(queries.shape[1]))
    scores = (
        jnp.einsum("hdxp,hdyp->hxyp", queries, keys, preferred_element_type=jnp.float32) * scale
    )
    weights = jax.nn.softmax(scores, axis=2).astype(jnp.bfloat16)
    attended = jnp.einsum("hxyp,hdyp->hdxp", weights, values, preferred_element_type=jnp.float32)
    heads, depth, sx, count = attended.shape
    return attended.astype(jnp.bfloat16).reshape(heads * depth, sx, count)


def finish(block, attended, w_attn_out):
    return (block.astype(jnp.float32) + project(w_attn_out, attended)).astype(jnp.bfloat16)


def on_device(
    inputs,
    w_in,
    w_fine_enc,
    w_down_mid,
    w_mid_enc,
    w_down_bottom,
    w_query,
    w_key,
    w_value,
    w_attn_out,
    w_up_mid,
    w_mid_dec,
    w_up_fine,
    w_fine_dec,
    w_head,
):
    fields = extended(inputs.transpose(1, 0, 2, 3), (("gx", 0, inputs.shape[1]),))
    first = inside_rows(fine_conv(fields, w_in).astype(jnp.bfloat16), -7)
    fine_wide = inside_rows(fine_conv(first, w_fine_enc).astype(jnp.bfloat16), -6)
    mid_in = activate(fine_down(fine_wide, w_down_mid))
    mid_wide = inside_rows(mid_conv(mid_in, w_mid_enc, MID_CROSS), -2, 1)
    mid_skip = mid_wide[:, 2:-2]
    bottom = activate(conv_down(mid_skip, unfold(w_down_bottom, 2, C2, C1)))
    chans, sx, sv, ss = bottom.shape
    flat = bottom.reshape(chans, sx, sv * ss)
    rows = lax.all_to_all(flat, "gx", split_axis=2, concat_axis=1, tiled=True)
    normed = normalize(rows)
    queries = split_heads(w_query, normed)
    keys = split_heads(w_key, normed)
    values = split_heads(w_value, normed)
    result = finish(rows, combine(queries, keys, values), w_attn_out)
    count = result.shape[2]
    groups = result.shape[1] // sx
    rim = jnp.pad(result, ((0, 0), (1, 1), (0, 0)))
    low = rim[:, : groups * sx].reshape(chans, groups, sx, count)
    high = rim[:, 2 : groups * sx + 2].reshape(chans, groups, sx, count)
    windows = jnp.concatenate([low, high], axis=2).reshape(chans, groups * 2 * sx, count)
    mixed = lax.all_to_all(windows, "gx", split_axis=1, concat_axis=2, tiled=True)
    bottom_out = mixed.reshape(chans, 2 * sx, sv, ss)
    mid_up = (
        conv_up(bottom_out, unfold(w_up_mid, 2, C2, C1)) + mid_wide.astype(jnp.float32)
    ).astype(jnp.bfloat16)
    mid_dec = inside_rows(mid_conv(mid_up, w_mid_dec, MID_CROSS), -1, 1)
    fine_up_field = (fine_up(mid_dec, w_up_fine) + fine_wide[4:-4].astype(jnp.float32)).astype(
        jnp.bfloat16
    )
    return fine_conv(fine_up_field[1:-1], w_fine_dec, head=w_head)


def solution(mesh):
    placed = (P(None, "gx", "gz", "gy"),) + (P(),) * 14
    return jax.shard_map(
        on_device, mesh=mesh, in_specs=placed, out_specs=P(None, "gx", "gz", "gy"), check_vma=False
    )
```

```python
import jax
import jax.numpy as jnp
from jax import lax
from jax.experimental import pallas as pl
from jax.experimental.pallas import tpu as pltpu
from jax.sharding import PartitionSpec as P

C1 = 64
C2 = 256
HEADS = 4


NUMS = ("NCDHW", "OIDHW", "NCDHW")
FINE_SIDES = (("gx", 0, 1), ("gy", 3, 1), ("gz", 2, 1))
FINE_CROSS = (("gy", 3, 1), ("gz", 2, 1))
MID_SIDES = (("gx", 1, 1), ("gy", 3, 1), ("gz", 2, 1))
MID_CROSS = (("gy", 3, 1), ("gz", 2, 1))


def extended(block, sides):
    for axis, dim, width in sides:
        count = lax.axis_size(axis)
        top = lax.slice_in_dim(block, block.shape[dim] - width, None, axis=dim)
        bottom = lax.slice_in_dim(block, 0, width, axis=dim)
        if count == 2:
            first = lax.axis_index(axis) == 0
            got = lax.ppermute(jnp.where(first, top, bottom), axis, [(0, 1), (1, 0)])
            low = jnp.where(first, jnp.zeros_like(got), got)
            high = jnp.where(first, got, jnp.zeros_like(got))
        else:
            forward = [(i, i + 1) for i in range(count - 1)]
            backward = [(target, source) for source, target in forward]
            low = lax.ppermute(top, axis, forward)
            high = lax.ppermute(bottom, axis, backward)
        block = jnp.concatenate([low, block, high], axis=dim)
    return block


def inside_rows(field, offset, dim=0):
    rows = field.shape[dim]
    own = rows + 2 * offset
    index = lax.axis_index("gx") * own + offset + jnp.arange(rows)
    keep = (index >= 0) & (index < own * lax.axis_size("gx"))
    shape = [1] * field.ndim
    shape[dim] = rows
    return jnp.where(keep.reshape(shape), field, jnp.zeros_like(field))


def unfold(weight, side, first, second):
    return weight.reshape(side, side, side, first, second).transpose(3, 4, 0, 1, 2)


def round_up(value, step):
    return (value + step - 1) // step * step


def fine_kernel(p_ref, e_ref, w_ref, *rest, sx, sv, ss, rows, head):
    if head:
        h_ref, o_ref, band_ref, shifted_ref = rest
    else:
        o_ref, band_ref, shifted_ref = rest
    cout, cin = w_ref.shape[1:]
    depth = cin * rows
    sv_bits, row_bits = sv.bit_length() - 1, rows.bit_length() - 1
    r = lax.broadcasted_iota(jnp.int32, (cout * sv, cout), 0)
    q = lax.broadcasted_iota(jnp.int32, (cout * sv, cout), 1)
    widen_rows = ((r >> sv_bits) == q).astype(jnp.bfloat16)
    r = lax.broadcasted_iota(jnp.int32, (cin, depth), 0)
    q = lax.broadcasted_iota(jnp.int32, (cin, depth), 1)
    widen_cols = ((q >> row_bits) == r).astype(jnp.bfloat16)
    r = lax.broadcasted_iota(jnp.int32, (cout * sv, depth), 0)
    q = lax.broadcasted_iota(jnp.int32, (cout * sv, depth), 1)
    w = q & (rows - 1)
    place = jnp.where(w < sv, w + 1, jnp.where(w == sv, 0, jnp.where(w == sv + 1, sv + 1, -8)))
    offset = place - (r & (sv - 1))
    for a in range(3):
        for c in range(3):
            band = jnp.zeros((cout * sv, depth), jnp.float32)
            for b in range(3):
                tap = w_ref[(a * 3 + b) * 3 + c]
                grown = jnp.dot(widen_rows, tap, preferred_element_type=jnp.float32)
                grown = jnp.dot(
                    grown.astype(jnp.bfloat16), widen_cols, preferred_element_type=jnp.float32
                )
                band = band + jnp.where(offset == b, grown, 0.0)
            band_ref[:, pl.ds((a * 3 + c) * depth, depth)] = band.astype(jnp.bfloat16)

    lane = lax.broadcasted_iota(jnp.int32, (depth, ss), 1)

    def shift(x, carry):
        slab = p_ref[x].astype(jnp.float32)
        edges = jnp.transpose(e_ref[x].astype(jnp.float32))
        low = jnp.where(lane == 0, edges[:, 0:1], pltpu.roll(slab, 1, 1))
        high = jnp.where(lane == ss - 1, edges[:, 1:2], pltpu.roll(slab, ss - 1, 1))
        shifted_ref[x, 0] = low.astype(jnp.bfloat16)
        shifted_ref[x, 1] = slab.astype(jnp.bfloat16)
        shifted_ref[x, 2] = high.astype(jnp.bfloat16)
        return carry

    lax.fori_loop(0, sx + 2, shift, 0)

    def rows_pair(g, carry):
        x = 2 * g
        stack = jnp.concatenate(
            [
                shifted_ref[pl.ds(x, 3)].reshape(9 * depth, ss),
                shifted_ref[pl.ds(x + 1, 3)].reshape(9 * depth, ss),
            ],
            axis=1,
        )
        acc = jnp.dot(band_ref[...], stack, preferred_element_type=jnp.float32)
        act = (acc * jax.nn.sigmoid(acc)).astype(jnp.bfloat16)
        for k in range(2):
            part = act[:, k * ss : (k + 1) * ss]
            if head:
                res = jnp.dot(h_ref[...], part, preferred_element_type=jnp.float32)
                o_ref[:, x + k] = res.reshape(res.shape[0] // sv, sv, ss)
            else:
                o_ref[x + k] = part.astype(jnp.float32).reshape(cout, sv, ss)
        return carry

    lax.fori_loop(0, sx // 2, rows_pair, 0)


def faces(block, axis, dim):
    count = lax.axis_size(axis)
    top = lax.slice_in_dim(block, block.shape[dim] - 1, None, axis=dim)
    bottom = lax.slice_in_dim(block, 0, 1, axis=dim)
    if count == 2:
        first = lax.axis_index(axis) == 0
        got = lax.ppermute(jnp.where(first, top, bottom), axis, [(0, 1), (1, 0)])
        return jnp.where(first, jnp.zeros_like(got), got), jnp.where(first, got, jnp.zeros_like(got))
    forward = [(i, i + 1) for i in range(count - 1)]
    backward = [(target, source) for source, target in forward]
    return lax.ppermute(top, axis, forward), lax.ppermute(bottom, axis, backward)


def fine_conv(field, weight, head=None):
    rows_x, cin, sv, ss = field.shape
    sx = rows_x - 2
    cout = weight.shape[0]
    rows = round_up(sv + 2, 16)
    wide = round_up(cin * rows, 128) // rows
    block = jnp.pad(field, ((0, 0), (0, wide - cin), (0, 0), (0, 0)))
    below, above = faces(block, "gz", 2)
    spare = jnp.zeros((rows_x, wide, rows - sv - 2, ss), block.dtype)
    padded = jnp.concatenate([block, below, above, spare], axis=2)
    left, right = faces(padded, "gy", 3)
    edges = jnp.concatenate([left, right], axis=3).transpose(0, 3, 1, 2)
    edges = jnp.pad(edges.reshape(rows_x, 2, wide * rows), ((0, 0), (0, 6), (0, 0)))
    padded = padded.reshape(rows_x, wide * rows, ss)
    taps = jnp.pad(weight, ((0, 0), (0, wide - cin), (0, 0), (0, 0), (0, 0)))
    operands = [padded, edges, taps.transpose(2, 3, 4, 0, 1).reshape(27, cout, wide)]
    if head is None:
        out_shape = jax.ShapeDtypeStruct((sx, cout, sv, ss), jnp.float32)
    else:
        eye = jnp.eye(sv, dtype=jnp.float32)
        kron = jnp.einsum("po,vw->pvow", head.astype(jnp.float32), eye)
        operands.append(kron.reshape(head.shape[0] * sv, cout * sv).astype(jnp.bfloat16))
        out_shape = jax.ShapeDtypeStruct((head.shape[0], sx, sv, ss), jnp.float32)
    kernel = lambda *refs: fine_kernel(
        *refs, sx=sx, sv=sv, ss=ss, rows=rows, head=head is not None
    )
    return pl.pallas_call(
        kernel,
        out_shape=out_shape,
        scratch_shapes=[
            pltpu.VMEM((cout * sv, 9 * wide * rows), jnp.bfloat16),
            pltpu.VMEM((sx + 2, 3, wide * rows, ss), jnp.bfloat16),
        ],
    )(*operands)


def mid_kernel(p_ref, w_ref, o_ref, shifted_ref, *, sx, sv, ss, span):
    lanes = p_ref.shape[-1]
    pitch = ss + 2

    def shift(x, carry):
        slab = p_ref[x].astype(jnp.float32)
        for b in range(3):
            for c in range(3):
                step = b * pitch + c
                piece = slab if step == 0 else pltpu.roll(slab, lanes - step, 1)
                shifted_ref[x, b * 3 + c] = piece[:, :span].astype(jnp.bfloat16)
        return carry

    lax.fori_loop(0, sx + 2, shift, 0)
    chans = shifted_ref.shape[2]

    def rows_pair(g, carry):
        x = 2 * g
        stack = jnp.concatenate(
            [
                shifted_ref[pl.ds(x, 3)].reshape(27 * chans, span),
                shifted_ref[pl.ds(x + 1, 3)].reshape(27 * chans, span),
            ],
            axis=1,
        )
        acc = jnp.dot(w_ref[...], stack, preferred_element_type=jnp.float32)
        act = (acc * jax.nn.sigmoid(acc)).astype(jnp.bfloat16).astype(jnp.float32)
        for k in range(2):
            part = act[:, k * span : (k + 1) * span]
            for v in range(sv):
                piece = part if v == 0 else pltpu.roll(part, span - v * pitch, 1)
                o_ref[x + k, v] = piece[:, :ss]
        return carry

    lax.fori_loop(0, sx // 2, rows_pair, 0)


def mid_conv(field, weight, sides=MID_SIDES):
    chans = field.shape[0]
    padded = extended(field, sides)
    _, sx, sv, ss = padded.shape
    sx, sv, ss = sx - 2, sv - 2, ss - 2
    flat = (sv + 2) * (ss + 2)
    lanes = round_up(flat, 128)
    span = round_up((sv - 1) * (ss + 2) + ss, 128)
    padded = padded.transpose(1, 0, 2, 3).reshape(sx + 2, chans, flat)
    padded = jnp.pad(padded, ((0, 0), (0, 0), (0, lanes - flat)))
    cout = weight.shape[1] // chans
    taps = weight.reshape(27, cout, chans).transpose(1, 0, 2).reshape(cout, 27 * chans)
    kernel = lambda *refs: mid_kernel(*refs, sx=sx, sv=sv, ss=ss, span=span)
    out = pl.pallas_call(
        kernel,
        out_shape=jax.ShapeDtypeStruct((sx, sv, cout, ss), jnp.float32),
        scratch_shapes=[pltpu.VMEM((sx + 2, 9, chans, span), jnp.bfloat16)],
    )(padded, taps)
    return out.transpose(2, 0, 1, 3).astype(jnp.bfloat16)


def conv_down(field, weight):
    return lax.conv_general_dilated(
        field[None],
        weight,
        (2, 2, 2),
        "VALID",
        dimension_numbers=NUMS,
        preferred_element_type=jnp.float32,
    )[0]


def fine_down(field, weight):
    sx, c, sv, ss = field.shape
    blocks = field.reshape(sx // 2, 2, c, sv // 2, 2, ss // 2, 2)
    return jnp.einsum("xaivbsc,oiabc->oxvs", blocks, weight, preferred_element_type=jnp.float32)


def fine_up(field, weight):
    outer = jnp.einsum("ixvs,ioabc->xaovbsc", field, weight, preferred_element_type=jnp.float32)
    chans, sx, sv, ss = (weight.shape[1], field.shape[1], field.shape[2], field.shape[3])
    return outer.reshape(2 * sx, chans, 2 * sv, 2 * ss)


def conv_up(field, weight):
    outer = jnp.einsum("ixvs,ioabc->oxavbsc", field, weight, preferred_element_type=jnp.float32)
    chans, sx, sv, ss = (weight.shape[1], field.shape[1], field.shape[2], field.shape[3])
    return outer.reshape(chans, 2 * sx, 2 * sv, 2 * ss)


def activate(value):
    return jax.nn.silu(value).astype(jnp.bfloat16)


def project(weight, field):
    return jnp.einsum("oc,cxp->oxp", weight, field, preferred_element_type=jnp.float32)


def normalize(block):
    values_f = block.astype(jnp.float32)
    mean_sq = jnp.mean(values_f * values_f, axis=0)
    return (values_f * lax.rsqrt(mean_sq + 1e-05)).astype(jnp.bfloat16)


def split_heads(weight, normed):
    chans, sx, count = normed.shape
    return project(weight, normed).astype(jnp.bfloat16).reshape(HEADS, chans // HEADS, sx, count)


def combine(queries, keys, values):
    scale = 1.0 / jnp.sqrt(jnp.float32(queries.shape[1]))
    scores = (
        jnp.einsum("hdxp,hdyp->hxyp", queries, keys, preferred_element_type=jnp.float32) * scale
    )
    weights = jax.nn.softmax(scores, axis=2).astype(jnp.bfloat16)
    attended = jnp.einsum("hxyp,hdyp->hdxp", weights, values, preferred_element_type=jnp.float32)
    heads, depth, sx, count = attended.shape
    return attended.astype(jnp.bfloat16).reshape(heads * depth, sx, count)


def finish(block, attended, w_attn_out):
    return (block.astype(jnp.float32) + project(w_attn_out, attended)).astype(jnp.bfloat16)


def on_device(
    inputs,
    w_in,
    w_fine_enc,
    w_down_mid,
    w_mid_enc,
    w_down_bottom,
    w_query,
    w_key,
    w_value,
    w_attn_out,
    w_up_mid,
    w_mid_dec,
    w_up_fine,
    w_fine_dec,
    w_head,
):
    fields = extended(inputs.transpose(1, 0, 2, 3), (("gx", 0, inputs.shape[1]),))
    first = inside_rows(fine_conv(fields, w_in).astype(jnp.bfloat16), -7)
    fine_wide = inside_rows(fine_conv(first, w_fine_enc).astype(jnp.bfloat16), -6)
    mid_in = activate(fine_down(fine_wide, w_down_mid))
    mid_wide = inside_rows(mid_conv(mid_in, w_mid_enc, MID_CROSS), -2, 1)
    mid_skip = mid_wide[:, 2:-2]
    bottom = activate(conv_down(mid_skip, unfold(w_down_bottom, 2, C2, C1)))
    chans, sx, sv, ss = bottom.shape
    flat = bottom.reshape(chans, sx, sv * ss)
    rows = lax.all_to_all(flat, "gx", split_axis=2, concat_axis=1, tiled=True)
    normed = normalize(rows)
    queries = split_heads(w_query, normed)
    keys = split_heads(w_key, normed)
    values = split_heads(w_value, normed)
    result = finish(rows, combine(queries, keys, values), w_attn_out)
    count = result.shape[2]
    groups = result.shape[1] // sx
    rim = jnp.pad(result, ((0, 0), (1, 1), (0, 0)))
    low = rim[:, : groups * sx].reshape(chans, groups, sx, count)
    high = rim[:, 2 : groups * sx + 2].reshape(chans, groups, sx, count)
    windows = jnp.concatenate([low, high], axis=2).reshape(chans, groups * 2 * sx, count)
    mixed = lax.all_to_all(windows, "gx", split_axis=1, concat_axis=2, tiled=True)
    bottom_out = mixed.reshape(chans, 2 * sx, sv, ss)
    mid_up = (
        conv_up(bottom_out, unfold(w_up_mid, 2, C2, C1)) + mid_wide.astype(jnp.float32)
    ).astype(jnp.bfloat16)
    mid_dec = inside_rows(mid_conv(mid_up, w_mid_dec, MID_CROSS), -1, 1)
    fine_up_field = (fine_up(mid_dec, w_up_fine) + fine_wide[4:-4].astype(jnp.float32)).astype(
        jnp.bfloat16
    )
    return fine_conv(fine_up_field[1:-1], w_fine_dec, head=w_head)


def solution(mesh):
    placed = (P(None, "gx", "gz", "gy"),) + (P(),) * 14
    return jax.shard_map(
        on_device, mesh=mesh, in_specs=placed, out_specs=P(None, "gx", "gz", "gy"), check_vma=False
    )
```

```python
import jax
import jax.numpy as jnp
from jax import lax
from jax.experimental import pallas as pl
from jax.experimental.pallas import tpu as pltpu
from jax.sharding import PartitionSpec as P

C1 = 64
C2 = 256
HEADS = 4


NUMS = ("NCDHW", "OIDHW", "NCDHW")
FINE_SIDES = (("gx", 0, 1), ("gy", 3, 1), ("gz", 2, 1))
FINE_CROSS = (("gy", 3, 1), ("gz", 2, 1))
MID_SIDES = (("gx", 1, 1), ("gy", 3, 1), ("gz", 2, 1))
MID_CROSS = (("gy", 3, 1), ("gz", 2, 1))


def extended(block, sides):
    for axis, dim, width in sides:
        count = lax.axis_size(axis)
        top = lax.slice_in_dim(block, block.shape[dim] - width, None, axis=dim)
        bottom = lax.slice_in_dim(block, 0, width, axis=dim)
        if count == 2:
            first = lax.axis_index(axis) == 0
            got = lax.ppermute(jnp.where(first, top, bottom), axis, [(0, 1), (1, 0)])
            low = jnp.where(first, jnp.zeros_like(got), got)
            high = jnp.where(first, got, jnp.zeros_like(got))
        else:
            forward = [(i, i + 1) for i in range(count - 1)]
            backward = [(target, source) for source, target in forward]
            low = lax.ppermute(top, axis, forward)
            high = lax.ppermute(bottom, axis, backward)
        block = jnp.concatenate([low, block, high], axis=dim)
    return block


def inside_rows(field, offset, dim=0):
    rows = field.shape[dim]
    own = rows + 2 * offset
    index = lax.axis_index("gx") * own + offset + jnp.arange(rows)
    keep = (index >= 0) & (index < own * lax.axis_size("gx"))
    shape = [1] * field.ndim
    shape[dim] = rows
    return jnp.where(keep.reshape(shape), field, jnp.zeros_like(field))


def unfold(weight, side, first, second):
    return weight.reshape(side, side, side, first, second).transpose(3, 4, 0, 1, 2)


def round_up(value, step):
    return (value + step - 1) // step * step


def fine_kernel(p_ref, e_ref, w_ref, *rest, sx, sv, ss, rows, head):
    if head:
        h_ref, o_ref, band_ref, shifted_ref = rest
    else:
        o_ref, band_ref, shifted_ref = rest
    cout, cin = w_ref.shape[1:]
    depth = cin * rows
    sv_bits, row_bits = sv.bit_length() - 1, rows.bit_length() - 1
    r = lax.broadcasted_iota(jnp.int32, (cout * sv, cout), 0)
    q = lax.broadcasted_iota(jnp.int32, (cout * sv, cout), 1)
    widen_rows = ((r >> sv_bits) == q).astype(jnp.bfloat16)
    r = lax.broadcasted_iota(jnp.int32, (cin, depth), 0)
    q = lax.broadcasted_iota(jnp.int32, (cin, depth), 1)
    widen_cols = ((q >> row_bits) == r).astype(jnp.bfloat16)
    r = lax.broadcasted_iota(jnp.int32, (cout * sv, depth), 0)
    q = lax.broadcasted_iota(jnp.int32, (cout * sv, depth), 1)
    w = q & (rows - 1)
    place = jnp.where(w < sv, w + 1, jnp.where(w == sv, 0, jnp.where(w == sv + 1, sv + 1, -8)))
    offset = place - (r & (sv - 1))
    for a in range(3):
        for c in range(3):
            band = jnp.zeros((cout * sv, depth), jnp.float32)
            for b in range(3):
                tap = w_ref[(a * 3 + b) * 3 + c]
                grown = jnp.dot(widen_rows, tap, preferred_element_type=jnp.float32)
                grown = jnp.dot(
                    grown.astype(jnp.bfloat16), widen_cols, preferred_element_type=jnp.float32
                )
                band = band + jnp.where(offset == b, grown, 0.0)
            band_ref[:, pl.ds((a * 3 + c) * depth, depth)] = band.astype(jnp.bfloat16)

    lane = lax.broadcasted_iota(jnp.int32, (depth, ss), 1)

    def shift(x, carry):
        slab = p_ref[x].astype(jnp.float32)
        edges = jnp.transpose(e_ref[x].astype(jnp.float32))
        low = jnp.where(lane == 0, edges[:, 0:1], pltpu.roll(slab, 1, 1))
        high = jnp.where(lane == ss - 1, edges[:, 1:2], pltpu.roll(slab, ss - 1, 1))
        shifted_ref[x, 0] = low.astype(jnp.bfloat16)
        shifted_ref[x, 1] = slab.astype(jnp.bfloat16)
        shifted_ref[x, 2] = high.astype(jnp.bfloat16)
        return carry

    lax.fori_loop(0, sx + 2, shift, 0)

    group = 4 if sx % 4 == 0 else 2

    def rows_pair(g, carry):
        x = group * g
        stack = jnp.concatenate(
            [shifted_ref[pl.ds(x + k, 3)].reshape(9 * depth, ss) for k in range(group)], axis=1
        )
        acc = jnp.dot(band_ref[...], stack, preferred_element_type=jnp.float32)
        act = (acc * jax.nn.sigmoid(acc)).astype(jnp.bfloat16)
        for k in range(group):
            part = act[:, k * ss : (k + 1) * ss]
            if head:
                res = jnp.dot(h_ref[...], part, preferred_element_type=jnp.float32)
                o_ref[:, x + k] = res.reshape(res.shape[0] // sv, sv, ss)
            else:
                o_ref[x + k] = part.astype(jnp.float32).reshape(cout, sv, ss)
        return carry

    lax.fori_loop(0, sx // group, rows_pair, 0)


def faces(block, axis, dim):
    count = lax.axis_size(axis)
    top = lax.slice_in_dim(block, block.shape[dim] - 1, None, axis=dim)
    bottom = lax.slice_in_dim(block, 0, 1, axis=dim)
    if count == 2:
        first = lax.axis_index(axis) == 0
        got = lax.ppermute(jnp.where(first, top, bottom), axis, [(0, 1), (1, 0)])
        return jnp.where(first, jnp.zeros_like(got), got), jnp.where(first, got, jnp.zeros_like(got))
    forward = [(i, i + 1) for i in range(count - 1)]
    backward = [(target, source) for source, target in forward]
    return lax.ppermute(top, axis, forward), lax.ppermute(bottom, axis, backward)


def fine_conv(field, weight, head=None):
    rows_x, cin, sv, ss = field.shape
    sx = rows_x - 2
    cout = weight.shape[0]
    rows = round_up(sv + 2, 16)
    wide = round_up(cin * rows, 128) // rows
    block = jnp.pad(field, ((0, 0), (0, wide - cin), (0, 0), (0, 0)))
    below, above = faces(block, "gz", 2)
    spare = jnp.zeros((rows_x, wide, rows - sv - 2, ss), block.dtype)
    padded = jnp.concatenate([block, below, above, spare], axis=2)
    left, right = faces(padded, "gy", 3)
    edges = jnp.concatenate([left, right], axis=3).transpose(0, 3, 1, 2)
    edges = jnp.pad(edges.reshape(rows_x, 2, wide * rows), ((0, 0), (0, 6), (0, 0)))
    padded = padded.reshape(rows_x, wide * rows, ss)
    taps = jnp.pad(weight, ((0, 0), (0, wide - cin), (0, 0), (0, 0), (0, 0)))
    operands = [padded, edges, taps.transpose(2, 3, 4, 0, 1).reshape(27, cout, wide)]
    if head is None:
        out_shape = jax.ShapeDtypeStruct((sx, cout, sv, ss), jnp.float32)
    else:
        eye = jnp.eye(sv, dtype=jnp.float32)
        kron = jnp.einsum("po,vw->pvow", head.astype(jnp.float32), eye)
        operands.append(kron.reshape(head.shape[0] * sv, cout * sv).astype(jnp.bfloat16))
        out_shape = jax.ShapeDtypeStruct((head.shape[0], sx, sv, ss), jnp.float32)
    kernel = lambda *refs: fine_kernel(
        *refs, sx=sx, sv=sv, ss=ss, rows=rows, head=head is not None
    )
    return pl.pallas_call(
        kernel,
        out_shape=out_shape,
        scratch_shapes=[
            pltpu.VMEM((cout * sv, 9 * wide * rows), jnp.bfloat16),
            pltpu.VMEM((sx + 2, 3, wide * rows, ss), jnp.bfloat16),
        ],
    )(*operands)


def mid_kernel(p_ref, w_ref, o_ref, shifted_ref, *, sx, sv, ss, span):
    lanes = p_ref.shape[-1]
    pitch = ss + 2

    def shift(x, carry):
        slab = p_ref[x].astype(jnp.float32)
        for b in range(3):
            for c in range(3):
                step = b * pitch + c
                piece = slab if step == 0 else pltpu.roll(slab, lanes - step, 1)
                shifted_ref[x, b * 3 + c] = piece[:, :span].astype(jnp.bfloat16)
        return carry

    lax.fori_loop(0, sx + 2, shift, 0)
    chans = shifted_ref.shape[2]

    group = 4 if sx % 4 == 0 else 2

    def rows_pair(g, carry):
        x = group * g
        stack = jnp.concatenate(
            [shifted_ref[pl.ds(x + k, 3)].reshape(27 * chans, span) for k in range(group)], axis=1
        )
        acc = jnp.dot(w_ref[...], stack, preferred_element_type=jnp.float32)
        act = (acc * jax.nn.sigmoid(acc)).astype(jnp.bfloat16).astype(jnp.float32)
        for k in range(group):
            part = act[:, k * span : (k + 1) * span]
            for v in range(sv):
                piece = part if v == 0 else pltpu.roll(part, span - v * pitch, 1)
                o_ref[x + k, v] = piece[:, :ss]
        return carry

    lax.fori_loop(0, sx // group, rows_pair, 0)


def mid_conv(field, weight, sides=MID_SIDES):
    chans = field.shape[0]
    padded = extended(field, sides)
    _, sx, sv, ss = padded.shape
    sx, sv, ss = sx - 2, sv - 2, ss - 2
    flat = (sv + 2) * (ss + 2)
    lanes = round_up(flat, 128)
    span = round_up((sv - 1) * (ss + 2) + ss, 128)
    padded = padded.transpose(1, 0, 2, 3).reshape(sx + 2, chans, flat)
    padded = jnp.pad(padded, ((0, 0), (0, 0), (0, lanes - flat)))
    cout = weight.shape[1] // chans
    taps = weight.reshape(27, cout, chans).transpose(1, 0, 2).reshape(cout, 27 * chans)
    kernel = lambda *refs: mid_kernel(*refs, sx=sx, sv=sv, ss=ss, span=span)
    out = pl.pallas_call(
        kernel,
        out_shape=jax.ShapeDtypeStruct((sx, sv, cout, ss), jnp.float32),
        scratch_shapes=[pltpu.VMEM((sx + 2, 9, chans, span), jnp.bfloat16)],
    )(padded, taps)
    return out.transpose(2, 0, 1, 3).astype(jnp.bfloat16)


def conv_down(field, weight):
    return lax.conv_general_dilated(
        field[None],
        weight,
        (2, 2, 2),
        "VALID",
        dimension_numbers=NUMS,
        preferred_element_type=jnp.float32,
    )[0]


def fine_down(field, weight):
    sx, c, sv, ss = field.shape
    blocks = field.reshape(sx // 2, 2, c, sv // 2, 2, ss // 2, 2)
    return jnp.einsum("xaivbsc,oiabc->oxvs", blocks, weight, preferred_element_type=jnp.float32)


def fine_up(field, weight):
    outer = jnp.einsum("ixvs,ioabc->xaovbsc", field, weight, preferred_element_type=jnp.float32)
    chans, sx, sv, ss = (weight.shape[1], field.shape[1], field.shape[2], field.shape[3])
    return outer.reshape(2 * sx, chans, 2 * sv, 2 * ss)


def conv_up(field, weight):
    outer = jnp.einsum("ixvs,ioabc->oxavbsc", field, weight, preferred_element_type=jnp.float32)
    chans, sx, sv, ss = (weight.shape[1], field.shape[1], field.shape[2], field.shape[3])
    return outer.reshape(chans, 2 * sx, 2 * sv, 2 * ss)


def activate(value):
    return jax.nn.silu(value).astype(jnp.bfloat16)


def project(weight, field):
    return jnp.einsum("oc,cxp->oxp", weight, field, preferred_element_type=jnp.float32)


def normalize(block):
    values_f = block.astype(jnp.float32)
    mean_sq = jnp.mean(values_f * values_f, axis=0)
    return (values_f * lax.rsqrt(mean_sq + 1e-05)).astype(jnp.bfloat16)


def split_heads(weight, normed):
    chans, sx, count = normed.shape
    return project(weight, normed).astype(jnp.bfloat16).reshape(HEADS, chans // HEADS, sx, count)


def combine(queries, keys, values):
    scale = 1.0 / jnp.sqrt(jnp.float32(queries.shape[1]))
    scores = (
        jnp.einsum("hdxp,hdyp->hxyp", queries, keys, preferred_element_type=jnp.float32) * scale
    )
    weights = jax.nn.softmax(scores, axis=2).astype(jnp.bfloat16)
    attended = jnp.einsum("hxyp,hdyp->hdxp", weights, values, preferred_element_type=jnp.float32)
    heads, depth, sx, count = attended.shape
    return attended.astype(jnp.bfloat16).reshape(heads * depth, sx, count)


def finish(block, attended, w_attn_out):
    return (block.astype(jnp.float32) + project(w_attn_out, attended)).astype(jnp.bfloat16)


def on_device(
    inputs,
    w_in,
    w_fine_enc,
    w_down_mid,
    w_mid_enc,
    w_down_bottom,
    w_query,
    w_key,
    w_value,
    w_attn_out,
    w_up_mid,
    w_mid_dec,
    w_up_fine,
    w_fine_dec,
    w_head,
):
    fields = extended(inputs.transpose(1, 0, 2, 3), (("gx", 0, inputs.shape[1]),))
    first = inside_rows(fine_conv(fields, w_in).astype(jnp.bfloat16), -7)
    fine_wide = inside_rows(fine_conv(first, w_fine_enc).astype(jnp.bfloat16), -6)
    mid_in = activate(fine_down(fine_wide, w_down_mid))
    mid_wide = inside_rows(mid_conv(mid_in, w_mid_enc, MID_CROSS), -2, 1)
    mid_skip = mid_wide[:, 2:-2]
    bottom = activate(conv_down(mid_skip, unfold(w_down_bottom, 2, C2, C1)))
    chans, sx, sv, ss = bottom.shape
    flat = bottom.reshape(chans, sx, sv * ss)
    rows = lax.all_to_all(flat, "gx", split_axis=2, concat_axis=1, tiled=True)
    normed = normalize(rows)
    queries = split_heads(w_query, normed)
    keys = split_heads(w_key, normed)
    values = split_heads(w_value, normed)
    result = finish(rows, combine(queries, keys, values), w_attn_out)
    count = result.shape[2]
    groups = result.shape[1] // sx
    rim = jnp.pad(result, ((0, 0), (1, 1), (0, 0)))
    low = rim[:, : groups * sx].reshape(chans, groups, sx, count)
    high = rim[:, 2 : groups * sx + 2].reshape(chans, groups, sx, count)
    windows = jnp.concatenate([low, high], axis=2).reshape(chans, groups * 2 * sx, count)
    mixed = lax.all_to_all(windows, "gx", split_axis=1, concat_axis=2, tiled=True)
    bottom_out = mixed.reshape(chans, 2 * sx, sv, ss)
    mid_up = (
        conv_up(bottom_out, unfold(w_up_mid, 2, C2, C1)) + mid_wide.astype(jnp.float32)
    ).astype(jnp.bfloat16)
    mid_dec = inside_rows(mid_conv(mid_up, w_mid_dec, MID_CROSS), -1, 1)
    fine_up_field = (fine_up(mid_dec, w_up_fine) + fine_wide[4:-4].astype(jnp.float32)).astype(
        jnp.bfloat16
    )
    return fine_conv(fine_up_field[1:-1], w_fine_dec, head=w_head)


def solution(mesh):
    placed = (P(None, "gx", "gz", "gy"),) + (P(),) * 14
    return jax.shard_map(
        on_device, mesh=mesh, in_specs=placed, out_specs=P(None, "gx", "gz", "gy"), check_vma=False
    )
```

```python
import jax
import jax.numpy as jnp
from jax import lax
from jax.experimental import pallas as pl
from jax.experimental.pallas import tpu as pltpu
from jax.sharding import PartitionSpec as P

C1 = 64
C2 = 256
HEADS = 4


NUMS = ("NCDHW", "OIDHW", "NCDHW")
FINE_SIDES = (("gx", 0, 1), ("gy", 3, 1), ("gz", 2, 1))
FINE_CROSS = (("gy", 3, 1), ("gz", 2, 1))
MID_SIDES = (("gx", 1, 1), ("gy", 3, 1), ("gz", 2, 1))
MID_CROSS = (("gy", 3, 1), ("gz", 2, 1))


def extended(block, sides):
    for axis, dim, width in sides:
        count = lax.axis_size(axis)
        top = lax.slice_in_dim(block, block.shape[dim] - width, None, axis=dim)
        bottom = lax.slice_in_dim(block, 0, width, axis=dim)
        if count == 2:
            first = lax.axis_index(axis) == 0
            got = lax.ppermute(jnp.where(first, top, bottom), axis, [(0, 1), (1, 0)])
            low = jnp.where(first, jnp.zeros_like(got), got)
            high = jnp.where(first, got, jnp.zeros_like(got))
        else:
            forward = [(i, i + 1) for i in range(count - 1)]
            backward = [(target, source) for source, target in forward]
            low = lax.ppermute(top, axis, forward)
            high = lax.ppermute(bottom, axis, backward)
        block = jnp.concatenate([low, block, high], axis=dim)
    return block


def inside_rows(field, offset, dim=0):
    rows = field.shape[dim]
    own = rows + 2 * offset
    index = lax.axis_index("gx") * own + offset + jnp.arange(rows)
    keep = (index >= 0) & (index < own * lax.axis_size("gx"))
    shape = [1] * field.ndim
    shape[dim] = rows
    return jnp.where(keep.reshape(shape), field, jnp.zeros_like(field))


def unfold(weight, side, first, second):
    return weight.reshape(side, side, side, first, second).transpose(3, 4, 0, 1, 2)


def round_up(value, step):
    return (value + step - 1) // step * step


def fine_kernel(p_ref, e_ref, w_ref, *rest, sx, sv, ss, rows, head):
    if head:
        h_ref, o_ref, band_ref, shifted_ref = rest
    else:
        o_ref, band_ref, shifted_ref = rest
    cout, cin = w_ref.shape[1:]
    depth = cin * rows
    sv_bits, row_bits = sv.bit_length() - 1, rows.bit_length() - 1
    r = lax.broadcasted_iota(jnp.int32, (cout * sv, cout), 0)
    q = lax.broadcasted_iota(jnp.int32, (cout * sv, cout), 1)
    widen_rows = ((r >> sv_bits) == q).astype(jnp.bfloat16)
    r = lax.broadcasted_iota(jnp.int32, (cin, depth), 0)
    q = lax.broadcasted_iota(jnp.int32, (cin, depth), 1)
    widen_cols = ((q >> row_bits) == r).astype(jnp.bfloat16)
    r = lax.broadcasted_iota(jnp.int32, (cout * sv, depth), 0)
    q = lax.broadcasted_iota(jnp.int32, (cout * sv, depth), 1)
    w = q & (rows - 1)
    place = jnp.where(w < sv, w + 1, jnp.where(w == sv, 0, jnp.where(w == sv + 1, sv + 1, -8)))
    offset = place - (r & (sv - 1))
    for a in range(3):
        for c in range(3):
            band = jnp.zeros((cout * sv, depth), jnp.float32)
            for b in range(3):
                tap = w_ref[(a * 3 + b) * 3 + c]
                grown = jnp.dot(widen_rows, tap, preferred_element_type=jnp.float32)
                grown = jnp.dot(
                    grown.astype(jnp.bfloat16), widen_cols, preferred_element_type=jnp.float32
                )
                band = band + jnp.where(offset == b, grown, 0.0)
            band_ref[:, pl.ds((a * 3 + c) * depth, depth)] = band.astype(jnp.bfloat16)

    lane = lax.broadcasted_iota(jnp.int32, (depth, ss), 1)

    def shift(x, carry):
        slab = p_ref[x].astype(jnp.float32)
        edges = jnp.transpose(e_ref[x].astype(jnp.float32))
        low = jnp.where(lane == 0, edges[:, 0:1], pltpu.roll(slab, 1, 1))
        high = jnp.where(lane == ss - 1, edges[:, 1:2], pltpu.roll(slab, ss - 1, 1))
        shifted_ref[x, 0] = low.astype(jnp.bfloat16)
        shifted_ref[x, 1] = slab.astype(jnp.bfloat16)
        shifted_ref[x, 2] = high.astype(jnp.bfloat16)
        return carry

    lax.fori_loop(0, sx + 2, shift, 0)

    group = 4 if sx % 4 == 0 else 2

    def rows_pair(g, carry):
        x = group * g
        stack = jnp.concatenate(
            [shifted_ref[pl.ds(x + k, 3)].reshape(9 * depth, ss) for k in range(group)], axis=1
        )
        acc = jnp.dot(band_ref[...], stack, preferred_element_type=jnp.float32)
        act = (acc * jax.nn.sigmoid(acc)).astype(jnp.bfloat16)
        for k in range(group):
            part = act[:, k * ss : (k + 1) * ss]
            if head:
                res = jnp.dot(h_ref[...], part, preferred_element_type=jnp.float32)
                o_ref[:, x + k] = res.reshape(res.shape[0] // sv, sv, ss)
            else:
                o_ref[x + k] = part.astype(jnp.float32).reshape(cout, sv, ss)
        return carry

    lax.fori_loop(0, sx // group, rows_pair, 0)


def faces(block, axis, dim):
    count = lax.axis_size(axis)
    top = lax.slice_in_dim(block, block.shape[dim] - 1, None, axis=dim)
    bottom = lax.slice_in_dim(block, 0, 1, axis=dim)
    if count == 2:
        first = lax.axis_index(axis) == 0
        got = lax.ppermute(jnp.where(first, top, bottom), axis, [(0, 1), (1, 0)])
        return jnp.where(first, jnp.zeros_like(got), got), jnp.where(first, got, jnp.zeros_like(got))
    forward = [(i, i + 1) for i in range(count - 1)]
    backward = [(target, source) for source, target in forward]
    return lax.ppermute(top, axis, forward), lax.ppermute(bottom, axis, backward)


def fine_conv(field, weight, head=None):
    rows_x, cin, sv, ss = field.shape
    sx = rows_x - 2
    cout = weight.shape[0]
    rows = round_up(sv + 2, 16)
    wide = round_up(cin * rows, 128) // rows
    block = jnp.pad(field, ((0, 0), (0, wide - cin), (0, 0), (0, 0)))
    below, above = faces(block, "gz", 2)
    spare = jnp.zeros((rows_x, wide, rows - sv - 2, ss), block.dtype)
    padded = jnp.concatenate([block, below, above, spare], axis=2)
    left, right = faces(padded, "gy", 3)
    edges = jnp.concatenate([left, right], axis=3).transpose(0, 3, 1, 2)
    edges = jnp.pad(edges.reshape(rows_x, 2, wide * rows), ((0, 0), (0, 6), (0, 0)))
    padded = padded.reshape(rows_x, wide * rows, ss)
    taps = jnp.pad(weight, ((0, 0), (0, wide - cin), (0, 0), (0, 0), (0, 0)))
    operands = [padded, edges, taps.transpose(2, 3, 4, 0, 1).reshape(27, cout, wide)]
    if head is None:
        out_shape = jax.ShapeDtypeStruct((sx, cout, sv, ss), jnp.float32)
    else:
        eye = jnp.eye(sv, dtype=jnp.float32)
        kron = jnp.einsum("po,vw->pvow", head.astype(jnp.float32), eye)
        operands.append(kron.reshape(head.shape[0] * sv, cout * sv).astype(jnp.bfloat16))
        out_shape = jax.ShapeDtypeStruct((head.shape[0], sx, sv, ss), jnp.float32)
    kernel = lambda *refs: fine_kernel(
        *refs, sx=sx, sv=sv, ss=ss, rows=rows, head=head is not None
    )
    return pl.pallas_call(
        kernel,
        out_shape=out_shape,
        scratch_shapes=[
            pltpu.VMEM((cout * sv, 9 * wide * rows), jnp.bfloat16),
            pltpu.VMEM((sx + 2, 3, wide * rows, ss), jnp.bfloat16),
        ],
    )(*operands)


def mid_kernel(p_ref, w_ref, o_ref, shifted_ref, *, sx, sv, ss, span):
    lanes = p_ref.shape[-1]
    pitch = ss + 2

    def shift(x, carry):
        slab = p_ref[x].astype(jnp.float32)
        for b in range(3):
            for c in range(3):
                step = b * pitch + c
                piece = slab if step == 0 else pltpu.roll(slab, lanes - step, 1)
                shifted_ref[x, b * 3 + c] = piece[:, :span].astype(jnp.bfloat16)
        return carry

    lax.fori_loop(0, sx + 2, shift, 0)
    chans = shifted_ref.shape[2]

    group = 4 if sx % 4 == 0 else 2

    def rows_pair(g, carry):
        x = group * g
        stack = jnp.concatenate(
            [shifted_ref[pl.ds(x + k, 3)].reshape(27 * chans, span) for k in range(group)], axis=1
        )
        acc = jnp.dot(w_ref[...], stack, preferred_element_type=jnp.float32)
        act = (acc * jax.nn.sigmoid(acc)).astype(jnp.bfloat16).astype(jnp.float32)
        for k in range(group):
            part = act[:, k * span : (k + 1) * span]
            for v in range(sv):
                piece = part if v == 0 else pltpu.roll(part, span - v * pitch, 1)
                o_ref[x + k, v] = piece[:, :ss]
        return carry

    lax.fori_loop(0, sx // group, rows_pair, 0)


def mid_conv(field, weight, sides=MID_SIDES):
    chans = field.shape[0]
    padded = extended(field, sides)
    _, sx, sv, ss = padded.shape
    sx, sv, ss = sx - 2, sv - 2, ss - 2
    flat = (sv + 2) * (ss + 2)
    lanes = round_up(flat, 128)
    span = round_up((sv - 1) * (ss + 2) + ss, 128)
    padded = padded.transpose(1, 0, 2, 3).reshape(sx + 2, chans, flat)
    padded = jnp.pad(padded, ((0, 0), (0, 0), (0, lanes - flat)))
    cout = weight.shape[1] // chans
    taps = weight.reshape(27, cout, chans).transpose(1, 0, 2).reshape(cout, 27 * chans)
    kernel = lambda *refs: mid_kernel(*refs, sx=sx, sv=sv, ss=ss, span=span)
    out = pl.pallas_call(
        kernel,
        out_shape=jax.ShapeDtypeStruct((sx, sv, cout, ss), jnp.float32),
        scratch_shapes=[pltpu.VMEM((sx + 2, 9, chans, span), jnp.bfloat16)],
    )(padded, taps)
    return out.transpose(2, 0, 1, 3).astype(jnp.bfloat16)


def conv_down(field, weight):
    return lax.conv_general_dilated(
        field[None],
        weight,
        (2, 2, 2),
        "VALID",
        dimension_numbers=NUMS,
        preferred_element_type=jnp.float32,
    )[0]


def fine_down(field, weight):
    sx, c, sv, ss = field.shape
    blocks = field.reshape(sx // 2, 2, c, sv // 2, 2, ss // 2, 2)
    return jnp.einsum("xaivbsc,oiabc->oxvs", blocks, weight, preferred_element_type=jnp.float32)


def fine_up(field, weight):
    flipped = jnp.flip(weight, (2, 3, 4)).transpose(1, 0, 2, 3, 4)
    out = lax.conv_general_dilated(
        field[None],
        flipped,
        (1, 1, 1),
        [(1, 1)] * 3,
        lhs_dilation=(2, 2, 2),
        dimension_numbers=NUMS,
        preferred_element_type=jnp.float32,
    )[0]
    return out.transpose(1, 0, 2, 3)


def conv_up(field, weight):
    outer = jnp.einsum("ixvs,ioabc->oxavbsc", field, weight, preferred_element_type=jnp.float32)
    chans, sx, sv, ss = (weight.shape[1], field.shape[1], field.shape[2], field.shape[3])
    return outer.reshape(chans, 2 * sx, 2 * sv, 2 * ss)


def activate(value):
    return jax.nn.silu(value).astype(jnp.bfloat16)


def project(weight, field):
    return jnp.einsum("oc,cxp->oxp", weight, field, preferred_element_type=jnp.float32)


def normalize(block):
    values_f = block.astype(jnp.float32)
    mean_sq = jnp.mean(values_f * values_f, axis=0)
    return (values_f * lax.rsqrt(mean_sq + 1e-05)).astype(jnp.bfloat16)


def split_heads(weight, normed):
    chans, sx, count = normed.shape
    return project(weight, normed).astype(jnp.bfloat16).reshape(HEADS, chans // HEADS, sx, count)


def combine(queries, keys, values):
    scale = 1.0 / jnp.sqrt(jnp.float32(queries.shape[1]))
    scores = (
        jnp.einsum("hdxp,hdyp->hxyp", queries, keys, preferred_element_type=jnp.float32) * scale
    )
    weights = jax.nn.softmax(scores, axis=2).astype(jnp.bfloat16)
    attended = jnp.einsum("hxyp,hdyp->hdxp", weights, values, preferred_element_type=jnp.float32)
    heads, depth, sx, count = attended.shape
    return attended.astype(jnp.bfloat16).reshape(heads * depth, sx, count)


def finish(block, attended, w_attn_out):
    return (block.astype(jnp.float32) + project(w_attn_out, attended)).astype(jnp.bfloat16)


def on_device(
    inputs,
    w_in,
    w_fine_enc,
    w_down_mid,
    w_mid_enc,
    w_down_bottom,
    w_query,
    w_key,
    w_value,
    w_attn_out,
    w_up_mid,
    w_mid_dec,
    w_up_fine,
    w_fine_dec,
    w_head,
):
    fields = extended(inputs.transpose(1, 0, 2, 3), (("gx", 0, inputs.shape[1]),))
    first = inside_rows(fine_conv(fields, w_in).astype(jnp.bfloat16), -7)
    fine_wide = inside_rows(fine_conv(first, w_fine_enc).astype(jnp.bfloat16), -6)
    mid_in = activate(fine_down(fine_wide, w_down_mid))
    mid_wide = inside_rows(mid_conv(mid_in, w_mid_enc, MID_CROSS), -2, 1)
    mid_skip = mid_wide[:, 2:-2]
    bottom = activate(conv_down(mid_skip, unfold(w_down_bottom, 2, C2, C1)))
    chans, sx, sv, ss = bottom.shape
    flat = bottom.reshape(chans, sx, sv * ss)
    rows = lax.all_to_all(flat, "gx", split_axis=2, concat_axis=1, tiled=True)
    normed = normalize(rows)
    queries = split_heads(w_query, normed)
    keys = split_heads(w_key, normed)
    values = split_heads(w_value, normed)
    result = finish(rows, combine(queries, keys, values), w_attn_out)
    count = result.shape[2]
    groups = result.shape[1] // sx
    rim = jnp.pad(result, ((0, 0), (1, 1), (0, 0)))
    low = rim[:, : groups * sx].reshape(chans, groups, sx, count)
    high = rim[:, 2 : groups * sx + 2].reshape(chans, groups, sx, count)
    windows = jnp.concatenate([low, high], axis=2).reshape(chans, groups * 2 * sx, count)
    mixed = lax.all_to_all(windows, "gx", split_axis=1, concat_axis=2, tiled=True)
    bottom_out = mixed.reshape(chans, 2 * sx, sv, ss)
    mid_up = (
        conv_up(bottom_out, unfold(w_up_mid, 2, C2, C1)) + mid_wide.astype(jnp.float32)
    ).astype(jnp.bfloat16)
    mid_dec = inside_rows(mid_conv(mid_up, w_mid_dec, MID_CROSS), -1, 1)
    fine_up_field = (fine_up(mid_dec, w_up_fine) + fine_wide[4:-4].astype(jnp.float32)).astype(
        jnp.bfloat16
    )
    return fine_conv(fine_up_field[1:-1], w_fine_dec, head=w_head)


def solution(mesh):
    placed = (P(None, "gx", "gz", "gy"),) + (P(),) * 14
    return jax.shard_map(
        on_device, mesh=mesh, in_specs=placed, out_specs=P(None, "gx", "gz", "gy"), check_vma=False
    )
```

```python
import jax
import jax.numpy as jnp
from jax import lax
from jax.experimental import pallas as pl
from jax.experimental.pallas import tpu as pltpu
from jax.sharding import PartitionSpec as P

C1 = 64
C2 = 256
HEADS = 4


NUMS = ("NCDHW", "OIDHW", "NCDHW")
FINE_SIDES = (("gx", 0, 1), ("gy", 3, 1), ("gz", 2, 1))
FINE_CROSS = (("gy", 3, 1), ("gz", 2, 1))
MID_SIDES = (("gx", 1, 1), ("gy", 3, 1), ("gz", 2, 1))
MID_CROSS = (("gy", 3, 1), ("gz", 2, 1))


def extended(block, sides):
    for axis, dim, width in sides:
        count = lax.axis_size(axis)
        top = lax.slice_in_dim(block, block.shape[dim] - width, None, axis=dim)
        bottom = lax.slice_in_dim(block, 0, width, axis=dim)
        if count == 2:
            first = lax.axis_index(axis) == 0
            got = lax.ppermute(jnp.where(first, top, bottom), axis, [(0, 1), (1, 0)])
            low = jnp.where(first, jnp.zeros_like(got), got)
            high = jnp.where(first, got, jnp.zeros_like(got))
        else:
            forward = [(i, i + 1) for i in range(count - 1)]
            backward = [(target, source) for source, target in forward]
            low = lax.ppermute(top, axis, forward)
            high = lax.ppermute(bottom, axis, backward)
        block = jnp.concatenate([low, block, high], axis=dim)
    return block


def inside_rows(field, offset, dim=0):
    rows = field.shape[dim]
    own = rows + 2 * offset
    index = lax.axis_index("gx") * own + offset + jnp.arange(rows)
    keep = (index >= 0) & (index < own * lax.axis_size("gx"))
    shape = [1] * field.ndim
    shape[dim] = rows
    return jnp.where(keep.reshape(shape), field, jnp.zeros_like(field))


def unfold(weight, side, first, second):
    return weight.reshape(side, side, side, first, second).transpose(3, 4, 0, 1, 2)


def round_up(value, step):
    return (value + step - 1) // step * step


def fine_kernel(p_ref, e_ref, w_ref, *rest, sx, sv, ss, rows, head):
    if head:
        h_ref, o_ref, band_ref, shifted_ref = rest
    else:
        o_ref, band_ref, shifted_ref = rest
    cout, cin = w_ref.shape[1:]
    depth = cin * rows
    sv_bits, row_bits = sv.bit_length() - 1, rows.bit_length() - 1
    r = lax.broadcasted_iota(jnp.int32, (cout * sv, cout), 0)
    q = lax.broadcasted_iota(jnp.int32, (cout * sv, cout), 1)
    widen_rows = ((r >> sv_bits) == q).astype(jnp.bfloat16)
    r = lax.broadcasted_iota(jnp.int32, (cin, depth), 0)
    q = lax.broadcasted_iota(jnp.int32, (cin, depth), 1)
    widen_cols = ((q >> row_bits) == r).astype(jnp.bfloat16)
    r = lax.broadcasted_iota(jnp.int32, (cout * sv, depth), 0)
    q = lax.broadcasted_iota(jnp.int32, (cout * sv, depth), 1)
    w = q & (rows - 1)
    place = jnp.where(w < sv, w + 1, jnp.where(w == sv, 0, jnp.where(w == sv + 1, sv + 1, -8)))
    offset = place - (r & (sv - 1))
    for a in range(3):
        for c in range(3):
            band = jnp.zeros((cout * sv, depth), jnp.float32)
            for b in range(3):
                tap = w_ref[(a * 3 + b) * 3 + c]
                grown = jnp.dot(widen_rows, tap, preferred_element_type=jnp.float32)
                grown = jnp.dot(
                    grown.astype(jnp.bfloat16), widen_cols, preferred_element_type=jnp.float32
                )
                band = band + jnp.where(offset == b, grown, 0.0)
            band_ref[:, pl.ds((a * 3 + c) * depth, depth)] = band.astype(jnp.bfloat16)

    lane = lax.broadcasted_iota(jnp.int32, (depth, ss), 1)

    def shift(x, carry):
        slab = p_ref[x].astype(jnp.float32)
        edges = e_ref[x].astype(jnp.float32)
        low = jnp.where(lane == 0, edges[:, 0:1], pltpu.roll(slab, 1, 1))
        high = jnp.where(lane == ss - 1, edges[:, 1:2], pltpu.roll(slab, ss - 1, 1))
        shifted_ref[x, 0] = low.astype(jnp.bfloat16)
        shifted_ref[x, 1] = slab.astype(jnp.bfloat16)
        shifted_ref[x, 2] = high.astype(jnp.bfloat16)
        return carry

    lax.fori_loop(0, sx + 2, shift, 0)

    group = 4 if sx % 4 == 0 else 2

    def rows_pair(g, carry):
        x = group * g
        stack = jnp.concatenate(
            [shifted_ref[pl.ds(x + k, 3)].reshape(9 * depth, ss) for k in range(group)], axis=1
        )
        acc = jnp.dot(band_ref[...], stack, preferred_element_type=jnp.float32)
        act = (acc * jax.nn.sigmoid(acc)).astype(jnp.bfloat16)
        for k in range(group):
            part = act[:, k * ss : (k + 1) * ss]
            if head:
                res = jnp.dot(h_ref[...], part, preferred_element_type=jnp.float32)
                o_ref[:, x + k] = res.reshape(res.shape[0] // sv, sv, ss)
            else:
                o_ref[x + k] = part.astype(jnp.float32).reshape(cout, sv, ss)
        return carry

    lax.fori_loop(0, sx // group, rows_pair, 0)


def faces(block, axis, dim):
    count = lax.axis_size(axis)
    top = lax.slice_in_dim(block, block.shape[dim] - 1, None, axis=dim)
    bottom = lax.slice_in_dim(block, 0, 1, axis=dim)
    if count == 2:
        first = lax.axis_index(axis) == 0
        got = lax.ppermute(jnp.where(first, top, bottom), axis, [(0, 1), (1, 0)])
        return jnp.where(first, jnp.zeros_like(got), got), jnp.where(first, got, jnp.zeros_like(got))
    forward = [(i, i + 1) for i in range(count - 1)]
    backward = [(target, source) for source, target in forward]
    return lax.ppermute(top, axis, forward), lax.ppermute(bottom, axis, backward)


def fine_conv(field, weight, head=None):
    rows_x, cin, sv, ss = field.shape
    sx = rows_x - 2
    cout = weight.shape[0]
    rows = round_up(sv + 2, 16)
    wide = round_up(cin * rows, 128) // rows
    block = jnp.pad(field, ((0, 0), (0, wide - cin), (0, 0), (0, 0)))
    below, above = faces(block, "gz", 2)
    spare = jnp.zeros((rows_x, wide, rows - sv - 2, ss), block.dtype)
    padded = jnp.concatenate([block, below, above, spare], axis=2)
    left, right = faces(padded, "gy", 3)
    edges = jnp.concatenate([left, right], axis=3).reshape(rows_x, wide * rows, 2)
    padded = padded.reshape(rows_x, wide * rows, ss)
    taps = jnp.pad(weight, ((0, 0), (0, wide - cin), (0, 0), (0, 0), (0, 0)))
    operands = [padded, edges, taps.transpose(2, 3, 4, 0, 1).reshape(27, cout, wide)]
    if head is None:
        out_shape = jax.ShapeDtypeStruct((sx, cout, sv, ss), jnp.float32)
    else:
        eye = jnp.eye(sv, dtype=jnp.float32)
        kron = jnp.einsum("po,vw->pvow", head.astype(jnp.float32), eye)
        operands.append(kron.reshape(head.shape[0] * sv, cout * sv).astype(jnp.bfloat16))
        out_shape = jax.ShapeDtypeStruct((head.shape[0], sx, sv, ss), jnp.float32)
    kernel = lambda *refs: fine_kernel(
        *refs, sx=sx, sv=sv, ss=ss, rows=rows, head=head is not None
    )
    return pl.pallas_call(
        kernel,
        out_shape=out_shape,
        scratch_shapes=[
            pltpu.VMEM((cout * sv, 9 * wide * rows), jnp.bfloat16),
            pltpu.VMEM((sx + 2, 3, wide * rows, ss), jnp.bfloat16),
        ],
    )(*operands)


def mid_kernel(p_ref, w_ref, o_ref, shifted_ref, *, sx, sv, ss, span):
    lanes = p_ref.shape[-1]
    pitch = ss + 2

    def shift(x, carry):
        slab = p_ref[x].astype(jnp.float32)
        for b in range(3):
            for c in range(3):
                step = b * pitch + c
                piece = slab if step == 0 else pltpu.roll(slab, lanes - step, 1)
                shifted_ref[x, b * 3 + c] = piece[:, :span].astype(jnp.bfloat16)
        return carry

    lax.fori_loop(0, sx + 2, shift, 0)
    chans = shifted_ref.shape[2]

    group = 4 if sx % 4 == 0 else 2

    def rows_pair(g, carry):
        x = group * g
        stack = jnp.concatenate(
            [shifted_ref[pl.ds(x + k, 3)].reshape(27 * chans, span) for k in range(group)], axis=1
        )
        acc = jnp.dot(w_ref[...], stack, preferred_element_type=jnp.float32)
        act = (acc * jax.nn.sigmoid(acc)).astype(jnp.bfloat16).astype(jnp.float32)
        for k in range(group):
            part = act[:, k * span : (k + 1) * span]
            for v in range(sv):
                piece = part if v == 0 else pltpu.roll(part, span - v * pitch, 1)
                o_ref[x + k, v] = piece[:, :ss]
        return carry

    lax.fori_loop(0, sx // group, rows_pair, 0)


def mid_conv(field, weight, sides=MID_SIDES):
    chans = field.shape[0]
    padded = extended(field, sides)
    _, sx, sv, ss = padded.shape
    sx, sv, ss = sx - 2, sv - 2, ss - 2
    flat = (sv + 2) * (ss + 2)
    lanes = round_up(flat, 128)
    span = round_up((sv - 1) * (ss + 2) + ss, 128)
    padded = padded.transpose(1, 0, 2, 3).reshape(sx + 2, chans, flat)
    padded = jnp.pad(padded, ((0, 0), (0, 0), (0, lanes - flat)))
    cout = weight.shape[1] // chans
    taps = weight.reshape(27, cout, chans).transpose(1, 0, 2).reshape(cout, 27 * chans)
    kernel = lambda *refs: mid_kernel(*refs, sx=sx, sv=sv, ss=ss, span=span)
    out = pl.pallas_call(
        kernel,
        out_shape=jax.ShapeDtypeStruct((sx, sv, cout, ss), jnp.float32),
        scratch_shapes=[pltpu.VMEM((sx + 2, 9, chans, span), jnp.bfloat16)],
    )(padded, taps)
    return out.transpose(2, 0, 1, 3).astype(jnp.bfloat16)


def conv_down(field, weight):
    return lax.conv_general_dilated(
        field[None],
        weight,
        (2, 2, 2),
        "VALID",
        dimension_numbers=NUMS,
        preferred_element_type=jnp.float32,
    )[0]


def fine_down(field, weight):
    sx, c, sv, ss = field.shape
    blocks = field.reshape(sx // 2, 2, c, sv // 2, 2, ss // 2, 2)
    return jnp.einsum("xaivbsc,oiabc->oxvs", blocks, weight, preferred_element_type=jnp.float32)


def fine_up(field, weight):
    outer = jnp.einsum("ixvs,ioabc->xaovbsc", field, weight, preferred_element_type=jnp.float32)
    chans, sx, sv, ss = (weight.shape[1], field.shape[1], field.shape[2], field.shape[3])
    return outer.reshape(2 * sx, chans, 2 * sv, 2 * ss)


def conv_up(field, weight):
    outer = jnp.einsum("ixvs,ioabc->oxavbsc", field, weight, preferred_element_type=jnp.float32)
    chans, sx, sv, ss = (weight.shape[1], field.shape[1], field.shape[2], field.shape[3])
    return outer.reshape(chans, 2 * sx, 2 * sv, 2 * ss)


def activate(value):
    return jax.nn.silu(value).astype(jnp.bfloat16)


def project(weight, field):
    return jnp.einsum("oc,cxp->oxp", weight, field, preferred_element_type=jnp.float32)


def normalize(block):
    values_f = block.astype(jnp.float32)
    mean_sq = jnp.mean(values_f * values_f, axis=0)
    return (values_f * lax.rsqrt(mean_sq + 1e-05)).astype(jnp.bfloat16)


def split_heads(weight, normed):
    chans, sx, count = normed.shape
    return project(weight, normed).astype(jnp.bfloat16).reshape(HEADS, chans // HEADS, sx, count)


def combine(queries, keys, values):
    scale = 1.0 / jnp.sqrt(jnp.float32(queries.shape[1]))
    scores = (
        jnp.einsum("hdxp,hdyp->hxyp", queries, keys, preferred_element_type=jnp.float32) * scale
    )
    weights = jax.nn.softmax(scores, axis=2).astype(jnp.bfloat16)
    attended = jnp.einsum("hxyp,hdyp->hdxp", weights, values, preferred_element_type=jnp.float32)
    heads, depth, sx, count = attended.shape
    return attended.astype(jnp.bfloat16).reshape(heads * depth, sx, count)


def finish(block, attended, w_attn_out):
    return (block.astype(jnp.float32) + project(w_attn_out, attended)).astype(jnp.bfloat16)


def on_device(
    inputs,
    w_in,
    w_fine_enc,
    w_down_mid,
    w_mid_enc,
    w_down_bottom,
    w_query,
    w_key,
    w_value,
    w_attn_out,
    w_up_mid,
    w_mid_dec,
    w_up_fine,
    w_fine_dec,
    w_head,
):
    fields = extended(inputs.transpose(1, 0, 2, 3), (("gx", 0, inputs.shape[1]),))
    first = inside_rows(fine_conv(fields, w_in).astype(jnp.bfloat16), -7)
    fine_wide = inside_rows(fine_conv(first, w_fine_enc).astype(jnp.bfloat16), -6)
    mid_in = activate(fine_down(fine_wide, w_down_mid))
    mid_wide = inside_rows(mid_conv(mid_in, w_mid_enc, MID_CROSS), -2, 1)
    mid_skip = mid_wide[:, 2:-2]
    bottom = activate(conv_down(mid_skip, unfold(w_down_bottom, 2, C2, C1)))
    chans, sx, sv, ss = bottom.shape
    flat = bottom.reshape(chans, sx, sv * ss)
    rows = lax.all_to_all(flat, "gx", split_axis=2, concat_axis=1, tiled=True)
    normed = normalize(rows)
    queries = split_heads(w_query, normed)
    keys = split_heads(w_key, normed)
    values = split_heads(w_value, normed)
    result = finish(rows, combine(queries, keys, values), w_attn_out)
    count = result.shape[2]
    groups = result.shape[1] // sx
    rim = jnp.pad(result, ((0, 0), (1, 1), (0, 0)))
    low = rim[:, : groups * sx].reshape(chans, groups, sx, count)
    high = rim[:, 2 : groups * sx + 2].reshape(chans, groups, sx, count)
    windows = jnp.concatenate([low, high], axis=2).reshape(chans, groups * 2 * sx, count)
    mixed = lax.all_to_all(windows, "gx", split_axis=1, concat_axis=2, tiled=True)
    bottom_out = mixed.reshape(chans, 2 * sx, sv, ss)
    mid_up = (
        conv_up(bottom_out, unfold(w_up_mid, 2, C2, C1)) + mid_wide.astype(jnp.float32)
    ).astype(jnp.bfloat16)
    mid_dec = inside_rows(mid_conv(mid_up, w_mid_dec, MID_CROSS), -1, 1)
    fine_up_field = (fine_up(mid_dec, w_up_fine) + fine_wide[4:-4].astype(jnp.float32)).astype(
        jnp.bfloat16
    )
    return fine_conv(fine_up_field[1:-1], w_fine_dec, head=w_head)


def solution(mesh):
    placed = (P(None, "gx", "gz", "gy"),) + (P(),) * 14
    return jax.shard_map(
        on_device, mesh=mesh, in_specs=placed, out_specs=P(None, "gx", "gz", "gy"), check_vma=False
    )
```

```python
import jax
import jax.numpy as jnp
from jax import lax
from jax.experimental import pallas as pl
from jax.experimental.pallas import tpu as pltpu
from jax.sharding import PartitionSpec as P

C1 = 64
C2 = 256
HEADS = 4


NUMS = ("NCDHW", "OIDHW", "NCDHW")
FINE_SIDES = (("gx", 0, 1), ("gy", 3, 1), ("gz", 2, 1))
FINE_CROSS = (("gy", 3, 1), ("gz", 2, 1))
MID_SIDES = (("gx", 1, 1), ("gy", 3, 1), ("gz", 2, 1))
MID_CROSS = (("gy", 3, 1), ("gz", 2, 1))


def extended(block, sides):
    for axis, dim, width in sides:
        count = lax.axis_size(axis)
        top = lax.slice_in_dim(block, block.shape[dim] - width, None, axis=dim)
        bottom = lax.slice_in_dim(block, 0, width, axis=dim)
        if count == 2:
            first = lax.axis_index(axis) == 0
            got = lax.ppermute(jnp.where(first, top, bottom), axis, [(0, 1), (1, 0)])
            low = jnp.where(first, jnp.zeros_like(got), got)
            high = jnp.where(first, got, jnp.zeros_like(got))
        else:
            forward = [(i, i + 1) for i in range(count - 1)]
            backward = [(target, source) for source, target in forward]
            low = lax.ppermute(top, axis, forward)
            high = lax.ppermute(bottom, axis, backward)
        block = jnp.concatenate([low, block, high], axis=dim)
    return block


def inside_rows(field, offset, dim=0):
    rows = field.shape[dim]
    own = rows + 2 * offset
    index = lax.axis_index("gx") * own + offset + jnp.arange(rows)
    keep = (index >= 0) & (index < own * lax.axis_size("gx"))
    shape = [1] * field.ndim
    shape[dim] = rows
    return jnp.where(keep.reshape(shape), field, jnp.zeros_like(field))


def unfold(weight, side, first, second):
    return weight.reshape(side, side, side, first, second).transpose(3, 4, 0, 1, 2)


def round_up(value, step):
    return (value + step - 1) // step * step


def fine_kernel(p_ref, e_ref, w_ref, *rest, sx, sv, ss, rows, head):
    if head:
        h_ref, o_ref, band_ref, shifted_ref = rest
    else:
        o_ref, band_ref, shifted_ref = rest
    cout, cin = w_ref.shape[1:]
    depth = cin * rows
    sv_bits, row_bits = sv.bit_length() - 1, rows.bit_length() - 1
    r = lax.broadcasted_iota(jnp.int32, (cout * sv, cout), 0)
    q = lax.broadcasted_iota(jnp.int32, (cout * sv, cout), 1)
    widen_rows = ((r >> sv_bits) == q).astype(jnp.bfloat16)
    r = lax.broadcasted_iota(jnp.int32, (cin, depth), 0)
    q = lax.broadcasted_iota(jnp.int32, (cin, depth), 1)
    widen_cols = ((q >> row_bits) == r).astype(jnp.bfloat16)
    r = lax.broadcasted_iota(jnp.int32, (cout * sv, depth), 0)
    q = lax.broadcasted_iota(jnp.int32, (cout * sv, depth), 1)
    w = q & (rows - 1)
    place = jnp.where(w < sv, w + 1, jnp.where(w == sv, 0, jnp.where(w == sv + 1, sv + 1, -8)))
    offset = place - (r & (sv - 1))
    for a in range(3):
        for c in range(3):
            band = jnp.zeros((cout * sv, depth), jnp.float32)
            for b in range(3):
                tap = w_ref[(a * 3 + b) * 3 + c]
                grown = jnp.dot(widen_rows, tap, preferred_element_type=jnp.float32)
                grown = jnp.dot(
                    grown.astype(jnp.bfloat16), widen_cols, preferred_element_type=jnp.float32
                )
                band = band + jnp.where(offset == b, grown, 0.0)
            band_ref[:, pl.ds((a * 3 + c) * depth, depth)] = band.astype(jnp.bfloat16)

    lane = lax.broadcasted_iota(jnp.int32, (depth, ss), 1)

    def shift(x, carry):
        slab = p_ref[x].astype(jnp.float32)
        edges = e_ref[x].astype(jnp.float32)
        low = jnp.where(lane == 0, edges, pltpu.roll(slab, 1, 1))
        high = jnp.where(lane == ss - 1, edges, pltpu.roll(slab, ss - 1, 1))
        shifted_ref[x, 0] = low.astype(jnp.bfloat16)
        shifted_ref[x, 1] = slab.astype(jnp.bfloat16)
        shifted_ref[x, 2] = high.astype(jnp.bfloat16)
        return carry

    lax.fori_loop(0, sx + 2, shift, 0)

    group = 4 if sx % 4 == 0 else 2

    def rows_pair(g, carry):
        x = group * g
        stack = jnp.concatenate(
            [shifted_ref[pl.ds(x + k, 3)].reshape(9 * depth, ss) for k in range(group)], axis=1
        )
        acc = jnp.dot(band_ref[...], stack, preferred_element_type=jnp.float32)
        act = (acc * jax.nn.sigmoid(acc)).astype(jnp.bfloat16)
        for k in range(group):
            part = act[:, k * ss : (k + 1) * ss]
            if head:
                res = jnp.dot(h_ref[...], part, preferred_element_type=jnp.float32)
                o_ref[:, x + k] = res.reshape(res.shape[0] // sv, sv, ss)
            else:
                o_ref[x + k] = part.astype(jnp.float32).reshape(cout, sv, ss)
        return carry

    lax.fori_loop(0, sx // group, rows_pair, 0)


def faces(block, axis, dim):
    count = lax.axis_size(axis)
    top = lax.slice_in_dim(block, block.shape[dim] - 1, None, axis=dim)
    bottom = lax.slice_in_dim(block, 0, 1, axis=dim)
    if count == 2:
        first = lax.axis_index(axis) == 0
        got = lax.ppermute(jnp.where(first, top, bottom), axis, [(0, 1), (1, 0)])
        return jnp.where(first, jnp.zeros_like(got), got), jnp.where(first, got, jnp.zeros_like(got))
    forward = [(i, i + 1) for i in range(count - 1)]
    backward = [(target, source) for source, target in forward]
    return lax.ppermute(top, axis, forward), lax.ppermute(bottom, axis, backward)


def fine_conv(field, weight, head=None):
    rows_x, cin, sv, ss = field.shape
    sx = rows_x - 2
    cout = weight.shape[0]
    rows = round_up(sv + 2, 16)
    wide = round_up(cin * rows, 128) // rows
    block = jnp.pad(field, ((0, 0), (0, wide - cin), (0, 0), (0, 0)))
    below, above = faces(block, "gz", 2)
    spare = jnp.zeros((rows_x, wide, rows - sv - 2, ss), block.dtype)
    padded = jnp.concatenate([block, below, above, spare], axis=2)
    left, right = faces(padded, "gy", 3)
    middle = jnp.zeros(left.shape[:3] + (ss - 2,), left.dtype)
    edges = jnp.concatenate([left, middle, right], axis=3).reshape(rows_x, wide * rows, ss)
    padded = padded.reshape(rows_x, wide * rows, ss)
    taps = jnp.pad(weight, ((0, 0), (0, wide - cin), (0, 0), (0, 0), (0, 0)))
    operands = [padded, edges, taps.transpose(2, 3, 4, 0, 1).reshape(27, cout, wide)]
    if head is None:
        out_shape = jax.ShapeDtypeStruct((sx, cout, sv, ss), jnp.float32)
    else:
        eye = jnp.eye(sv, dtype=jnp.float32)
        kron = jnp.einsum("po,vw->pvow", head.astype(jnp.float32), eye)
        operands.append(kron.reshape(head.shape[0] * sv, cout * sv).astype(jnp.bfloat16))
        out_shape = jax.ShapeDtypeStruct((head.shape[0], sx, sv, ss), jnp.float32)
    kernel = lambda *refs: fine_kernel(
        *refs, sx=sx, sv=sv, ss=ss, rows=rows, head=head is not None
    )
    return pl.pallas_call(
        kernel,
        out_shape=out_shape,
        scratch_shapes=[
            pltpu.VMEM((cout * sv, 9 * wide * rows), jnp.bfloat16),
            pltpu.VMEM((sx + 2, 3, wide * rows, ss), jnp.bfloat16),
        ],
    )(*operands)


def mid_kernel(p_ref, w_ref, o_ref, shifted_ref, *, sx, sv, ss, span):
    lanes = p_ref.shape[-1]
    pitch = ss + 2

    def shift(x, carry):
        slab = p_ref[x].astype(jnp.float32)
        for b in range(3):
            for c in range(3):
                step = b * pitch + c
                piece = slab if step == 0 else pltpu.roll(slab, lanes - step, 1)
                shifted_ref[x, b * 3 + c] = piece[:, :span].astype(jnp.bfloat16)
        return carry

    lax.fori_loop(0, sx + 2, shift, 0)
    chans = shifted_ref.shape[2]

    group = 4 if sx % 4 == 0 else 2

    def rows_pair(g, carry):
        x = group * g
        stack = jnp.concatenate(
            [shifted_ref[pl.ds(x + k, 3)].reshape(27 * chans, span) for k in range(group)], axis=1
        )
        acc = jnp.dot(w_ref[...], stack, preferred_element_type=jnp.float32)
        act = (acc * jax.nn.sigmoid(acc)).astype(jnp.bfloat16).astype(jnp.float32)
        for k in range(group):
            part = act[:, k * span : (k + 1) * span]
            for v in range(sv):
                piece = part if v == 0 else pltpu.roll(part, span - v * pitch, 1)
                o_ref[x + k, v] = piece[:, :ss]
        return carry

    lax.fori_loop(0, sx // group, rows_pair, 0)


def mid_conv(field, weight, sides=MID_SIDES):
    chans = field.shape[0]
    padded = extended(field, sides)
    _, sx, sv, ss = padded.shape
    sx, sv, ss = sx - 2, sv - 2, ss - 2
    flat = (sv + 2) * (ss + 2)
    lanes = round_up(flat, 128)
    span = round_up((sv - 1) * (ss + 2) + ss, 128)
    padded = padded.transpose(1, 0, 2, 3).reshape(sx + 2, chans, flat)
    padded = jnp.pad(padded, ((0, 0), (0, 0), (0, lanes - flat)))
    cout = weight.shape[1] // chans
    taps = weight.reshape(27, cout, chans).transpose(1, 0, 2).reshape(cout, 27 * chans)
    kernel = lambda *refs: mid_kernel(*refs, sx=sx, sv=sv, ss=ss, span=span)
    out = pl.pallas_call(
        kernel,
        out_shape=jax.ShapeDtypeStruct((sx, sv, cout, ss), jnp.float32),
        scratch_shapes=[pltpu.VMEM((sx + 2, 9, chans, span), jnp.bfloat16)],
    )(padded, taps)
    return out.transpose(2, 0, 1, 3).astype(jnp.bfloat16)


def conv_down(field, weight):
    return lax.conv_general_dilated(
        field[None],
        weight,
        (2, 2, 2),
        "VALID",
        dimension_numbers=NUMS,
        preferred_element_type=jnp.float32,
    )[0]


def fine_down(field, weight):
    sx, c, sv, ss = field.shape
    blocks = field.reshape(sx // 2, 2, c, sv // 2, 2, ss // 2, 2)
    return jnp.einsum("xaivbsc,oiabc->oxvs", blocks, weight, preferred_element_type=jnp.float32)


def fine_up(field, weight):
    outer = jnp.einsum("ixvs,ioabc->xaovbsc", field, weight, preferred_element_type=jnp.float32)
    chans, sx, sv, ss = (weight.shape[1], field.shape[1], field.shape[2], field.shape[3])
    return outer.reshape(2 * sx, chans, 2 * sv, 2 * ss)


def conv_up(field, weight):
    outer = jnp.einsum("ixvs,ioabc->oxavbsc", field, weight, preferred_element_type=jnp.float32)
    chans, sx, sv, ss = (weight.shape[1], field.shape[1], field.shape[2], field.shape[3])
    return outer.reshape(chans, 2 * sx, 2 * sv, 2 * ss)


def activate(value):
    return jax.nn.silu(value).astype(jnp.bfloat16)


def project(weight, field):
    return jnp.einsum("oc,cxp->oxp", weight, field, preferred_element_type=jnp.float32)


def normalize(block):
    values_f = block.astype(jnp.float32)
    mean_sq = jnp.mean(values_f * values_f, axis=0)
    return (values_f * lax.rsqrt(mean_sq + 1e-05)).astype(jnp.bfloat16)


def split_heads(weight, normed):
    chans, sx, count = normed.shape
    return project(weight, normed).astype(jnp.bfloat16).reshape(HEADS, chans // HEADS, sx, count)


def combine(queries, keys, values):
    scale = 1.0 / jnp.sqrt(jnp.float32(queries.shape[1]))
    scores = (
        jnp.einsum("hdxp,hdyp->hxyp", queries, keys, preferred_element_type=jnp.float32) * scale
    )
    weights = jax.nn.softmax(scores, axis=2).astype(jnp.bfloat16)
    attended = jnp.einsum("hxyp,hdyp->hdxp", weights, values, preferred_element_type=jnp.float32)
    heads, depth, sx, count = attended.shape
    return attended.astype(jnp.bfloat16).reshape(heads * depth, sx, count)


def finish(block, attended, w_attn_out):
    return (block.astype(jnp.float32) + project(w_attn_out, attended)).astype(jnp.bfloat16)


def on_device(
    inputs,
    w_in,
    w_fine_enc,
    w_down_mid,
    w_mid_enc,
    w_down_bottom,
    w_query,
    w_key,
    w_value,
    w_attn_out,
    w_up_mid,
    w_mid_dec,
    w_up_fine,
    w_fine_dec,
    w_head,
):
    fields = extended(inputs.transpose(1, 0, 2, 3), (("gx", 0, inputs.shape[1]),))
    first = inside_rows(fine_conv(fields, w_in).astype(jnp.bfloat16), -7)
    fine_wide = inside_rows(fine_conv(first, w_fine_enc).astype(jnp.bfloat16), -6)
    mid_in = activate(fine_down(fine_wide, w_down_mid))
    mid_wide = inside_rows(mid_conv(mid_in, w_mid_enc, MID_CROSS), -2, 1)
    mid_skip = mid_wide[:, 2:-2]
    bottom = activate(conv_down(mid_skip, unfold(w_down_bottom, 2, C2, C1)))
    chans, sx, sv, ss = bottom.shape
    flat = bottom.reshape(chans, sx, sv * ss)
    rows = lax.all_to_all(flat, "gx", split_axis=2, concat_axis=1, tiled=True)
    normed = normalize(rows)
    queries = split_heads(w_query, normed)
    keys = split_heads(w_key, normed)
    values = split_heads(w_value, normed)
    result = finish(rows, combine(queries, keys, values), w_attn_out)
    count = result.shape[2]
    groups = result.shape[1] // sx
    rim = jnp.pad(result, ((0, 0), (1, 1), (0, 0)))
    low = rim[:, : groups * sx].reshape(chans, groups, sx, count)
    high = rim[:, 2 : groups * sx + 2].reshape(chans, groups, sx, count)
    windows = jnp.concatenate([low, high], axis=2).reshape(chans, groups * 2 * sx, count)
    mixed = lax.all_to_all(windows, "gx", split_axis=1, concat_axis=2, tiled=True)
    bottom_out = mixed.reshape(chans, 2 * sx, sv, ss)
    mid_up = (
        conv_up(bottom_out, unfold(w_up_mid, 2, C2, C1)) + mid_wide.astype(jnp.float32)
    ).astype(jnp.bfloat16)
    mid_dec = inside_rows(mid_conv(mid_up, w_mid_dec, MID_CROSS), -1, 1)
    fine_up_field = (fine_up(mid_dec, w_up_fine) + fine_wide[4:-4].astype(jnp.float32)).astype(
        jnp.bfloat16
    )
    return fine_conv(fine_up_field[1:-1], w_fine_dec, head=w_head)


def solution(mesh):
    placed = (P(None, "gx", "gz", "gy"),) + (P(),) * 14
    return jax.shard_map(
        on_device, mesh=mesh, in_specs=placed, out_specs=P(None, "gx", "gz", "gy"), check_vma=False
    )
```

```python
import jax
import jax.numpy as jnp
from jax import lax
from jax.experimental import pallas as pl
from jax.experimental.pallas import tpu as pltpu
from jax.sharding import PartitionSpec as P

C1 = 64
C2 = 256
HEADS = 4


NUMS = ("NCDHW", "OIDHW", "NCDHW")
FINE_SIDES = (("gx", 0, 1), ("gy", 3, 1), ("gz", 2, 1))
FINE_CROSS = (("gy", 3, 1), ("gz", 2, 1))
MID_SIDES = (("gx", 1, 1), ("gy", 3, 1), ("gz", 2, 1))
MID_CROSS = (("gy", 3, 1), ("gz", 2, 1))


def extended(block, sides):
    for axis, dim, width in sides:
        count = lax.axis_size(axis)
        top = lax.slice_in_dim(block, block.shape[dim] - width, None, axis=dim)
        bottom = lax.slice_in_dim(block, 0, width, axis=dim)
        if count == 2:
            first = lax.axis_index(axis) == 0
            got = lax.ppermute(jnp.where(first, top, bottom), axis, [(0, 1), (1, 0)])
            low = jnp.where(first, jnp.zeros_like(got), got)
            high = jnp.where(first, got, jnp.zeros_like(got))
        else:
            forward = [(i, i + 1) for i in range(count - 1)]
            backward = [(target, source) for source, target in forward]
            low = lax.ppermute(top, axis, forward)
            high = lax.ppermute(bottom, axis, backward)
        block = jnp.concatenate([low, block, high], axis=dim)
    return block


def inside_rows(field, offset, dim=0):
    rows = field.shape[dim]
    own = rows + 2 * offset
    index = lax.axis_index("gx") * own + offset + jnp.arange(rows)
    keep = (index >= 0) & (index < own * lax.axis_size("gx"))
    shape = [1] * field.ndim
    shape[dim] = rows
    return jnp.where(keep.reshape(shape), field, jnp.zeros_like(field))


def unfold(weight, side, first, second):
    return weight.reshape(side, side, side, first, second).transpose(3, 4, 0, 1, 2)


def round_up(value, step):
    return (value + step - 1) // step * step


def fine_kernel(p_ref, e_ref, w_ref, *rest, sx, sv, ss, rows, head):
    if head:
        h_ref, o_ref, band_ref, shifted_ref = rest
    else:
        o_ref, band_ref, shifted_ref = rest
    cout, cin = w_ref.shape[1:]
    depth = cin * rows
    sv_bits, row_bits = sv.bit_length() - 1, rows.bit_length() - 1
    r = lax.broadcasted_iota(jnp.int32, (cout * sv, cout), 0)
    q = lax.broadcasted_iota(jnp.int32, (cout * sv, cout), 1)
    widen_rows = ((r >> sv_bits) == q).astype(jnp.bfloat16)
    r = lax.broadcasted_iota(jnp.int32, (cin, depth), 0)
    q = lax.broadcasted_iota(jnp.int32, (cin, depth), 1)
    widen_cols = ((q >> row_bits) == r).astype(jnp.bfloat16)
    r = lax.broadcasted_iota(jnp.int32, (cout * sv, depth), 0)
    q = lax.broadcasted_iota(jnp.int32, (cout * sv, depth), 1)
    w = q & (rows - 1)
    place = jnp.where(w < sv, w + 1, jnp.where(w == sv, 0, jnp.where(w == sv + 1, sv + 1, -8)))
    offset = place - (r & (sv - 1))
    for a in range(3):
        for c in range(3):

            def add_tap(b, band):
                tap = w_ref[(a * 3 + b) * 3 + c]
                grown = jnp.dot(widen_rows, tap, preferred_element_type=jnp.float32)
                grown = jnp.dot(
                    grown.astype(jnp.bfloat16), widen_cols, preferred_element_type=jnp.float32
                )
                return band + jnp.where(offset == b, grown, 0.0)

            band = lax.fori_loop(0, 3, add_tap, jnp.zeros((cout * sv, depth), jnp.float32))
            band_ref[:, pl.ds((a * 3 + c) * depth, depth)] = band.astype(jnp.bfloat16)

    lane = lax.broadcasted_iota(jnp.int32, (depth, ss), 1)

    def shift(x, carry):
        slab = p_ref[x].astype(jnp.float32)
        edges = jnp.transpose(e_ref[x].astype(jnp.float32))
        low = jnp.where(lane == 0, edges[:, 0:1], pltpu.roll(slab, 1, 1))
        high = jnp.where(lane == ss - 1, edges[:, 1:2], pltpu.roll(slab, ss - 1, 1))
        shifted_ref[x, 0] = low.astype(jnp.bfloat16)
        shifted_ref[x, 1] = slab.astype(jnp.bfloat16)
        shifted_ref[x, 2] = high.astype(jnp.bfloat16)
        return carry

    lax.fori_loop(0, sx + 2, shift, 0)

    group = 4 if sx % 4 == 0 else 2

    def rows_pair(g, carry):
        x = group * g
        stack = jnp.concatenate(
            [shifted_ref[pl.ds(x + k, 3)].reshape(9 * depth, ss) for k in range(group)], axis=1
        )
        acc = jnp.dot(band_ref[...], stack, preferred_element_type=jnp.float32)
        act = (acc * jax.nn.sigmoid(acc)).astype(jnp.bfloat16)
        for k in range(group):
            part = act[:, k * ss : (k + 1) * ss]
            if head:
                res = jnp.dot(h_ref[...], part, preferred_element_type=jnp.float32)
                o_ref[:, x + k] = res.reshape(res.shape[0] // sv, sv, ss)
            else:
                o_ref[x + k] = part.astype(jnp.float32).reshape(cout, sv, ss)
        return carry

    lax.fori_loop(0, sx // group, rows_pair, 0)


def faces(block, axis, dim):
    count = lax.axis_size(axis)
    top = lax.slice_in_dim(block, block.shape[dim] - 1, None, axis=dim)
    bottom = lax.slice_in_dim(block, 0, 1, axis=dim)
    if count == 2:
        first = lax.axis_index(axis) == 0
        got = lax.ppermute(jnp.where(first, top, bottom), axis, [(0, 1), (1, 0)])
        return jnp.where(first, jnp.zeros_like(got), got), jnp.where(first, got, jnp.zeros_like(got))
    forward = [(i, i + 1) for i in range(count - 1)]
    backward = [(target, source) for source, target in forward]
    return lax.ppermute(top, axis, forward), lax.ppermute(bottom, axis, backward)


def fine_conv(field, weight, head=None):
    rows_x, cin, sv, ss = field.shape
    sx = rows_x - 2
    cout = weight.shape[0]
    rows = round_up(sv + 2, 16)
    wide = round_up(cin * rows, 128) // rows
    block = jnp.pad(field, ((0, 0), (0, wide - cin), (0, 0), (0, 0)))
    below, above = faces(block, "gz", 2)
    spare = jnp.zeros((rows_x, wide, rows - sv - 2, ss), block.dtype)
    padded = jnp.concatenate([block, below, above, spare], axis=2)
    left, right = faces(padded, "gy", 3)
    edges = jnp.concatenate([left, right], axis=3).transpose(0, 3, 1, 2)
    edges = jnp.pad(edges.reshape(rows_x, 2, wide * rows), ((0, 0), (0, 6), (0, 0)))
    padded = padded.reshape(rows_x, wide * rows, ss)
    taps = jnp.pad(weight, ((0, 0), (0, wide - cin), (0, 0), (0, 0), (0, 0)))
    operands = [padded, edges, taps.transpose(2, 3, 4, 0, 1).reshape(27, cout, wide)]
    if head is None:
        out_shape = jax.ShapeDtypeStruct((sx, cout, sv, ss), jnp.float32)
    else:
        eye = jnp.eye(sv, dtype=jnp.float32)
        kron = jnp.einsum("po,vw->pvow", head.astype(jnp.float32), eye)
        operands.append(kron.reshape(head.shape[0] * sv, cout * sv).astype(jnp.bfloat16))
        out_shape = jax.ShapeDtypeStruct((head.shape[0], sx, sv, ss), jnp.float32)
    kernel = lambda *refs: fine_kernel(
        *refs, sx=sx, sv=sv, ss=ss, rows=rows, head=head is not None
    )
    return pl.pallas_call(
        kernel,
        out_shape=out_shape,
        scratch_shapes=[
            pltpu.VMEM((cout * sv, 9 * wide * rows), jnp.bfloat16),
            pltpu.VMEM((sx + 2, 3, wide * rows, ss), jnp.bfloat16),
        ],
    )(*operands)


def mid_kernel(p_ref, w_ref, o_ref, shifted_ref, *, sx, sv, ss, span):
    lanes = p_ref.shape[-1]
    pitch = ss + 2

    def shift(x, carry):
        slab = p_ref[x].astype(jnp.float32)
        for b in range(3):
            for c in range(3):
                step = b * pitch + c
                piece = slab if step == 0 else pltpu.roll(slab, lanes - step, 1)
                shifted_ref[x, b * 3 + c] = piece[:, :span].astype(jnp.bfloat16)
        return carry

    lax.fori_loop(0, sx + 2, shift, 0)
    chans = shifted_ref.shape[2]

    group = 4 if sx % 4 == 0 else 2

    def rows_pair(g, carry):
        x = group * g
        stack = jnp.concatenate(
            [shifted_ref[pl.ds(x + k, 3)].reshape(27 * chans, span) for k in range(group)], axis=1
        )
        acc = jnp.dot(w_ref[...], stack, preferred_element_type=jnp.float32)
        act = (acc * jax.nn.sigmoid(acc)).astype(jnp.bfloat16).astype(jnp.float32)
        for k in range(group):
            part = act[:, k * span : (k + 1) * span]
            for v in range(sv):
                piece = part if v == 0 else pltpu.roll(part, span - v * pitch, 1)
                o_ref[x + k, v] = piece[:, :ss]
        return carry

    lax.fori_loop(0, sx // group, rows_pair, 0)


def mid_conv(field, weight, sides=MID_SIDES):
    chans = field.shape[0]
    padded = extended(field, sides)
    _, sx, sv, ss = padded.shape
    sx, sv, ss = sx - 2, sv - 2, ss - 2
    flat = (sv + 2) * (ss + 2)
    lanes = round_up(flat, 128)
    span = round_up((sv - 1) * (ss + 2) + ss, 128)
    padded = padded.transpose(1, 0, 2, 3).reshape(sx + 2, chans, flat)
    padded = jnp.pad(padded, ((0, 0), (0, 0), (0, lanes - flat)))
    cout = weight.shape[1] // chans
    taps = weight.reshape(27, cout, chans).transpose(1, 0, 2).reshape(cout, 27 * chans)
    kernel = lambda *refs: mid_kernel(*refs, sx=sx, sv=sv, ss=ss, span=span)
    out = pl.pallas_call(
        kernel,
        out_shape=jax.ShapeDtypeStruct((sx, sv, cout, ss), jnp.float32),
        scratch_shapes=[pltpu.VMEM((sx + 2, 9, chans, span), jnp.bfloat16)],
    )(padded, taps)
    return out.transpose(2, 0, 1, 3).astype(jnp.bfloat16)


def conv_down(field, weight):
    return lax.conv_general_dilated(
        field[None],
        weight,
        (2, 2, 2),
        "VALID",
        dimension_numbers=NUMS,
        preferred_element_type=jnp.float32,
    )[0]


def fine_down(field, weight):
    sx, c, sv, ss = field.shape
    blocks = field.reshape(sx // 2, 2, c, sv // 2, 2, ss // 2, 2)
    return jnp.einsum("xaivbsc,oiabc->oxvs", blocks, weight, preferred_element_type=jnp.float32)


def fine_up(field, weight):
    outer = jnp.einsum("ixvs,ioabc->xaovbsc", field, weight, preferred_element_type=jnp.float32)
    chans, sx, sv, ss = (weight.shape[1], field.shape[1], field.shape[2], field.shape[3])
    return outer.reshape(2 * sx, chans, 2 * sv, 2 * ss)


def conv_up(field, weight):
    outer = jnp.einsum("ixvs,ioabc->oxavbsc", field, weight, preferred_element_type=jnp.float32)
    chans, sx, sv, ss = (weight.shape[1], field.shape[1], field.shape[2], field.shape[3])
    return outer.reshape(chans, 2 * sx, 2 * sv, 2 * ss)


def activate(value):
    return jax.nn.silu(value).astype(jnp.bfloat16)


def project(weight, field):
    return jnp.einsum("oc,cxp->oxp", weight, field, preferred_element_type=jnp.float32)


def normalize(block):
    values_f = block.astype(jnp.float32)
    mean_sq = jnp.mean(values_f * values_f, axis=0)
    return (values_f * lax.rsqrt(mean_sq + 1e-05)).astype(jnp.bfloat16)


def split_heads(weight, normed):
    chans, sx, count = normed.shape
    return project(weight, normed).astype(jnp.bfloat16).reshape(HEADS, chans // HEADS, sx, count)


def combine(queries, keys, values):
    scale = 1.0 / jnp.sqrt(jnp.float32(queries.shape[1]))
    scores = (
        jnp.einsum("hdxp,hdyp->hxyp", queries, keys, preferred_element_type=jnp.float32) * scale
    )
    weights = jax.nn.softmax(scores, axis=2).astype(jnp.bfloat16)
    attended = jnp.einsum("hxyp,hdyp->hdxp", weights, values, preferred_element_type=jnp.float32)
    heads, depth, sx, count = attended.shape
    return attended.astype(jnp.bfloat16).reshape(heads * depth, sx, count)


def finish(block, attended, w_attn_out):
    return (block.astype(jnp.float32) + project(w_attn_out, attended)).astype(jnp.bfloat16)


def on_device(
    inputs,
    w_in,
    w_fine_enc,
    w_down_mid,
    w_mid_enc,
    w_down_bottom,
    w_query,
    w_key,
    w_value,
    w_attn_out,
    w_up_mid,
    w_mid_dec,
    w_up_fine,
    w_fine_dec,
    w_head,
):
    fields = extended(inputs.transpose(1, 0, 2, 3), (("gx", 0, inputs.shape[1]),))
    first = inside_rows(fine_conv(fields, w_in).astype(jnp.bfloat16), -7)
    fine_wide = inside_rows(fine_conv(first, w_fine_enc).astype(jnp.bfloat16), -6)
    mid_in = activate(fine_down(fine_wide, w_down_mid))
    mid_wide = inside_rows(mid_conv(mid_in, w_mid_enc, MID_CROSS), -2, 1)
    mid_skip = mid_wide[:, 2:-2]
    bottom = activate(conv_down(mid_skip, unfold(w_down_bottom, 2, C2, C1)))
    chans, sx, sv, ss = bottom.shape
    flat = bottom.reshape(chans, sx, sv * ss)
    rows = lax.all_to_all(flat, "gx", split_axis=2, concat_axis=1, tiled=True)
    normed = normalize(rows)
    queries = split_heads(w_query, normed)
    keys = split_heads(w_key, normed)
    values = split_heads(w_value, normed)
    result = finish(rows, combine(queries, keys, values), w_attn_out)
    count = result.shape[2]
    groups = result.shape[1] // sx
    rim = jnp.pad(result, ((0, 0), (1, 1), (0, 0)))
    low = rim[:, : groups * sx].reshape(chans, groups, sx, count)
    high = rim[:, 2 : groups * sx + 2].reshape(chans, groups, sx, count)
    windows = jnp.concatenate([low, high], axis=2).reshape(chans, groups * 2 * sx, count)
    mixed = lax.all_to_all(windows, "gx", split_axis=1, concat_axis=2, tiled=True)
    bottom_out = mixed.reshape(chans, 2 * sx, sv, ss)
    mid_up = (
        conv_up(bottom_out, unfold(w_up_mid, 2, C2, C1)) + mid_wide.astype(jnp.float32)
    ).astype(jnp.bfloat16)
    mid_dec = inside_rows(mid_conv(mid_up, w_mid_dec, MID_CROSS), -1, 1)
    fine_up_field = (fine_up(mid_dec, w_up_fine) + fine_wide[4:-4].astype(jnp.float32)).astype(
        jnp.bfloat16
    )
    return fine_conv(fine_up_field[1:-1], w_fine_dec, head=w_head)


def solution(mesh):
    placed = (P(None, "gx", "gz", "gy"),) + (P(),) * 14
    return jax.shard_map(
        on_device, mesh=mesh, in_specs=placed, out_specs=P(None, "gx", "gz", "gy"), check_vma=False
    )
```

```python
import jax
import jax.numpy as jnp
from jax import lax
from jax.experimental import pallas as pl
from jax.experimental.pallas import tpu as pltpu
from jax.sharding import PartitionSpec as P

C1 = 64
C2 = 256
HEADS = 4


NUMS = ("NCDHW", "OIDHW", "NCDHW")
FINE_SIDES = (("gx", 0, 1), ("gy", 3, 1), ("gz", 2, 1))
FINE_CROSS = (("gy", 3, 1), ("gz", 2, 1))
MID_SIDES = (("gx", 1, 1), ("gy", 3, 1), ("gz", 2, 1))
MID_CROSS = (("gy", 3, 1), ("gz", 2, 1))


def extended(block, sides):
    for axis, dim, width in sides:
        count = lax.axis_size(axis)
        top = lax.slice_in_dim(block, block.shape[dim] - width, None, axis=dim)
        bottom = lax.slice_in_dim(block, 0, width, axis=dim)
        if count == 2:
            first = lax.axis_index(axis) == 0
            got = lax.ppermute(jnp.where(first, top, bottom), axis, [(0, 1), (1, 0)])
            low = jnp.where(first, jnp.zeros_like(got), got)
            high = jnp.where(first, got, jnp.zeros_like(got))
        else:
            forward = [(i, i + 1) for i in range(count - 1)]
            backward = [(target, source) for source, target in forward]
            low = lax.ppermute(top, axis, forward)
            high = lax.ppermute(bottom, axis, backward)
        block = jnp.concatenate([low, block, high], axis=dim)
    return block


def inside_rows(field, offset, dim=0):
    rows = field.shape[dim]
    own = rows + 2 * offset
    index = lax.axis_index("gx") * own + offset + jnp.arange(rows)
    keep = (index >= 0) & (index < own * lax.axis_size("gx"))
    shape = [1] * field.ndim
    shape[dim] = rows
    return jnp.where(keep.reshape(shape), field, jnp.zeros_like(field))


def unfold(weight, side, first, second):
    return weight.reshape(side, side, side, first, second).transpose(3, 4, 0, 1, 2)


def round_up(value, step):
    return (value + step - 1) // step * step


def fine_kernel(p_ref, e_ref, w_ref, *rest, sx, sv, ss, rows, head):
    if head:
        h_ref, o_ref, band_ref, shifted_ref = rest
    else:
        o_ref, band_ref, shifted_ref = rest
    cout, cin = w_ref.shape[1:]
    depth = cin * rows
    sv_bits, row_bits = sv.bit_length() - 1, rows.bit_length() - 1
    r = lax.broadcasted_iota(jnp.int32, (cout * sv, cout), 0)
    q = lax.broadcasted_iota(jnp.int32, (cout * sv, cout), 1)
    widen_rows = ((r >> sv_bits) == q).astype(jnp.bfloat16)
    r = lax.broadcasted_iota(jnp.int32, (cin, depth), 0)
    q = lax.broadcasted_iota(jnp.int32, (cin, depth), 1)
    widen_cols = ((q >> row_bits) == r).astype(jnp.bfloat16)
    r = lax.broadcasted_iota(jnp.int32, (cout * sv, depth), 0)
    q = lax.broadcasted_iota(jnp.int32, (cout * sv, depth), 1)
    w = q & (rows - 1)
    place = jnp.where(w < sv, w + 1, jnp.where(w == sv, 0, jnp.where(w == sv + 1, sv + 1, -8)))
    offset = place - (r & (sv - 1))
    for a in range(3):
        for c in range(3):
            band = jnp.zeros((cout * sv, depth), jnp.float32)
            for b in range(3):
                tap = w_ref[(a * 3 + b) * 3 + c]
                grown = jnp.dot(widen_rows, tap, preferred_element_type=jnp.float32)
                grown = jnp.dot(
                    grown.astype(jnp.bfloat16), widen_cols, preferred_element_type=jnp.float32
                )
                band = band + jnp.where(offset == b, grown, 0.0)
            band_ref[:, pl.ds((a * 3 + c) * depth, depth)] = band.astype(jnp.bfloat16)

    lane = lax.broadcasted_iota(jnp.int32, (depth, ss), 1)

    def shift(x, carry):
        slab = p_ref[x].astype(jnp.float32)
        edges = jnp.transpose(e_ref[x].astype(jnp.float32))
        low = jnp.where(lane == 0, edges[:, 0:1], pltpu.roll(slab, 1, 1))
        high = jnp.where(lane == ss - 1, edges[:, 1:2], pltpu.roll(slab, ss - 1, 1))
        shifted_ref[x, 0] = low.astype(jnp.bfloat16)
        shifted_ref[x, 1] = slab.astype(jnp.bfloat16)
        shifted_ref[x, 2] = high.astype(jnp.bfloat16)
        return carry

    lax.fori_loop(0, sx + 2, shift, 0)

    group = 4 if sx % 4 == 0 else 2

    def rows_pair(g, carry):
        x = group * g
        stack = jnp.concatenate(
            [shifted_ref[pl.ds(x + k, 3)].reshape(9 * depth, ss) for k in range(group)], axis=1
        )
        acc = jnp.dot(band_ref[...], stack, preferred_element_type=jnp.float32)
        act = (acc * jax.nn.sigmoid(acc)).astype(jnp.bfloat16)
        for k in range(group):
            part = act[:, k * ss : (k + 1) * ss]
            if head:
                res = jnp.dot(h_ref[...], part, preferred_element_type=jnp.float32)
                o_ref[:, x + k] = res.reshape(res.shape[0] // sv, sv, ss)
            else:
                o_ref[x + k] = part.astype(jnp.float32).reshape(cout, sv, ss)
        return carry

    lax.fori_loop(0, sx // group, rows_pair, 0)


def faces(block, axis, dim):
    count = lax.axis_size(axis)
    top = lax.slice_in_dim(block, block.shape[dim] - 1, None, axis=dim)
    bottom = lax.slice_in_dim(block, 0, 1, axis=dim)
    if count == 2:
        first = lax.axis_index(axis) == 0
        got = lax.ppermute(jnp.where(first, top, bottom), axis, [(0, 1), (1, 0)])
        return jnp.where(first, jnp.zeros_like(got), got), jnp.where(first, got, jnp.zeros_like(got))
    forward = [(i, i + 1) for i in range(count - 1)]
    backward = [(target, source) for source, target in forward]
    return lax.ppermute(top, axis, forward), lax.ppermute(bottom, axis, backward)


def fine_conv(field, weight, head=None):
    rows_x, cin, sv, ss = field.shape
    sx = rows_x - 2
    cout = weight.shape[0]
    rows = round_up(sv + 2, 16)
    wide = round_up(cin * rows, 128) // rows
    block = jnp.pad(field, ((0, 0), (0, wide - cin), (0, 0), (0, 0)))
    below, above = faces(block, "gz", 2)
    spare = jnp.zeros((rows_x, wide, rows - sv - 2, ss), block.dtype)
    padded = jnp.concatenate([block, below, above, spare], axis=2)
    left, right = faces(padded, "gy", 3)
    edges = jnp.concatenate([left, right], axis=3).transpose(0, 3, 1, 2)
    edges = jnp.pad(edges.reshape(rows_x, 2, wide * rows), ((0, 0), (0, 6), (0, 0)))
    padded = padded.reshape(rows_x, wide * rows, ss)
    taps = jnp.pad(weight, ((0, 0), (0, wide - cin), (0, 0), (0, 0), (0, 0)))
    operands = [padded, edges, taps.transpose(2, 3, 4, 0, 1).reshape(27, cout, wide)]
    if head is None:
        out_shape = jax.ShapeDtypeStruct((sx, cout, sv, ss), jnp.float32)
    else:
        eye = jnp.eye(sv, dtype=jnp.float32)
        kron = jnp.einsum("po,vw->pvow", head.astype(jnp.float32), eye)
        operands.append(kron.reshape(head.shape[0] * sv, cout * sv).astype(jnp.bfloat16))
        out_shape = jax.ShapeDtypeStruct((head.shape[0], sx, sv, ss), jnp.float32)
    kernel = lambda *refs: fine_kernel(
        *refs, sx=sx, sv=sv, ss=ss, rows=rows, head=head is not None
    )
    return pl.pallas_call(
        kernel,
        out_shape=out_shape,
        scratch_shapes=[
            pltpu.VMEM((cout * sv, 9 * wide * rows), jnp.bfloat16),
            pltpu.VMEM((sx + 2, 3, wide * rows, ss), jnp.bfloat16),
        ],
    )(*operands)


def mid_kernel(p_ref, w_ref, o_ref, shifted_ref, *, sx, sv, ss, span):
    lanes = p_ref.shape[-1]
    pitch = ss + 2

    def shift(x, carry):
        slab = p_ref[x].astype(jnp.float32)
        for b in range(3):
            for c in range(3):
                step = b * pitch + c
                piece = slab if step == 0 else pltpu.roll(slab, lanes - step, 1)
                shifted_ref[x, b * 3 + c] = piece[:, :span].astype(jnp.bfloat16)
        return carry

    lax.fori_loop(0, sx + 2, shift, 0)
    chans = shifted_ref.shape[2]

    group = sx if sx <= 8 else (4 if sx % 4 == 0 else 2)

    def rows_pair(g, carry):
        x = group * g
        stack = jnp.concatenate(
            [shifted_ref[pl.ds(x + k, 3)].reshape(27 * chans, span) for k in range(group)], axis=1
        )
        acc = jnp.dot(w_ref[...], stack, preferred_element_type=jnp.float32)
        act = (acc * jax.nn.sigmoid(acc)).astype(jnp.bfloat16).astype(jnp.float32)
        for k in range(group):
            part = act[:, k * span : (k + 1) * span]
            for v in range(sv):
                piece = part if v == 0 else pltpu.roll(part, span - v * pitch, 1)
                o_ref[x + k, v] = piece[:, :ss]
        return carry

    lax.fori_loop(0, sx // group, rows_pair, 0)


def mid_conv(field, weight, sides=MID_SIDES):
    chans = field.shape[0]
    padded = extended(field, sides)
    _, sx, sv, ss = padded.shape
    sx, sv, ss = sx - 2, sv - 2, ss - 2
    flat = (sv + 2) * (ss + 2)
    lanes = round_up(flat, 128)
    span = round_up((sv - 1) * (ss + 2) + ss, 128)
    padded = padded.transpose(1, 0, 2, 3).reshape(sx + 2, chans, flat)
    padded = jnp.pad(padded, ((0, 0), (0, 0), (0, lanes - flat)))
    cout = weight.shape[1] // chans
    taps = weight.reshape(27, cout, chans).transpose(1, 0, 2).reshape(cout, 27 * chans)
    kernel = lambda *refs: mid_kernel(*refs, sx=sx, sv=sv, ss=ss, span=span)
    out = pl.pallas_call(
        kernel,
        out_shape=jax.ShapeDtypeStruct((sx, sv, cout, ss), jnp.float32),
        scratch_shapes=[pltpu.VMEM((sx + 2, 9, chans, span), jnp.bfloat16)],
    )(padded, taps)
    return out.transpose(2, 0, 1, 3).astype(jnp.bfloat16)


def conv_down(field, weight):
    return lax.conv_general_dilated(
        field[None],
        weight,
        (2, 2, 2),
        "VALID",
        dimension_numbers=NUMS,
        preferred_element_type=jnp.float32,
    )[0]


def fine_down(field, weight):
    sx, c, sv, ss = field.shape
    blocks = field.reshape(sx // 2, 2, c, sv // 2, 2, ss // 2, 2)
    return jnp.einsum("xaivbsc,oiabc->oxvs", blocks, weight, preferred_element_type=jnp.float32)


def fine_up(field, weight):
    outer = jnp.einsum("ixvs,ioabc->xaovbsc", field, weight, preferred_element_type=jnp.float32)
    chans, sx, sv, ss = (weight.shape[1], field.shape[1], field.shape[2], field.shape[3])
    return outer.reshape(2 * sx, chans, 2 * sv, 2 * ss)


def conv_up(field, weight):
    outer = jnp.einsum("ixvs,ioabc->oxavbsc", field, weight, preferred_element_type=jnp.float32)
    chans, sx, sv, ss = (weight.shape[1], field.shape[1], field.shape[2], field.shape[3])
    return outer.reshape(chans, 2 * sx, 2 * sv, 2 * ss)


def activate(value):
    return jax.nn.silu(value).astype(jnp.bfloat16)


def project(weight, field):
    return jnp.einsum("oc,cxp->oxp", weight, field, preferred_element_type=jnp.float32)


def normalize(block):
    values_f = block.astype(jnp.float32)
    mean_sq = jnp.mean(values_f * values_f, axis=0)
    return (values_f * lax.rsqrt(mean_sq + 1e-05)).astype(jnp.bfloat16)


def split_heads(weight, normed):
    chans, sx, count = normed.shape
    return project(weight, normed).astype(jnp.bfloat16).reshape(HEADS, chans // HEADS, sx, count)


def combine(queries, keys, values):
    scale = 1.0 / jnp.sqrt(jnp.float32(queries.shape[1]))
    scores = (
        jnp.einsum("hdxp,hdyp->hxyp", queries, keys, preferred_element_type=jnp.float32) * scale
    )
    weights = jax.nn.softmax(scores, axis=2).astype(jnp.bfloat16)
    attended = jnp.einsum("hxyp,hdyp->hdxp", weights, values, preferred_element_type=jnp.float32)
    heads, depth, sx, count = attended.shape
    return attended.astype(jnp.bfloat16).reshape(heads * depth, sx, count)


def finish(block, attended, w_attn_out):
    return (block.astype(jnp.float32) + project(w_attn_out, attended)).astype(jnp.bfloat16)


def on_device(
    inputs,
    w_in,
    w_fine_enc,
    w_down_mid,
    w_mid_enc,
    w_down_bottom,
    w_query,
    w_key,
    w_value,
    w_attn_out,
    w_up_mid,
    w_mid_dec,
    w_up_fine,
    w_fine_dec,
    w_head,
):
    fields = extended(inputs.transpose(1, 0, 2, 3), (("gx", 0, inputs.shape[1]),))
    first = inside_rows(fine_conv(fields, w_in).astype(jnp.bfloat16), -7)
    fine_wide = inside_rows(fine_conv(first, w_fine_enc).astype(jnp.bfloat16), -6)
    mid_in = activate(fine_down(fine_wide, w_down_mid))
    mid_wide = inside_rows(mid_conv(mid_in, w_mid_enc, MID_CROSS), -2, 1)
    mid_skip = mid_wide[:, 2:-2]
    bottom = activate(conv_down(mid_skip, unfold(w_down_bottom, 2, C2, C1)))
    chans, sx, sv, ss = bottom.shape
    flat = bottom.reshape(chans, sx, sv * ss)
    rows = lax.all_to_all(flat, "gx", split_axis=2, concat_axis=1, tiled=True)
    normed = normalize(rows)
    queries = split_heads(w_query, normed)
    keys = split_heads(w_key, normed)
    values = split_heads(w_value, normed)
    result = finish(rows, combine(queries, keys, values), w_attn_out)
    count = result.shape[2]
    groups = result.shape[1] // sx
    rim = jnp.pad(result, ((0, 0), (1, 1), (0, 0)))
    low = rim[:, : groups * sx].reshape(chans, groups, sx, count)
    high = rim[:, 2 : groups * sx + 2].reshape(chans, groups, sx, count)
    windows = jnp.concatenate([low, high], axis=2).reshape(chans, groups * 2 * sx, count)
    mixed = lax.all_to_all(windows, "gx", split_axis=1, concat_axis=2, tiled=True)
    bottom_out = mixed.reshape(chans, 2 * sx, sv, ss)
    mid_up = (
        conv_up(bottom_out, unfold(w_up_mid, 2, C2, C1)) + mid_wide.astype(jnp.float32)
    ).astype(jnp.bfloat16)
    mid_dec = inside_rows(mid_conv(mid_up, w_mid_dec, MID_CROSS), -1, 1)
    fine_up_field = (fine_up(mid_dec, w_up_fine) + fine_wide[4:-4].astype(jnp.float32)).astype(
        jnp.bfloat16
    )
    return fine_conv(fine_up_field[1:-1], w_fine_dec, head=w_head)


def solution(mesh):
    placed = (P(None, "gx", "gz", "gy"),) + (P(),) * 14
    return jax.shard_map(
        on_device, mesh=mesh, in_specs=placed, out_specs=P(None, "gx", "gz", "gy"), check_vma=False
    )
```

```python
import jax
import jax.numpy as jnp
from jax import lax
from jax.experimental import pallas as pl
from jax.experimental.pallas import tpu as pltpu
from jax.sharding import PartitionSpec as P

C1 = 64
C2 = 256
HEADS = 4


NUMS = ("NCDHW", "OIDHW", "NCDHW")
FINE_SIDES = (("gx", 0, 1), ("gy", 3, 1), ("gz", 2, 1))
FINE_CROSS = (("gy", 3, 1), ("gz", 2, 1))
MID_SIDES = (("gx", 1, 1), ("gy", 3, 1), ("gz", 2, 1))
MID_CROSS = (("gy", 3, 1), ("gz", 2, 1))


def extended(block, sides):
    for axis, dim, width in sides:
        count = lax.axis_size(axis)
        top = lax.slice_in_dim(block, block.shape[dim] - width, None, axis=dim)
        bottom = lax.slice_in_dim(block, 0, width, axis=dim)
        if count == 2:
            first = lax.axis_index(axis) == 0
            got = lax.ppermute(jnp.where(first, top, bottom), axis, [(0, 1), (1, 0)])
            low = jnp.where(first, jnp.zeros_like(got), got)
            high = jnp.where(first, got, jnp.zeros_like(got))
        else:
            forward = [(i, i + 1) for i in range(count - 1)]
            backward = [(target, source) for source, target in forward]
            low = lax.ppermute(top, axis, forward)
            high = lax.ppermute(bottom, axis, backward)
        block = jnp.concatenate([low, block, high], axis=dim)
    return block


def inside_rows(field, offset, dim=0):
    rows = field.shape[dim]
    own = rows + 2 * offset
    index = lax.axis_index("gx") * own + offset + jnp.arange(rows)
    keep = (index >= 0) & (index < own * lax.axis_size("gx"))
    shape = [1] * field.ndim
    shape[dim] = rows
    return jnp.where(keep.reshape(shape), field, jnp.zeros_like(field))


def unfold(weight, side, first, second):
    return weight.reshape(side, side, side, first, second).transpose(3, 4, 0, 1, 2)


def round_up(value, step):
    return (value + step - 1) // step * step


def fine_kernel(p_ref, e_ref, w_ref, *rest, sx, sv, ss, rows, head):
    if head:
        h_ref, o_ref, band_ref, shifted_ref = rest
    else:
        o_ref, band_ref, shifted_ref = rest
    cout, cin = w_ref.shape[1:]
    depth = cin * rows
    sv_bits, row_bits = sv.bit_length() - 1, rows.bit_length() - 1
    r = lax.broadcasted_iota(jnp.int32, (cout * sv, cout), 0)
    q = lax.broadcasted_iota(jnp.int32, (cout * sv, cout), 1)
    widen_rows = ((r >> sv_bits) == q).astype(jnp.bfloat16)
    r = lax.broadcasted_iota(jnp.int32, (cin, depth), 0)
    q = lax.broadcasted_iota(jnp.int32, (cin, depth), 1)
    widen_cols = ((q >> row_bits) == r).astype(jnp.bfloat16)
    r = lax.broadcasted_iota(jnp.int32, (cout * sv, depth), 0)
    q = lax.broadcasted_iota(jnp.int32, (cout * sv, depth), 1)
    w = q & (rows - 1)
    place = jnp.where(w < sv, w + 1, jnp.where(w == sv, 0, jnp.where(w == sv + 1, sv + 1, -8)))
    offset = place - (r & (sv - 1))
    for a in range(3):
        for c in range(3):
            band = jnp.zeros((cout * sv, depth), jnp.float32)
            for b in range(3):
                tap = w_ref[(a * 3 + b) * 3 + c]
                grown = jnp.dot(widen_rows, tap, preferred_element_type=jnp.float32)
                grown = jnp.dot(
                    grown.astype(jnp.bfloat16), widen_cols, preferred_element_type=jnp.float32
                )
                band = band + jnp.where(offset == b, grown, 0.0)
            band_ref[:, pl.ds((a * 3 + c) * depth, depth)] = band.astype(jnp.bfloat16)

    lane = lax.broadcasted_iota(jnp.int32, (depth, ss), 1)

    def shift(x, carry):
        slab = p_ref[x].astype(jnp.float32)
        edges = jnp.transpose(e_ref[x].astype(jnp.float32))
        low = jnp.where(lane == 0, edges[:, 0:1], pltpu.roll(slab, 1, 1))
        high = jnp.where(lane == ss - 1, edges[:, 1:2], pltpu.roll(slab, ss - 1, 1))
        shifted_ref[x, 0] = low.astype(jnp.bfloat16)
        shifted_ref[x, 1] = slab.astype(jnp.bfloat16)
        shifted_ref[x, 2] = high.astype(jnp.bfloat16)
        return carry

    lax.fori_loop(0, sx + 2, shift, 0)

    group = sx if sx <= 8 else (4 if sx % 4 == 0 else 2)

    def rows_pair(g, carry):
        x = group * g
        stack = jnp.concatenate(
            [shifted_ref[pl.ds(x + k, 3)].reshape(9 * depth, ss) for k in range(group)], axis=1
        )
        acc = jnp.dot(band_ref[...], stack, preferred_element_type=jnp.float32)
        act = (acc * jax.nn.sigmoid(acc)).astype(jnp.bfloat16)
        for k in range(group):
            part = act[:, k * ss : (k + 1) * ss]
            if head:
                res = jnp.dot(h_ref[...], part, preferred_element_type=jnp.float32)
                o_ref[:, x + k] = res.reshape(res.shape[0] // sv, sv, ss)
            else:
                o_ref[x + k] = part.astype(jnp.float32).reshape(cout, sv, ss)
        return carry

    lax.fori_loop(0, sx // group, rows_pair, 0)


def faces(block, axis, dim):
    count = lax.axis_size(axis)
    top = lax.slice_in_dim(block, block.shape[dim] - 1, None, axis=dim)
    bottom = lax.slice_in_dim(block, 0, 1, axis=dim)
    if count == 2:
        first = lax.axis_index(axis) == 0
        got = lax.ppermute(jnp.where(first, top, bottom), axis, [(0, 1), (1, 0)])
        return jnp.where(first, jnp.zeros_like(got), got), jnp.where(first, got, jnp.zeros_like(got))
    forward = [(i, i + 1) for i in range(count - 1)]
    backward = [(target, source) for source, target in forward]
    return lax.ppermute(top, axis, forward), lax.ppermute(bottom, axis, backward)


def fine_conv(field, weight, head=None):
    rows_x, cin, sv, ss = field.shape
    sx = rows_x - 2
    cout = weight.shape[0]
    rows = round_up(sv + 2, 16)
    wide = round_up(cin * rows, 128) // rows
    block = jnp.pad(field, ((0, 0), (0, wide - cin), (0, 0), (0, 0)))
    below, above = faces(block, "gz", 2)
    spare = jnp.zeros((rows_x, wide, rows - sv - 2, ss), block.dtype)
    padded = jnp.concatenate([block, below, above, spare], axis=2)
    left, right = faces(padded, "gy", 3)
    edges = jnp.concatenate([left, right], axis=3).transpose(0, 3, 1, 2)
    edges = jnp.pad(edges.reshape(rows_x, 2, wide * rows), ((0, 0), (0, 6), (0, 0)))
    padded = padded.reshape(rows_x, wide * rows, ss)
    taps = jnp.pad(weight, ((0, 0), (0, wide - cin), (0, 0), (0, 0), (0, 0)))
    operands = [padded, edges, taps.transpose(2, 3, 4, 0, 1).reshape(27, cout, wide)]
    if head is None:
        out_shape = jax.ShapeDtypeStruct((sx, cout, sv, ss), jnp.float32)
    else:
        eye = jnp.eye(sv, dtype=jnp.float32)
        kron = jnp.einsum("po,vw->pvow", head.astype(jnp.float32), eye)
        operands.append(kron.reshape(head.shape[0] * sv, cout * sv).astype(jnp.bfloat16))
        out_shape = jax.ShapeDtypeStruct((head.shape[0], sx, sv, ss), jnp.float32)
    kernel = lambda *refs: fine_kernel(
        *refs, sx=sx, sv=sv, ss=ss, rows=rows, head=head is not None
    )
    return pl.pallas_call(
        kernel,
        out_shape=out_shape,
        scratch_shapes=[
            pltpu.VMEM((cout * sv, 9 * wide * rows), jnp.bfloat16),
            pltpu.VMEM((sx + 2, 3, wide * rows, ss), jnp.bfloat16),
        ],
    )(*operands)


def mid_kernel(p_ref, w_ref, o_ref, shifted_ref, *, sx, sv, ss, span):
    lanes = p_ref.shape[-1]
    pitch = ss + 2

    def shift(x, carry):
        slab = p_ref[x].astype(jnp.float32)
        for b in range(3):
            for c in range(3):
                step = b * pitch + c
                piece = slab if step == 0 else pltpu.roll(slab, lanes - step, 1)
                shifted_ref[x, b * 3 + c] = piece[:, :span].astype(jnp.bfloat16)
        return carry

    lax.fori_loop(0, sx + 2, shift, 0)
    chans = shifted_ref.shape[2]

    group = 4 if sx % 4 == 0 else 2

    def rows_pair(g, carry):
        x = group * g
        stack = jnp.concatenate(
            [shifted_ref[pl.ds(x + k, 3)].reshape(27 * chans, span) for k in range(group)], axis=1
        )
        acc = jnp.dot(w_ref[...], stack, preferred_element_type=jnp.float32)
        act = (acc * jax.nn.sigmoid(acc)).astype(jnp.bfloat16).astype(jnp.float32)
        for k in range(group):
            part = act[:, k * span : (k + 1) * span]
            for v in range(sv):
                piece = part if v == 0 else pltpu.roll(part, span - v * pitch, 1)
                o_ref[x + k, v] = piece[:, :ss]
        return carry

    lax.fori_loop(0, sx // group, rows_pair, 0)


def mid_conv(field, weight, sides=MID_SIDES):
    chans = field.shape[0]
    padded = extended(field, sides)
    _, sx, sv, ss = padded.shape
    sx, sv, ss = sx - 2, sv - 2, ss - 2
    flat = (sv + 2) * (ss + 2)
    lanes = round_up(flat, 128)
    span = round_up((sv - 1) * (ss + 2) + ss, 128)
    padded = padded.transpose(1, 0, 2, 3).reshape(sx + 2, chans, flat)
    padded = jnp.pad(padded, ((0, 0), (0, 0), (0, lanes - flat)))
    cout = weight.shape[1] // chans
    taps = weight.reshape(27, cout, chans).transpose(1, 0, 2).reshape(cout, 27 * chans)
    kernel = lambda *refs: mid_kernel(*refs, sx=sx, sv=sv, ss=ss, span=span)
    out = pl.pallas_call(
        kernel,
        out_shape=jax.ShapeDtypeStruct((sx, sv, cout, ss), jnp.float32),
        scratch_shapes=[pltpu.VMEM((sx + 2, 9, chans, span), jnp.bfloat16)],
    )(padded, taps)
    return out.transpose(2, 0, 1, 3).astype(jnp.bfloat16)


def conv_down(field, weight):
    return lax.conv_general_dilated(
        field[None],
        weight,
        (2, 2, 2),
        "VALID",
        dimension_numbers=NUMS,
        preferred_element_type=jnp.float32,
    )[0]


def fine_down(field, weight):
    sx, c, sv, ss = field.shape
    blocks = field.reshape(sx // 2, 2, c, sv // 2, 2, ss // 2, 2)
    return jnp.einsum("xaivbsc,oiabc->oxvs", blocks, weight, preferred_element_type=jnp.float32)


def fine_up(field, weight):
    outer = jnp.einsum("ixvs,ioabc->xaovbsc", field, weight, preferred_element_type=jnp.float32)
    chans, sx, sv, ss = (weight.shape[1], field.shape[1], field.shape[2], field.shape[3])
    return outer.reshape(2 * sx, chans, 2 * sv, 2 * ss)


def conv_up(field, weight):
    outer = jnp.einsum("ixvs,ioabc->oxavbsc", field, weight, preferred_element_type=jnp.float32)
    chans, sx, sv, ss = (weight.shape[1], field.shape[1], field.shape[2], field.shape[3])
    return outer.reshape(chans, 2 * sx, 2 * sv, 2 * ss)


def activate(value):
    return jax.nn.silu(value).astype(jnp.bfloat16)


def project(weight, field):
    return jnp.einsum("oc,cxp->oxp", weight, field, preferred_element_type=jnp.float32)


def normalize(block):
    values_f = block.astype(jnp.float32)
    mean_sq = jnp.mean(values_f * values_f, axis=0)
    return (values_f * lax.rsqrt(mean_sq + 1e-05)).astype(jnp.bfloat16)


def split_heads(weight, normed):
    chans, sx, count = normed.shape
    return project(weight, normed).astype(jnp.bfloat16).reshape(HEADS, chans // HEADS, sx, count)


def combine(queries, keys, values):
    scale = 1.0 / jnp.sqrt(jnp.float32(queries.shape[1]))
    scores = (
        jnp.einsum("hdxp,hdyp->hxyp", queries, keys, preferred_element_type=jnp.float32) * scale
    )
    weights = jax.nn.softmax(scores, axis=2).astype(jnp.bfloat16)
    attended = jnp.einsum("hxyp,hdyp->hdxp", weights, values, preferred_element_type=jnp.float32)
    heads, depth, sx, count = attended.shape
    return attended.astype(jnp.bfloat16).reshape(heads * depth, sx, count)


def finish(block, attended, w_attn_out):
    return (block.astype(jnp.float32) + project(w_attn_out, attended)).astype(jnp.bfloat16)


def on_device(
    inputs,
    w_in,
    w_fine_enc,
    w_down_mid,
    w_mid_enc,
    w_down_bottom,
    w_query,
    w_key,
    w_value,
    w_attn_out,
    w_up_mid,
    w_mid_dec,
    w_up_fine,
    w_fine_dec,
    w_head,
):
    fields = extended(inputs.transpose(1, 0, 2, 3), (("gx", 0, inputs.shape[1]),))
    first = inside_rows(fine_conv(fields, w_in).astype(jnp.bfloat16), -7)
    fine_wide = inside_rows(fine_conv(first, w_fine_enc).astype(jnp.bfloat16), -6)
    mid_in = activate(fine_down(fine_wide, w_down_mid))
    mid_wide = inside_rows(mid_conv(mid_in, w_mid_enc, MID_CROSS), -2, 1)
    mid_skip = mid_wide[:, 2:-2]
    bottom = activate(conv_down(mid_skip, unfold(w_down_bottom, 2, C2, C1)))
    chans, sx, sv, ss = bottom.shape
    flat = bottom.reshape(chans, sx, sv * ss)
    rows = lax.all_to_all(flat, "gx", split_axis=2, concat_axis=1, tiled=True)
    normed = normalize(rows)
    queries = split_heads(w_query, normed)
    keys = split_heads(w_key, normed)
    values = split_heads(w_value, normed)
    result = finish(rows, combine(queries, keys, values), w_attn_out)
    count = result.shape[2]
    groups = result.shape[1] // sx
    rim = jnp.pad(result, ((0, 0), (1, 1), (0, 0)))
    low = rim[:, : groups * sx].reshape(chans, groups, sx, count)
    high = rim[:, 2 : groups * sx + 2].reshape(chans, groups, sx, count)
    windows = jnp.concatenate([low, high], axis=2).reshape(chans, groups * 2 * sx, count)
    mixed = lax.all_to_all(windows, "gx", split_axis=1, concat_axis=2, tiled=True)
    bottom_out = mixed.reshape(chans, 2 * sx, sv, ss)
    mid_up = (
        conv_up(bottom_out, unfold(w_up_mid, 2, C2, C1)) + mid_wide.astype(jnp.float32)
    ).astype(jnp.bfloat16)
    mid_dec = inside_rows(mid_conv(mid_up, w_mid_dec, MID_CROSS), -1, 1)
    fine_up_field = (fine_up(mid_dec, w_up_fine) + fine_wide[4:-4].astype(jnp.float32)).astype(
        jnp.bfloat16
    )
    return fine_conv(fine_up_field[1:-1], w_fine_dec, head=w_head)


def solution(mesh):
    placed = (P(None, "gx", "gz", "gy"),) + (P(),) * 14
    return jax.shard_map(
        on_device, mesh=mesh, in_specs=placed, out_specs=P(None, "gx", "gz", "gy"), check_vma=False
    )
```
